32 devices in a mesh: groups: 2 (over y), sect: 4 (over z), band: 2 (over x), sub: 2 (over core).
Axes of the slice: x: 2, y: 2, z: 4, core: 2. Of those that a mesh axis runs over, the one named last changes fastest.
Arguments:
- images: bfloat16 [2, 256, 256, 256], P('band', ('groups', 'sect', 'sub')), parts along dimension 1, may hold values from -48 to 48
- offsets: float32 [2, 256, 2], P('band', ('groups', 'sect', 'sub')), parts along dimension 1, may hold values from -0.5 to 0.5
- widths: float32 [2, 256, 2], P('band', ('groups', 'sect', 'sub')), parts along dimension 1, may hold values from 0.1 to 1
- weights: bfloat16 [2, 256], P('band', ('groups', 'sect', 'sub')), parts along dimension 1, may hold values from 0.25 to 4
- dest: int32 [2, 256], P('band', ('groups', 'sect', 'sub')), parts along dimension 1, may hold values from 0 to 7, as said below
- cells: int32 [2, 256], P('band', ('groups', 'sect', 'sub')), parts along dimension 1, may hold values from 0 to 3, as said below
- band_gain: float32 [2], P('band'), may hold values from 2 to 8
Outputs:
- coadd: bfloat16 [2, 256, 16384], P('band', None, ('groups', 'sect', 'sub')), parts along dimension 2
- detection: float32 [256, 16384], P('band', ('groups', 'sect', 'sub')), parts along dimension 1
The draws below stay inside these ranges and needn't reach their ends.
There are 2 independent parts, one for each index of `groups`. The reference program is written for one: setup_inputs(seed, part) draws one part's arguments, and reference() takes and returns one part's arrays. A program takes and returns all parts, laid end to end along the dimension named above; an argument that names none is the same for every part. Nothing has to cross between parts.
Inputs may be any that keep to these rules, and one draw needn't show every extreme that they name: `dest`: among the 16 blocks of one device in one band, no owner is named more than 4 times; in every band one owner is named exactly 4 times by every device's blocks. `cells`: in every band, at most one block of each owner falls in that owner's cell 4 - 1.
All inputs are finite; a program needn't handle non-finite values.
Results may differ from the reference program's by a relative error of at most 0.0012.
The reference program's roundings to bfloat16 on the way count: a program that leaves them out, or rounds other values in their place, can miss the bound.
Values may be sent and summed in bfloat16 or wider, within the bound.
No kernel may reach another device: no remote copies, remote signals or barrier semaphores. Data moves between devices by JAX's collectives and lax.ppermute only.
A program may use at most 64 MiB of HBM per device.

```python
import math
import jax
import jax.numpy as jnp
from jax import lax

PIX = 256
BLK_DEV = 16
CELL_DEV = 4
PSF_R = 8
DET_R = 4
BANDS = 2
OWNERS = 8
CAP = 4
WBLK = 128
CELLS = 32
XW = 8192


def draw_images(key, part):
    base = jax.random.fold_in(key, 5021)
    speckle_key, level_key = jax.random.split(base)
    row_index = jnp.arange(PIX, dtype=jnp.int32)
    parity = (1 - 2 * (row_index % 2)).astype(jnp.float32)
    speckle = 2.5 * jnp.clip(jax.random.normal(speckle_key, (BANDS, WBLK, PIX, PIX), jnp.float32), -3.0, 3.0)
    amplitude = jax.random.uniform(level_key, (BANDS, WBLK), jnp.float32, 28.0, 40.0)
    return (speckle + amplitude[:, :, None, None] * parity[None, None, :, None]).astype(jnp.bfloat16)


def owner_table(key):
    base = jax.random.fold_in(key, 7177)
    hot_key, slot_key = jax.random.split(base)
    hottest = jax.random.randint(hot_key, (BANDS,), 0, OWNERS)
    source_keys = jax.random.split(slot_key, BANDS * OWNERS)
    hot_each = jnp.repeat(hottest, OWNERS)
    slot_owner = jnp.arange(OWNERS * CAP, dtype=jnp.int32) // CAP

    def one_source(source_key, hot_owner):
        order_key, mixing_key = jax.random.split(source_key)
        scores = jax.random.permutation(order_key, OWNERS * CAP)
        scores = jnp.where(slot_owner == hot_owner, -1 - jnp.arange(OWNERS * CAP, dtype=jnp.int32), scores.astype(jnp.int32))
        picked = jnp.argsort(scores, stable=True)[:BLK_DEV]
        chosen = slot_owner[picked]
        return jax.random.permutation(mixing_key, chosen)
    owners_named = jax.vmap(one_source)(source_keys, hot_each)
    return owners_named.reshape(BANDS, OWNERS * BLK_DEV).astype(jnp.int32)


def draw_dest(key, part):
    return owner_table(key)


def draw_cells(key, part):
    owners_named = owner_table(key)
    cell_key = jax.random.fold_in(key, 9311)
    score_key = jax.random.fold_in(key, 4409)
    lower_cells = jax.random.randint(cell_key, (BANDS, WBLK), 0, CELL_DEV - 1).astype(jnp.int32)
    band_keys = jax.random.split(score_key, BANDS)
    owner_ids = jnp.arange(OWNERS, dtype=jnp.int32)
    block_ids = jnp.arange(WBLK, dtype=jnp.int32)

    def one_band(band_key, named, lower):
        scores = jax.random.permutation(band_key, WBLK).astype(jnp.int32)
        matching = named[None, :] == owner_ids[:, None]
        masked = jnp.where(matching, scores[None, :], WBLK + scores[None, :])
        picked = jnp.argsort(masked, axis=1, stable=True)[:, 0].astype(jnp.int32)
        valid = named[picked] == owner_ids
        lone = jnp.any(jnp.logical_and(block_ids[None, :] == picked[:, None], valid[:, None]), axis=0)
        return jnp.where(lone, CELL_DEV - 1, lower).astype(jnp.int32)
    return jax.vmap(one_band)(band_keys, owners_named, lower_cells).astype(jnp.int32)


def steps_of(rng, extent, shards, least, top_value):
    factor_of = 1.0
    for dim, blocks in shards:
        draws = jax.random.uniform(jax.random.fold_in(jax.random.fold_in(rng, 6), dim), (blocks,), jnp.float32, least / len(shards), top_value / len(shards))
        factor_of = factor_of * jnp.repeat(jnp.exp(draws), extent[dim] // blocks).reshape((-1,) + (1,) * (len(extent) - 1 - dim))
    return factor_of


def setup_inputs(seed: int = 0, part: int = 0) -> dict:
    arg_keys = jax.random.split(jax.random.key(seed), 8)
    own_keys = jax.random.split(jax.random.fold_in(arg_keys[7], part), 8)
    images = draw_images(jax.random.fold_in(jax.random.fold_in(arg_keys[7], part), 71), part)
    offsets = jnp.clip(jax.random.uniform(own_keys[1], (BANDS, WBLK, 2), jnp.float32, -0.5, 0.5) * steps_of(own_keys[1], (BANDS, WBLK, 2), ((0, 2), (1, 8)), -0.4, 0.0), -0.5, 0.5)
    widths = jnp.clip(jnp.exp(math.log(1.0) - 2.3025851 * jax.random.uniform(own_keys[2], (BANDS, WBLK, 2), jnp.float32) ** steps_of(own_keys[2], (BANDS, WBLK, 2), ((0, 2), (1, 8)), -0.2, 0.2)), 0.1, 1.0)
    weights = jnp.clip(jnp.exp(math.log(4.0) - 2.7725887 * jax.random.uniform(own_keys[3], (BANDS, WBLK), jnp.float32) ** steps_of(own_keys[3], (BANDS, WBLK), ((0, 2), (1, 8)), -0.2, 0.2)), 0.25, 4.0).astype(jnp.bfloat16)
    dest = draw_dest(jax.random.fold_in(jax.random.fold_in(arg_keys[7], part), 71), part)
    cells = draw_cells(jax.random.fold_in(jax.random.fold_in(arg_keys[7], part), 71), part)
    band_gain = jnp.clip(jnp.exp(math.log(8.0) - 1.3862944 * jax.random.uniform(arg_keys[6], (BANDS,), jnp.float32) ** steps_of(arg_keys[6], (BANDS,), ((0, 2),), -0.2, 0.2)), 2.0, 8.0)
    return {"images": images, "offsets": offsets, "widths": widths, "weights": weights, "dest": dest, "cells": cells, "band_gain": band_gain}


det_sigma = 3.0


def lanczos_tap(spacing):
    return jnp.where(jnp.abs(spacing) < 3.0, jnp.sinc(spacing) * jnp.sinc(spacing / 3.0), 0.0)


def block_kernels(shift, spread, side):
    position = jnp.arange(side, dtype=jnp.float32)
    spacing = position[:, None] - position[None, :]
    weight_total = jnp.zeros_like(spread)
    summed = jnp.zeros((shift.shape[0], side, side), jnp.float32)
    for tap_shift in range(-PSF_R, PSF_R + 1):
        tap_weight = jnp.exp(-spread * float(tap_shift * tap_shift))
        weight_total = weight_total + tap_weight
        summed = summed + tap_weight[:, None, None] * lanczos_tap(spacing[None] + (shift[:, None, None] + float(tap_shift)))
    return summed / weight_total[:, None, None]


def filter_taps():
    values = [math.exp(-float(tap * tap) / (2.0 * det_sigma * det_sigma)) for tap in range(-DET_R, DET_R + 1)]
    whole = sum(values)
    return [value / whole for value in values]


def smooth_columns(padded, width):
    taps = filter_taps()
    total = jnp.zeros((padded.shape[0], width), jnp.float32)
    for index, tap in enumerate(range(-DET_R, DET_R + 1)):
        total = total + taps[index] * padded[:, DET_R + tap:DET_R + tap + width]
    return total


def smooth_rows(image):
    taps = filter_taps()
    height = image.shape[0]
    padded = jnp.pad(image, ((DET_R, DET_R), (0, 0)))
    total = jnp.zeros_like(image)
    for index, tap in enumerate(range(-DET_R, DET_R + 1)):
        total = total + taps[index] * padded[DET_R + tap:DET_R + tap + height, :]
    return total


def warp_group(packet):
    blocks, shifts, spreads = packet
    side = blocks.shape[-1]
    row_kernel = block_kernels(shifts[:, 0], spreads[:, 0], side).astype(jnp.bfloat16)
    col_kernel = block_kernels(shifts[:, 1], spreads[:, 1], side).astype(jnp.bfloat16)
    section = jnp.einsum('bij,bjk->bik', row_kernel.astype(jnp.float32), blocks.astype(jnp.float32)).astype(jnp.bfloat16)
    return jnp.einsum('bij,bkj->bik', section.astype(jnp.float32), col_kernel.astype(jnp.float32)).astype(jnp.bfloat16)


def reference(images, offsets, widths, weights, dest, cells, band_gain):
    side = images.shape[-1]
    group_count = BANDS * WBLK // BLK_DEV
    warped = lax.map(warp_group, (images.reshape(group_count, BLK_DEV, side, side),
                                  offsets.reshape(group_count, BLK_DEV, 2),
                                  widths.reshape(group_count, BLK_DEV, 2)))
    warped = warped.reshape(BANDS, WBLK, side * side)
    target = (dest * CELL_DEV + cells).astype(jnp.int32)
    coadd_list = []
    detection = jnp.zeros((side, XW), jnp.float32)
    for band_index in range(BANDS):
        band_weight = weights[band_index].astype(jnp.float32)
        weighted = warped[band_index].astype(jnp.float32) * band_weight[:, None]
        numerator = jax.ops.segment_sum(weighted, target[band_index], num_segments=CELLS)
        denominator = jax.ops.segment_sum(band_weight, target[band_index], num_segments=CELLS)
        cell_mean = (numerator / jnp.maximum(denominator, 1.0)[:, None]).astype(jnp.bfloat16)
        band_coadd = cell_mean.reshape(CELLS, side, side).transpose(1, 0, 2).reshape(side, CELLS * side)
        coadd_list.append(band_coadd)
        padded = jnp.pad(band_coadd.astype(jnp.float32), ((0, 0), (DET_R, DET_R)))
        smoothed = smooth_rows(smooth_columns(padded, XW))
        detection = detection + band_gain[band_index] * smoothed
    return jnp.stack(coadd_list), detection
```

```python
import math

import jax
import jax.numpy as jnp
from jax import lax
from jax.sharding import PartitionSpec as P

CELL_DEV = 4
PSF_R = 8
DET_R = 4


det_sigma = 3.0


def extended(array, sides, width):
    for axis, dim in sides:
        size, length = (lax.axis_size(axis), array.shape[dim])
        up = [(i, (i + 1) % size) for i in range(size - 1)]
        down = [(j, i) for i, j in up]
        last = lax.slice_in_dim(array, length - width, length, axis=dim)
        initial = lax.slice_in_dim(array, 0, width, axis=dim)
        before = lax.ppermute(last, axis, up)
        after = lax.ppermute(initial, axis, down)
        array = jnp.concatenate([before, array, after], axis=dim)
    return array


def lanczos_tap(spacing):
    return jnp.where(jnp.abs(spacing) < 3.0, jnp.sinc(spacing) * jnp.sinc(spacing / 3.0), 0.0)


def block_kernels(shift, spread, side):
    band = PSF_R + 4
    spacing = jnp.arange(-band, band + 1, dtype=jnp.float32)
    weight_total = jnp.zeros_like(spread)
    summed = jnp.zeros((shift.shape[0], 2 * band + 1), jnp.float32)
    for tap_shift in range(-PSF_R, PSF_R + 1):
        tap_weight = jnp.exp(-spread * float(tap_shift * tap_shift))
        weight_total = weight_total + tap_weight
        summed = summed + tap_weight[:, None] * lanczos_tap(
            spacing[None] + (shift[:, None] + float(tap_shift))
        )
    values = (summed / weight_total[:, None]).astype(jnp.bfloat16)
    position = jnp.arange(side, dtype=jnp.int32)
    lag = position[:, None] - position[None, :]
    matrix = jnp.zeros((shift.shape[0], side, side), jnp.bfloat16)
    for index in range(2 * band + 1):
        matrix = jnp.where((lag == index - band)[None], values[:, index, None, None], matrix)
    return matrix


def filter_taps():
    values = [
        math.exp(-float(tap * tap) / (2.0 * det_sigma * det_sigma))
        for tap in range(-DET_R, DET_R + 1)
    ]
    whole = sum(values)
    return [value / whole for value in values]


def smooth_columns(padded, width):
    taps = filter_taps()
    total = jnp.zeros((padded.shape[0], width), jnp.float32)
    for index, tap in enumerate(range(-DET_R, DET_R + 1)):
        total = total + taps[index] * padded[:, DET_R + tap : DET_R + tap + width]
    return total


def smooth_rows(image):
    taps = filter_taps()
    height = image.shape[0]
    padded = jnp.pad(image, ((DET_R, DET_R), (0, 0)))
    total = jnp.zeros_like(image)
    for index, tap in enumerate(range(-DET_R, DET_R + 1)):
        total = total + taps[index] * padded[DET_R + tap : DET_R + tap + height, :]
    return total


def local(images, offsets, widths, weights, dest, cells, band_gain):
    side = images.shape[-1]
    count = images.shape[1]
    sect_count = lax.axis_size("sect")
    sub_count = lax.axis_size("sub")
    owners = sect_count * sub_count
    capacity = max(2, -(-2 * count // owners))
    slot_count = owners * capacity
    row_kernel = block_kernels(offsets[0, :, 0], widths[0, :, 0], side)
    col_kernel = block_kernels(offsets[0, :, 1], widths[0, :, 1], side)
    section = jnp.einsum(
        "bij,bjk->bik", row_kernel, images[0], preferred_element_type=jnp.float32
    ).astype(jnp.bfloat16)
    warped = jnp.einsum(
        "bij,bkj->bik", section, col_kernel, preferred_element_type=jnp.float32
    ).astype(jnp.bfloat16)
    target = dest[0]
    same_owner = target[:, None] == target[None, :]
    block_order = jnp.arange(count, dtype=jnp.int32)
    earlier = block_order[None, :] < block_order[:, None]
    rank_within = jnp.sum(jnp.logical_and(same_owner, earlier), axis=1)
    slot_index = target * capacity + rank_within
    placing = (jnp.arange(slot_count, dtype=jnp.int32)[:, None] == slot_index[None, :]).astype(
        jnp.bfloat16
    )
    packed = jnp.dot(
        placing, warped.reshape(count, side * side), preferred_element_type=jnp.float32
    ).astype(jnp.bfloat16)
    cell_weight = jnp.where(
        cells[0][:, None] == jnp.arange(CELL_DEV, dtype=jnp.int32)[None, :],
        weights[0][:, None],
        jnp.zeros((), jnp.bfloat16),
    )
    packed_weight = jnp.dot(placing, cell_weight, preferred_element_type=jnp.float32).astype(
        jnp.bfloat16
    )
    received, received_weight = (
        lax.all_to_all(
            packed.reshape(owners, capacity, side * side),
            ("sect", "sub"),
            split_axis=0,
            concat_axis=0,
            tiled=True,
        ),
        lax.all_to_all(
            packed_weight.reshape(owners, capacity, CELL_DEV),
            ("sect", "sub"),
            split_axis=0,
            concat_axis=0,
            tiled=True,
        ),
    )
    received = received.reshape(slot_count, side * side)
    received_weight = received_weight.reshape(slot_count, CELL_DEV)
    numerator = jnp.einsum(
        "sc,sp->cp", received_weight, received, preferred_element_type=jnp.float32
    )
    denominator = jnp.sum(received_weight.astype(jnp.float32), axis=0)
    cell_mean = (numerator / jnp.maximum(denominator, 1.0)[:, None]).astype(jnp.bfloat16)
    coadd = (
        cell_mean.reshape(CELL_DEV, side, side).transpose(1, 0, 2).reshape(side, CELL_DEV * side)
    )
    padded = extended(coadd, ((("sect", "sub"), 1),), DET_R)
    smoothed = smooth_rows(smooth_columns(padded.astype(jnp.float32), CELL_DEV * side))
    band_term = band_gain[0] * smoothed
    detection = lax.psum_scatter(band_term, "band", scatter_dimension=0, tiled=True)
    return (coadd[None], detection)


def solution(mesh):
    return jax.shard_map(
        local,
        mesh=mesh,
        in_specs=(
            P("band", ("groups", "sect", "sub"), None, None),
            P("band", ("groups", "sect", "sub"), None),
            P("band", ("groups", "sect", "sub"), None),
            P("band", ("groups", "sect", "sub")),
            P("band", ("groups", "sect", "sub")),
            P("band", ("groups", "sect", "sub")),
            P("band"),
        ),
        out_specs=(
            P("band", None, ("groups", "sect", "sub")),
            P("band", ("groups", "sect", "sub")),
        ),
        check_vma=False,
    )
```

```python
import math

import jax
import jax.numpy as jnp
from jax import lax
from jax.sharding import PartitionSpec as P

CELL_DEV = 4
PSF_R = 8
DET_R = 4
CHUNKS = 4


det_sigma = 3.0


def extended(array, sides, width):
    for axis, dim in sides:
        size, length = (lax.axis_size(axis), array.shape[dim])
        up = [(i, (i + 1) % size) for i in range(size - 1)]
        down = [(j, i) for i, j in up]
        last = lax.slice_in_dim(array, length - width, length, axis=dim)
        initial = lax.slice_in_dim(array, 0, width, axis=dim)
        before = lax.ppermute(last, axis, up)
        after = lax.ppermute(initial, axis, down)
        array = jnp.concatenate([before, array, after], axis=dim)
    return array


def lanczos_tap(spacing):
    return jnp.where(jnp.abs(spacing) < 3.0, jnp.sinc(spacing) * jnp.sinc(spacing / 3.0), 0.0)


def block_kernels(shift, spread, side):
    band = PSF_R + 4
    spacing = jnp.arange(-band, band + 1, dtype=jnp.float32)
    weight_total = jnp.zeros_like(spread)
    summed = jnp.zeros((shift.shape[0], 2 * band + 1), jnp.float32)
    for tap_shift in range(-PSF_R, PSF_R + 1):
        tap_weight = jnp.exp(-spread * float(tap_shift * tap_shift))
        weight_total = weight_total + tap_weight
        summed = summed + tap_weight[:, None] * lanczos_tap(
            spacing[None] + (shift[:, None] + float(tap_shift))
        )
    values = (summed / weight_total[:, None]).astype(jnp.bfloat16)
    position = jnp.arange(side, dtype=jnp.int32)
    lag = position[:, None] - position[None, :]
    matrix = jnp.zeros((shift.shape[0], side, side), jnp.bfloat16)
    for index in range(2 * band + 1):
        matrix = jnp.where((lag == index - band)[None], values[:, index, None, None], matrix)
    return matrix


def filter_taps():
    values = [
        math.exp(-float(tap * tap) / (2.0 * det_sigma * det_sigma))
        for tap in range(-DET_R, DET_R + 1)
    ]
    whole = sum(values)
    return [value / whole for value in values]


def smooth_columns(padded, width):
    taps = filter_taps()
    total = jnp.zeros((padded.shape[0], width), jnp.float32)
    for index, tap in enumerate(range(-DET_R, DET_R + 1)):
        total = total + taps[index] * padded[:, DET_R + tap : DET_R + tap + width]
    return total


def smooth_rows_valid(framed, height):
    taps = filter_taps()
    total = jnp.zeros((height, framed.shape[1]), jnp.float32)
    for index, tap in enumerate(range(-DET_R, DET_R + 1)):
        total = total + taps[index] * framed[DET_R + tap : DET_R + tap + height, :]
    return total


def local(images, offsets, widths, weights, dest, cells, band_gain):
    side = images.shape[-1]
    count = images.shape[1]
    sect_count = lax.axis_size("sect")
    sub_count = lax.axis_size("sub")
    owners = sect_count * sub_count
    capacity = max(2, -(-2 * count // owners))
    slot_count = owners * capacity
    col_kernel = block_kernels(offsets[0, :, 1], widths[0, :, 1], side)
    target = dest[0]
    same_owner = target[:, None] == target[None, :]
    block_order = jnp.arange(count, dtype=jnp.int32)
    earlier = block_order[None, :] < block_order[:, None]
    rank_within = jnp.sum(jnp.logical_and(same_owner, earlier), axis=1)
    slot_index = target * capacity + rank_within
    matching = jnp.arange(slot_count, dtype=jnp.int32)[:, None] == slot_index[None, :]
    source = jnp.sum(jnp.where(matching, block_order[None, :], 0), axis=1)
    placing = matching.astype(jnp.bfloat16)
    cell_weight = jnp.where(
        cells[0][:, None] == jnp.arange(CELL_DEV, dtype=jnp.int32)[None, :],
        weights[0][:, None],
        jnp.zeros((), jnp.bfloat16),
    )
    packed_weight = jnp.dot(placing, cell_weight, preferred_element_type=jnp.float32).astype(
        jnp.bfloat16
    )
    received_weight = lax.all_to_all(
        packed_weight.reshape(owners, capacity, CELL_DEV),
        ("sect", "sub"),
        split_axis=0,
        concat_axis=0,
        tiled=True,
    ).reshape(slot_count, CELL_DEV)
    denominator = jnp.sum(received_weight.astype(jnp.float32), axis=0)
    rows = side // CHUNKS
    staged = (images[0], offsets[0, :, 0], widths[0, :, 0], col_kernel)
    pieces = []
    done = []
    for chunk in range(CHUNKS):
        if chunk >= 2:
            done[chunk - 2], staged = lax.optimization_barrier((done[chunk - 2], staged))
        blocks, shift, spread, columns = staged
        row_kernel = block_kernels(shift, spread, side)[:, chunk * rows : (chunk + 1) * rows]
        section = jnp.einsum(
            "bij,bjk->bik", row_kernel, blocks, preferred_element_type=jnp.float32
        ).astype(jnp.bfloat16)
        warped = jnp.einsum(
            "bij,bkj->bik", section, columns, preferred_element_type=jnp.float32
        ).astype(jnp.bfloat16)
        packed = jnp.take(warped, source, axis=0)
        done.append(
            lax.all_to_all(
                packed.reshape(owners, capacity, rows, side),
                ("sect", "sub"),
                split_axis=0,
                concat_axis=0,
                tiled=True,
            )
        )
    for chunk in range(CHUNKS):
        received = done[chunk].reshape(slot_count, rows, side)
        pieces.append(
            jnp.einsum(
                "sc,sij->cij", received_weight, received, preferred_element_type=jnp.float32
            )
        )
    numerator = jnp.concatenate(pieces, axis=1)
    cell_mean = (numerator / jnp.maximum(denominator, 1.0)[:, None, None]).astype(jnp.bfloat16)
    coadd = cell_mean.transpose(1, 0, 2).reshape(side, CELL_DEV * side)
    padded = extended(coadd, ((("sect", "sub"), 1),), DET_R)
    band_count = lax.axis_size("band")
    height = side // band_count
    framed = jnp.pad(padded, ((DET_R, DET_R), (0, 0)))
    windows = jnp.stack(
        [framed[k * height : k * height + height + 2 * DET_R] for k in range(band_count)]
    )
    gathered = lax.all_to_all(windows, "band", split_axis=0, concat_axis=0, tiled=True)
    gains = lax.all_gather(band_gain, "band", tiled=True)
    combined = jnp.zeros(gathered.shape[1:], jnp.float32)
    for k in range(band_count):
        combined = combined + gains[k] * gathered[k].astype(jnp.float32)
    detection = smooth_rows_valid(smooth_columns(combined, CELL_DEV * side), height)
    return (coadd[None], detection)


def solution(mesh):
    return jax.shard_map(
        local,
        mesh=mesh,
        in_specs=(
            P("band", ("groups", "sect", "sub"), None, None),
            P("band", ("groups", "sect", "sub"), None),
            P("band", ("groups", "sect", "sub"), None),
            P("band", ("groups", "sect", "sub")),
            P("band", ("groups", "sect", "sub")),
            P("band", ("groups", "sect", "sub")),
            P("band"),
        ),
        out_specs=(
            P("band", None, ("groups", "sect", "sub")),
            P("band", ("groups", "sect", "sub")),
        ),
        check_vma=False,
    )
```

```python
import math

import jax
import jax.numpy as jnp
from jax import lax
from jax.sharding import PartitionSpec as P

CELL_DEV = 4
PSF_R = 8
DET_R = 4


det_sigma = 3.0


def extended(array, sides, width):
    for axis, dim in sides:
        size, length = (lax.axis_size(axis), array.shape[dim])
        up = [(i, (i + 1) % size) for i in range(size - 1)]
        down = [(j, i) for i, j in up]
        last = lax.slice_in_dim(array, length - width, length, axis=dim)
        initial = lax.slice_in_dim(array, 0, width, axis=dim)
        before = lax.ppermute(last, axis, up)
        after = lax.ppermute(initial, axis, down)
        array = jnp.concatenate([before, array, after], axis=dim)
    return array


def lanczos_tap(spacing):
    return jnp.where(jnp.abs(spacing) < 3.0, jnp.sinc(spacing) * jnp.sinc(spacing / 3.0), 0.0)


def block_kernels(shift, spread, side):
    band = PSF_R + 4
    spacing = jnp.arange(-band, band + 1, dtype=jnp.float32)
    weight_total = jnp.zeros_like(spread)
    summed = jnp.zeros((shift.shape[0], 2 * band + 1), jnp.float32)
    for tap_shift in range(-PSF_R, PSF_R + 1):
        tap_weight = jnp.exp(-spread * float(tap_shift * tap_shift))
        weight_total = weight_total + tap_weight
        summed = summed + tap_weight[:, None] * lanczos_tap(
            spacing[None] + (shift[:, None] + float(tap_shift))
        )
    values = (summed / weight_total[:, None]).astype(jnp.bfloat16)
    position = jnp.arange(side, dtype=jnp.int32)
    lag = position[:, None] - position[None, :]
    matrix = jnp.zeros((shift.shape[0], side, side), jnp.bfloat16)
    for index in range(2 * band + 1):
        matrix = jnp.where((lag == index - band)[None], values[:, index, None, None], matrix)
    return matrix


def filter_taps():
    values = [
        math.exp(-float(tap * tap) / (2.0 * det_sigma * det_sigma))
        for tap in range(-DET_R, DET_R + 1)
    ]
    whole = sum(values)
    return [value / whole for value in values]


def smooth_columns(padded, width):
    taps = filter_taps()
    total = jnp.zeros((padded.shape[0], width), jnp.float32)
    for index, tap in enumerate(range(-DET_R, DET_R + 1)):
        total = total + taps[index] * padded[:, DET_R + tap : DET_R + tap + width]
    return total


def smooth_rows_valid(framed, height):
    taps = filter_taps()
    total = jnp.zeros((height, framed.shape[1]), jnp.float32)
    for index, tap in enumerate(range(-DET_R, DET_R + 1)):
        total = total + taps[index] * framed[DET_R + tap : DET_R + tap + height, :]
    return total


def local(images, offsets, widths, weights, dest, cells, band_gain):
    side = images.shape[-1]
    count = images.shape[1]
    sect_count = lax.axis_size("sect")
    sub_count = lax.axis_size("sub")
    owners = sect_count * sub_count
    capacity = max(2, -(-2 * count // owners))
    slot_count = owners * capacity
    row_kernel = block_kernels(offsets[0, :, 0], widths[0, :, 0], side)
    col_kernel = block_kernels(offsets[0, :, 1], widths[0, :, 1], side)
    section = jnp.einsum(
        "bij,bjk->bik", row_kernel, images[0], preferred_element_type=jnp.float32
    ).astype(jnp.bfloat16)
    warped = jnp.einsum(
        "bij,bkj->bik", section, col_kernel, preferred_element_type=jnp.float32
    ).astype(jnp.bfloat16)
    target = dest[0]
    same_owner = target[:, None] == target[None, :]
    block_order = jnp.arange(count, dtype=jnp.int32)
    earlier = block_order[None, :] < block_order[:, None]
    rank_within = jnp.sum(jnp.logical_and(same_owner, earlier), axis=1)
    slot_index = target * capacity + rank_within
    placing = (jnp.arange(slot_count, dtype=jnp.int32)[:, None] == slot_index[None, :]).astype(
        jnp.bfloat16
    )
    packed = jnp.einsum(
        "sb,bij->sij", placing, warped, preferred_element_type=jnp.float32
    ).astype(jnp.bfloat16)
    cell_weight = jnp.where(
        cells[0][:, None] == jnp.arange(CELL_DEV, dtype=jnp.int32)[None, :],
        weights[0][:, None],
        jnp.zeros((), jnp.bfloat16),
    )
    packed_weight = jnp.dot(placing, cell_weight, preferred_element_type=jnp.float32).astype(
        jnp.bfloat16
    )
    received, received_weight = (
        lax.all_to_all(
            packed.reshape(owners, capacity, side, side),
            ("sect", "sub"),
            split_axis=0,
            concat_axis=0,
            tiled=True,
        ),
        lax.all_to_all(
            packed_weight.reshape(owners, capacity, CELL_DEV),
            ("sect", "sub"),
            split_axis=0,
            concat_axis=0,
            tiled=True,
        ),
    )
    received = received.reshape(slot_count, side, side)
    received_weight = received_weight.reshape(slot_count, CELL_DEV)
    numerator = jnp.einsum(
        "sc,sij->cij", received_weight, received, preferred_element_type=jnp.float32
    )
    denominator = jnp.sum(received_weight.astype(jnp.float32), axis=0)
    cell_mean = (numerator / jnp.maximum(denominator, 1.0)[:, None, None]).astype(jnp.bfloat16)
    coadd = (
        cell_mean.reshape(CELL_DEV, side, side).transpose(1, 0, 2).reshape(side, CELL_DEV * side)
    )
    padded = extended(coadd, ((("sect", "sub"), 1),), DET_R)
    band_count = lax.axis_size("band")
    height = side // band_count
    framed = jnp.pad(band_gain[0] * padded.astype(jnp.float32), ((DET_R, DET_R), (0, 0)))
    windows = jnp.stack(
        [framed[k * height : k * height + height + 2 * DET_R] for k in range(band_count)]
    )
    gathered = lax.all_to_all(windows, "band", split_axis=0, concat_axis=0, tiled=True)
    combined = jnp.sum(gathered, axis=0)
    detection = smooth_rows_valid(smooth_columns(combined, CELL_DEV * side), height)
    return (coadd[None], detection)


def solution(mesh):
    return jax.shard_map(
        local,
        mesh=mesh,
        in_specs=(
            P("band", ("groups", "sect", "sub"), None, None),
            P("band", ("groups", "sect", "sub"), None),
            P("band", ("groups", "sect", "sub"), None),
            P("band", ("groups", "sect", "sub")),
            P("band", ("groups", "sect", "sub")),
            P("band", ("groups", "sect", "sub")),
            P("band"),
        ),
        out_specs=(
            P("band", None, ("groups", "sect", "sub")),
            P("band", ("groups", "sect", "sub")),
        ),
        check_vma=False,
    )
```

```python
import math

import jax
import jax.numpy as jnp
from jax import lax
from jax.sharding import PartitionSpec as P

CELL_DEV = 4
PSF_R = 8
DET_R = 4


det_sigma = 3.0


def extended(array, sides, width):
    for axis, dim in sides:
        size, length = (lax.axis_size(axis), array.shape[dim])
        up = [(i, (i + 1) % size) for i in range(size - 1)]
        down = [(j, i) for i, j in up]
        last = lax.slice_in_dim(array, length - width, length, axis=dim)
        initial = lax.slice_in_dim(array, 0, width, axis=dim)
        before = lax.ppermute(last, axis, up)
        after = lax.ppermute(initial, axis, down)
        array = jnp.concatenate([before, array, after], axis=dim)
    return array


def lanczos_tap(spacing):
    return jnp.where(jnp.abs(spacing) < 3.0, jnp.sinc(spacing) * jnp.sinc(spacing / 3.0), 0.0)


def block_kernels(shift, spread, side):
    band = PSF_R + 4
    spacing = jnp.arange(-band, band + 1, dtype=jnp.float32)
    weight_total = jnp.zeros_like(spread)
    summed = jnp.zeros((shift.shape[0], 2 * band + 1), jnp.float32)
    for tap_shift in range(-PSF_R, PSF_R + 1):
        tap_weight = jnp.exp(-spread * float(tap_shift * tap_shift))
        weight_total = weight_total + tap_weight
        summed = summed + tap_weight[:, None] * lanczos_tap(
            spacing[None] + (shift[:, None] + float(tap_shift))
        )
    values = (summed / weight_total[:, None]).astype(jnp.bfloat16)
    position = jnp.arange(side, dtype=jnp.int32)
    lag = position[:, None] - position[None, :]
    matrix = jnp.zeros((shift.shape[0], side, side), jnp.bfloat16)
    for index in range(2 * band + 1):
        matrix = jnp.where((lag == index - band)[None], values[:, index, None, None], matrix)
    return matrix


def filter_taps():
    values = [
        math.exp(-float(tap * tap) / (2.0 * det_sigma * det_sigma))
        for tap in range(-DET_R, DET_R + 1)
    ]
    whole = sum(values)
    return [value / whole for value in values]


def smooth_columns(padded, width):
    taps = filter_taps()
    total = jnp.zeros((padded.shape[0], width), jnp.float32)
    for index, tap in enumerate(range(-DET_R, DET_R + 1)):
        total = total + taps[index] * padded[:, DET_R + tap : DET_R + tap + width]
    return total


def smooth_rows_valid(framed, height):
    taps = filter_taps()
    total = jnp.zeros((height, framed.shape[1]), jnp.float32)
    for index, tap in enumerate(range(-DET_R, DET_R + 1)):
        total = total + taps[index] * framed[DET_R + tap : DET_R + tap + height, :]
    return total


def local(images, offsets, widths, weights, dest, cells, band_gain):
    side = images.shape[-1]
    count = images.shape[1]
    sect_count = lax.axis_size("sect")
    sub_count = lax.axis_size("sub")
    owners = sect_count * sub_count
    capacity = max(2, -(-2 * count // owners))
    slot_count = owners * capacity
    row_kernel = block_kernels(offsets[0, :, 0], widths[0, :, 0], side)
    col_kernel = block_kernels(offsets[0, :, 1], widths[0, :, 1], side)
    section = jnp.einsum(
        "bij,bjk->bik", row_kernel, images[0], preferred_element_type=jnp.float32
    ).astype(jnp.bfloat16)
    warped = jnp.einsum(
        "bij,bkj->bik", section, col_kernel, preferred_element_type=jnp.float32
    ).astype(jnp.bfloat16)
    target = dest[0]
    same_owner = target[:, None] == target[None, :]
    block_order = jnp.arange(count, dtype=jnp.int32)
    earlier = block_order[None, :] < block_order[:, None]
    rank_within = jnp.sum(jnp.logical_and(same_owner, earlier), axis=1)
    slot_index = target * capacity + rank_within
    matching = jnp.arange(slot_count, dtype=jnp.int32)[:, None] == slot_index[None, :]
    source = jnp.sum(jnp.where(matching, block_order[None, :], 0), axis=1)
    placing = matching.astype(jnp.bfloat16)
    packed = jnp.take(warped, source, axis=0, mode="clip")
    cell_weight = jnp.where(
        cells[0][:, None] == jnp.arange(CELL_DEV, dtype=jnp.int32)[None, :],
        weights[0][:, None],
        jnp.zeros((), jnp.bfloat16),
    )
    packed_weight = jnp.dot(placing, cell_weight, preferred_element_type=jnp.float32).astype(
        jnp.bfloat16
    )
    received, received_weight = (
        lax.all_to_all(
            packed.reshape(owners, capacity * side, side),
            ("sect", "sub"),
            split_axis=0,
            concat_axis=0,
            tiled=True,
        ),
        lax.all_to_all(
            packed_weight.reshape(owners, capacity, CELL_DEV),
            ("sect", "sub"),
            split_axis=0,
            concat_axis=0,
            tiled=True,
        ),
    )
    received = received.reshape(slot_count, side, side)
    received_weight = received_weight.reshape(slot_count, CELL_DEV)
    numerator = jnp.sum(
        received_weight.astype(jnp.float32)[:, :, None, None]
        * received.astype(jnp.float32)[:, None],
        axis=0,
    )
    denominator = jnp.sum(received_weight.astype(jnp.float32), axis=0)
    cell_mean = (numerator / jnp.maximum(denominator, 1.0)[:, None, None]).astype(jnp.bfloat16)
    coadd = (
        cell_mean.reshape(CELL_DEV, side, side).transpose(1, 0, 2).reshape(side, CELL_DEV * side)
    )
    padded = extended(coadd, ((("sect", "sub"), 1),), DET_R)
    band_count = lax.axis_size("band")
    height = side // band_count
    framed = jnp.pad(band_gain[0] * padded.astype(jnp.float32), ((DET_R, DET_R), (0, 0)))
    windows = jnp.stack(
        [framed[k * height : k * height + height + 2 * DET_R] for k in range(band_count)]
    )
    gathered = lax.all_to_all(windows, "band", split_axis=0, concat_axis=0, tiled=True)
    combined = jnp.sum(gathered, axis=0)
    detection = smooth_rows_valid(smooth_columns(combined, CELL_DEV * side), height)
    return (coadd[None], detection)


def solution(mesh):
    return jax.shard_map(
        local,
        mesh=mesh,
        in_specs=(
            P("band", ("groups", "sect", "sub"), None, None),
            P("band", ("groups", "sect", "sub"), None),
            P("band", ("groups", "sect", "sub"), None),
            P("band", ("groups", "sect", "sub")),
            P("band", ("groups", "sect", "sub")),
            P("band", ("groups", "sect", "sub")),
            P("band"),
        ),
        out_specs=(
            P("band", None, ("groups", "sect", "sub")),
            P("band", ("groups", "sect", "sub")),
        ),
        check_vma=False,
    )
```

```python
import math

import jax
import jax.numpy as jnp
from jax import lax
from jax.sharding import PartitionSpec as P

CELL_DEV = 4
PSF_R = 8
DET_R = 4


det_sigma = 3.0


def extended(array, sides, width):
    for axis, dim in sides:
        size, length = (lax.axis_size(axis), array.shape[dim])
        up = [(i, (i + 1) % size) for i in range(size - 1)]
        down = [(j, i) for i, j in up]
        last = lax.slice_in_dim(array, length - width, length, axis=dim)
        initial = lax.slice_in_dim(array, 0, width, axis=dim)
        before = lax.ppermute(last, axis, up)
        after = lax.ppermute(initial, axis, down)
        array = jnp.concatenate([before, array, after], axis=dim)
    return array


def lanczos_tap(spacing):
    return jnp.where(jnp.abs(spacing) < 3.0, jnp.sinc(spacing) * jnp.sinc(spacing / 3.0), 0.0)


def block_kernels(shift, spread, side):
    band = PSF_R + 4
    spacing = jnp.arange(-band, band + 1, dtype=jnp.float32)
    weight_total = jnp.zeros_like(spread)
    summed = jnp.zeros((shift.shape[0], 2 * band + 1), jnp.float32)
    for tap_shift in range(-PSF_R, PSF_R + 1):
        tap_weight = jnp.exp(-spread * float(tap_shift * tap_shift))
        weight_total = weight_total + tap_weight
        summed = summed + tap_weight[:, None] * lanczos_tap(
            spacing[None] + (shift[:, None] + float(tap_shift))
        )
    values = (summed / weight_total[:, None]).astype(jnp.bfloat16)
    position = jnp.arange(side, dtype=jnp.int32)
    lag = position[:, None] - position[None, :]
    matrix = jnp.zeros((shift.shape[0], side, side), jnp.bfloat16)
    for index in range(2 * band + 1):
        matrix = jnp.where((lag == index - band)[None], values[:, index, None, None], matrix)
    return matrix


def filter_taps():
    values = [
        math.exp(-float(tap * tap) / (2.0 * det_sigma * det_sigma))
        for tap in range(-DET_R, DET_R + 1)
    ]
    whole = sum(values)
    return [value / whole for value in values]


def smooth_columns(padded, width):
    taps = filter_taps()
    total = jnp.zeros((padded.shape[0], width), jnp.float32)
    for index, tap in enumerate(range(-DET_R, DET_R + 1)):
        total = total + taps[index] * padded[:, DET_R + tap : DET_R + tap + width]
    return total


def smooth_rows_valid(framed, height):
    taps = filter_taps()
    total = jnp.zeros((height, framed.shape[1]), jnp.float32)
    for index, tap in enumerate(range(-DET_R, DET_R + 1)):
        total = total + taps[index] * framed[DET_R + tap : DET_R + tap + height, :]
    return total


def local(images, offsets, widths, weights, dest, cells, band_gain):
    side = images.shape[-1]
    count = images.shape[1]
    sect_count = lax.axis_size("sect")
    sub_count = lax.axis_size("sub")
    owners = sect_count * sub_count
    capacity = max(2, -(-2 * count // owners))
    slot_count = owners * capacity
    row_kernel = block_kernels(offsets[0, :, 0], widths[0, :, 0], side)
    col_kernel = block_kernels(offsets[0, :, 1], widths[0, :, 1], side)
    section = jnp.einsum(
        "bij,bjk->bik", row_kernel, images[0], preferred_element_type=jnp.float32
    ).astype(jnp.bfloat16)
    warped = jnp.einsum(
        "bij,bkj->bik", section, col_kernel, preferred_element_type=jnp.float32
    ).astype(jnp.bfloat16)
    target = dest[0]
    same_owner = target[:, None] == target[None, :]
    block_order = jnp.arange(count, dtype=jnp.int32)
    earlier = block_order[None, :] < block_order[:, None]
    rank_within = jnp.sum(jnp.logical_and(same_owner, earlier), axis=1)
    slot_index = target * capacity + rank_within
    matching = jnp.arange(slot_count, dtype=jnp.int32)[:, None] == slot_index[None, :]
    source = jnp.sum(jnp.where(matching, block_order[None, :], 0), axis=1)
    placing = matching.astype(jnp.bfloat16)
    packed = jnp.take(warped, source, axis=0, mode="clip")
    cell_weight = jnp.where(
        cells[0][:, None] == jnp.arange(CELL_DEV, dtype=jnp.int32)[None, :],
        weights[0][:, None],
        jnp.zeros((), jnp.bfloat16),
    )
    packed_weight = jnp.dot(placing, cell_weight, preferred_element_type=jnp.float32).astype(
        jnp.bfloat16
    )
    received, received_weight = (
        lax.all_to_all(
            packed.reshape(owners, capacity * side, side),
            ("sect", "sub"),
            split_axis=0,
            concat_axis=0,
            tiled=True,
        ),
        lax.all_to_all(
            packed_weight.reshape(owners, capacity, CELL_DEV),
            ("sect", "sub"),
            split_axis=0,
            concat_axis=0,
            tiled=True,
        ),
    )
    received = received.reshape(slot_count, side, side)
    received_weight = received_weight.reshape(slot_count, CELL_DEV)
    numerator = jnp.einsum(
        "sc,sij->cij", received_weight, received, preferred_element_type=jnp.float32
    )
    denominator = jnp.sum(received_weight.astype(jnp.float32), axis=0)
    cell_mean = (numerator / jnp.maximum(denominator, 1.0)[:, None, None]).astype(jnp.bfloat16)
    coadd = (
        cell_mean.reshape(CELL_DEV, side, side).transpose(1, 0, 2).reshape(side, CELL_DEV * side)
    )
    padded = extended(coadd, ((("sect", "sub"), 1),), DET_R)
    band_count = lax.axis_size("band")
    height = side // band_count
    framed = jnp.pad(band_gain[0] * padded.astype(jnp.float32), ((DET_R, DET_R), (0, 0)))
    windows = jnp.stack(
        [framed[k * height : k * height + height + 2 * DET_R] for k in range(band_count)]
    )
    gathered = lax.all_to_all(windows, "band", split_axis=0, concat_axis=0, tiled=True)
    combined = jnp.sum(gathered, axis=0)
    detection = smooth_rows_valid(smooth_columns(combined, CELL_DEV * side), height)
    return (coadd[None], detection)


def solution(mesh):
    return jax.shard_map(
        local,
        mesh=mesh,
        in_specs=(
            P("band", ("groups", "sect", "sub"), None, None),
            P("band", ("groups", "sect", "sub"), None),
            P("band", ("groups", "sect", "sub"), None),
            P("band", ("groups", "sect", "sub")),
            P("band", ("groups", "sect", "sub")),
            P("band", ("groups", "sect", "sub")),
            P("band"),
        ),
        out_specs=(
            P("band", None, ("groups", "sect", "sub")),
            P("band", ("groups", "sect", "sub")),
        ),
        check_vma=False,
    )
```

```python
import math

import jax
import jax.numpy as jnp
from jax import lax
from jax.sharding import PartitionSpec as P

CELL_DEV = 4
PSF_R = 8
DET_R = 4


det_sigma = 3.0


def extended(array, sides, width):
    for axis, dim in sides:
        size, length = (lax.axis_size(axis), array.shape[dim])
        up = [(i, (i + 1) % size) for i in range(size - 1)]
        down = [(j, i) for i, j in up]
        last = lax.slice_in_dim(array, length - width, length, axis=dim)
        initial = lax.slice_in_dim(array, 0, width, axis=dim)
        before = lax.ppermute(last, axis, up)
        after = lax.ppermute(initial, axis, down)
        array = jnp.concatenate([before, array, after], axis=dim)
    return array


def lanczos_tap(spacing):
    return jnp.where(jnp.abs(spacing) < 3.0, jnp.sinc(spacing) * jnp.sinc(spacing / 3.0), 0.0)


def block_kernels(shift, spread, side):
    band = PSF_R + 4
    spacing = jnp.arange(-band, band + 1, dtype=jnp.float32)
    tap = jnp.arange(-PSF_R, PSF_R + 1, dtype=jnp.float32)
    tap_weight = jnp.exp(-spread[..., None] * (tap * tap))
    weight_total = jnp.sum(tap_weight, axis=-1)
    taps = lanczos_tap(spacing + (shift[..., None, None] + tap[:, None]))
    summed = jnp.sum(tap_weight[..., None] * taps, axis=-2)
    values = (summed / weight_total[..., None]).astype(jnp.bfloat16)
    position = jnp.arange(side, dtype=jnp.int32)
    lag = position[:, None] - position[None, :]
    matrix = jnp.zeros(shift.shape + (side, side), jnp.bfloat16)
    for index in range(2 * band + 1):
        matrix = jnp.where(lag == index - band, values[..., index, None, None], matrix)
    return matrix


def gain_pieces(gain):
    high = lax.reduce_precision(gain, exponent_bits=8, mantissa_bits=7)
    rest = gain - high
    middle = lax.reduce_precision(rest, exponent_bits=8, mantissa_bits=7)
    low = lax.reduce_precision(rest - middle, exponent_bits=8, mantissa_bits=7)
    return jnp.stack([high, middle, low]).astype(jnp.bfloat16)


def filter_taps():
    values = [
        math.exp(-float(tap * tap) / (2.0 * det_sigma * det_sigma))
        for tap in range(-DET_R, DET_R + 1)
    ]
    whole = sum(values)
    return [value / whole for value in values]


def smooth_columns(padded, width):
    taps = filter_taps()
    total = jnp.zeros((padded.shape[0], width), jnp.float32)
    for index, tap in enumerate(range(-DET_R, DET_R + 1)):
        total = total + taps[index] * padded[:, DET_R + tap : DET_R + tap + width]
    return total


def smooth_rows_valid(framed, height):
    taps = filter_taps()
    total = jnp.zeros((height, framed.shape[1]), jnp.float32)
    for index, tap in enumerate(range(-DET_R, DET_R + 1)):
        total = total + taps[index] * framed[DET_R + tap : DET_R + tap + height, :]
    return total


def local(images, offsets, widths, weights, dest, cells, band_gain):
    side = images.shape[-1]
    count = images.shape[1]
    sect_count = lax.axis_size("sect")
    sub_count = lax.axis_size("sub")
    owners = sect_count * sub_count
    capacity = max(2, -(-2 * count // owners))
    slot_count = owners * capacity
    kernels = block_kernels(offsets[0], widths[0], side)
    row_kernel = kernels[:, 0]
    col_kernel = kernels[:, 1]
    section = jnp.einsum(
        "bij,bjk->bik", row_kernel, images[0], preferred_element_type=jnp.float32
    ).astype(jnp.bfloat16)
    warped = jnp.einsum(
        "bij,bkj->bik", section, col_kernel, preferred_element_type=jnp.float32
    ).astype(jnp.bfloat16)
    target = dest[0]
    same_owner = target[:, None] == target[None, :]
    block_order = jnp.arange(count, dtype=jnp.int32)
    earlier = block_order[None, :] < block_order[:, None]
    rank_within = jnp.sum(jnp.logical_and(same_owner, earlier), axis=1)
    slot_index = target * capacity + rank_within
    matching = jnp.arange(slot_count, dtype=jnp.int32)[:, None] == slot_index[None, :]
    source = jnp.sum(jnp.where(matching, block_order[None, :], 0), axis=1)
    placing = matching.astype(jnp.bfloat16)
    packed = jnp.take(warped, source, axis=0, mode="clip")
    cell_weight = jnp.where(
        cells[0][:, None] == jnp.arange(CELL_DEV, dtype=jnp.int32)[None, :],
        weights[0][:, None],
        jnp.zeros((), jnp.bfloat16),
    )
    packed_weight = jnp.dot(placing, cell_weight, preferred_element_type=jnp.float32).astype(
        jnp.bfloat16
    )
    received, received_weight = (
        lax.all_to_all(
            packed.reshape(owners, capacity * side, side),
            ("sect", "sub"),
            split_axis=0,
            concat_axis=0,
            tiled=True,
        ),
        lax.all_to_all(
            packed_weight.reshape(owners, capacity, CELL_DEV),
            ("sect", "sub"),
            split_axis=0,
            concat_axis=0,
            tiled=True,
        ),
    )
    received = received.reshape(slot_count, side, side)
    received_weight = received_weight.reshape(slot_count, CELL_DEV)
    numerator = jnp.einsum(
        "sc,sij->cij", received_weight, received, preferred_element_type=jnp.float32
    )
    denominator = jnp.sum(received_weight.astype(jnp.float32), axis=0)
    cell_mean = (numerator / jnp.maximum(denominator, 1.0)[:, None, None]).astype(jnp.bfloat16)
    coadd = (
        cell_mean.reshape(CELL_DEV, side, side).transpose(1, 0, 2).reshape(side, CELL_DEV * side)
    )
    padded = extended(coadd, ((("sect", "sub"), 1),), DET_R)
    band_count = lax.axis_size("band")
    height = side // band_count
    framed = jnp.pad(padded, ((DET_R, DET_R), (0, 0)))
    gain_row = jnp.zeros((1, padded.shape[1]), jnp.bfloat16).at[0, :3].set(gain_pieces(band_gain[0]))
    windows = jnp.stack(
        [
            jnp.concatenate([framed[k * height : k * height + height + 2 * DET_R], gain_row])
            for k in range(band_count)
        ]
    )
    gathered = lax.all_to_all(windows, "band", split_axis=0, concat_axis=0, tiled=True)
    span = height + 2 * DET_R
    gains = jnp.sum(gathered[:, span, :3].astype(jnp.float32), axis=1)
    combined = jnp.zeros((span, padded.shape[1]), jnp.float32)
    for k in range(band_count):
        combined = combined + gains[k] * gathered[k, :span].astype(jnp.float32)
    detection = smooth_rows_valid(smooth_columns(combined, CELL_DEV * side), height)
    return (coadd[None], detection)


def solution(mesh):
    return jax.shard_map(
        local,
        mesh=mesh,
        in_specs=(
            P("band", ("groups", "sect", "sub"), None, None),
            P("band", ("groups", "sect", "sub"), None),
            P("band", ("groups", "sect", "sub"), None),
            P("band", ("groups", "sect", "sub")),
            P("band", ("groups", "sect", "sub")),
            P("band", ("groups", "sect", "sub")),
            P("band"),
        ),
        out_specs=(
            P("band", None, ("groups", "sect", "sub")),
            P("band", ("groups", "sect", "sub")),
        ),
        check_vma=False,
    )
```

```python
import math

import jax
import jax.numpy as jnp
from jax import lax
from jax.sharding import PartitionSpec as P

CELL_DEV = 4
PSF_R = 8
DET_R = 4


det_sigma = 3.0


def extended(array, sides, width):
    for axis, dim in sides:
        size, length = (lax.axis_size(axis), array.shape[dim])
        up = [(i, (i + 1) % size) for i in range(size - 1)]
        down = [(j, i) for i, j in up]
        last = lax.slice_in_dim(array, length - width, length, axis=dim)
        initial = lax.slice_in_dim(array, 0, width, axis=dim)
        before = lax.ppermute(last, axis, up)
        after = lax.ppermute(initial, axis, down)
        array = jnp.concatenate([before, array, after], axis=dim)
    return array


def lanczos_tap(spacing):
    return jnp.where(jnp.abs(spacing) < 3.0, jnp.sinc(spacing) * jnp.sinc(spacing / 3.0), 0.0)


def band_values(shift, spread):
    band = PSF_R + 4
    spacing = jnp.arange(-band, band + 1, dtype=jnp.float32)
    tap = jnp.arange(-PSF_R, PSF_R + 1, dtype=jnp.float32)
    tap_weight = jnp.exp(-spread[..., None] * (tap * tap))
    weight_total = jnp.sum(tap_weight, axis=-1)
    taps = lanczos_tap(spacing + (shift[..., None, None] + tap[:, None]))
    summed = jnp.sum(tap_weight[..., None] * taps, axis=-2)
    return (summed / weight_total[..., None]).astype(jnp.bfloat16)


def toeplitz(values, side):
    band = PSF_R + 4
    position = jnp.arange(side, dtype=jnp.int32)
    lag = position[:, None] - position[None, :]
    matrix = jnp.zeros(values.shape[:-1] + (side, side), jnp.bfloat16)
    for index in range(2 * band + 1):
        matrix = jnp.where(lag == index - band, values[..., index, None, None], matrix)
    return matrix


def gain_pieces(gain):
    high = lax.reduce_precision(gain, exponent_bits=8, mantissa_bits=7)
    rest = gain - high
    middle = lax.reduce_precision(rest, exponent_bits=8, mantissa_bits=7)
    low = lax.reduce_precision(rest - middle, exponent_bits=8, mantissa_bits=7)
    return jnp.stack([high, middle, low]).astype(jnp.bfloat16)


def filter_taps():
    values = [
        math.exp(-float(tap * tap) / (2.0 * det_sigma * det_sigma))
        for tap in range(-DET_R, DET_R + 1)
    ]
    whole = sum(values)
    return [value / whole for value in values]


def smooth_columns(padded, width):
    taps = filter_taps()
    total = jnp.zeros((padded.shape[0], width), jnp.float32)
    for index, tap in enumerate(range(-DET_R, DET_R + 1)):
        total = total + taps[index] * padded[:, DET_R + tap : DET_R + tap + width]
    return total


def smooth_rows_valid(framed, height):
    taps = filter_taps()
    total = jnp.zeros((height, framed.shape[1]), jnp.float32)
    for index, tap in enumerate(range(-DET_R, DET_R + 1)):
        total = total + taps[index] * framed[DET_R + tap : DET_R + tap + height, :]
    return total


def local(images, offsets, widths, weights, dest, cells, band_gain):
    side = images.shape[-1]
    count = images.shape[1]
    sect_count = lax.axis_size("sect")
    sub_count = lax.axis_size("sub")
    owners = sect_count * sub_count
    capacity = max(2, -(-2 * count // owners))
    slot_count = owners * capacity
    values = band_values(offsets[0], widths[0])
    row_kernel = toeplitz(values[:, 0], side)
    col_kernel = toeplitz(values[:, 1], side)
    section = jnp.einsum(
        "bij,bjk->bik", row_kernel, images[0], preferred_element_type=jnp.float32
    ).astype(jnp.bfloat16)
    warped = jnp.einsum(
        "bij,bkj->bik", section, col_kernel, preferred_element_type=jnp.float32
    ).astype(jnp.bfloat16)
    target = dest[0]
    same_owner = target[:, None] == target[None, :]
    block_order = jnp.arange(count, dtype=jnp.int32)
    earlier = block_order[None, :] < block_order[:, None]
    rank_within = jnp.sum(jnp.logical_and(same_owner, earlier), axis=1)
    slot_index = target * capacity + rank_within
    matching = jnp.arange(slot_count, dtype=jnp.int32)[:, None] == slot_index[None, :]
    source = jnp.sum(jnp.where(matching, block_order[None, :], 0), axis=1)
    placing = matching.astype(jnp.bfloat16)
    packed = jnp.take(warped, source, axis=0, mode="clip")
    cell_weight = jnp.where(
        cells[0][:, None] == jnp.arange(CELL_DEV, dtype=jnp.int32)[None, :],
        weights[0][:, None],
        jnp.zeros((), jnp.bfloat16),
    )
    packed_weight = jnp.dot(placing, cell_weight, preferred_element_type=jnp.float32).astype(
        jnp.bfloat16
    )
    received, received_weight = (
        lax.all_to_all(
            packed.reshape(owners, capacity * side, side),
            ("sect", "sub"),
            split_axis=0,
            concat_axis=0,
            tiled=True,
        ),
        lax.all_to_all(
            packed_weight.reshape(owners, capacity, CELL_DEV),
            ("sect", "sub"),
            split_axis=0,
            concat_axis=0,
            tiled=True,
        ),
    )
    received = received.reshape(slot_count, side, side)
    received_weight = received_weight.reshape(slot_count, CELL_DEV)
    numerator = jnp.einsum(
        "sc,sij->cij", received_weight, received, preferred_element_type=jnp.float32
    )
    denominator = jnp.sum(received_weight.astype(jnp.float32), axis=0)
    cell_mean = (numerator / jnp.maximum(denominator, 1.0)[:, None, None]).astype(jnp.bfloat16)
    coadd = (
        cell_mean.reshape(CELL_DEV, side, side).transpose(1, 0, 2).reshape(side, CELL_DEV * side)
    )
    padded = extended(coadd, ((("sect", "sub"), 1),), DET_R)
    band_count = lax.axis_size("band")
    height = side // band_count
    framed = jnp.pad(padded, ((DET_R, DET_R), (0, 0)))
    gain_row = jnp.zeros((1, padded.shape[1]), jnp.bfloat16).at[0, :3].set(gain_pieces(band_gain[0]))
    windows = jnp.stack(
        [
            jnp.concatenate([framed[k * height : k * height + height + 2 * DET_R], gain_row])
            for k in range(band_count)
        ]
    )
    gathered = lax.all_to_all(windows, "band", split_axis=0, concat_axis=0, tiled=True)
    span = height + 2 * DET_R
    gains = jnp.sum(gathered[:, span, :3].astype(jnp.float32), axis=1)
    combined = jnp.zeros((span, padded.shape[1]), jnp.float32)
    for k in range(band_count):
        combined = combined + gains[k] * gathered[k, :span].astype(jnp.float32)
    detection = smooth_rows_valid(smooth_columns(combined, CELL_DEV * side), height)
    return (coadd[None], detection)


def solution(mesh):
    return jax.shard_map(
        local,
        mesh=mesh,
        in_specs=(
            P("band", ("groups", "sect", "sub"), None, None),
            P("band", ("groups", "sect", "sub"), None),
            P("band", ("groups", "sect", "sub"), None),
            P("band", ("groups", "sect", "sub")),
            P("band", ("groups", "sect", "sub")),
            P("band", ("groups", "sect", "sub")),
            P("band"),
        ),
        out_specs=(
            P("band", None, ("groups", "sect", "sub")),
            P("band", ("groups", "sect", "sub")),
        ),
        check_vma=False,
    )
```

```python
import math

import jax
import jax.numpy as jnp
from jax import lax
from jax.sharding import PartitionSpec as P

CELL_DEV = 4
PSF_R = 8
DET_R = 4


det_sigma = 3.0


def extended(array, sides, width):
    for axis, dim in sides:
        size, length = (lax.axis_size(axis), array.shape[dim])
        up = [(i, (i + 1) % size) for i in range(size - 1)]
        down = [(j, i) for i, j in up]
        last = lax.slice_in_dim(array, length - width, length, axis=dim)
        initial = lax.slice_in_dim(array, 0, width, axis=dim)
        before = lax.ppermute(last, axis, up)
        after = lax.ppermute(initial, axis, down)
        array = jnp.concatenate([before, array, after], axis=dim)
    return array


def lanczos_tap(spacing):
    return jnp.where(jnp.abs(spacing) < 3.0, jnp.sinc(spacing) * jnp.sinc(spacing / 3.0), 0.0)


def band_values(shift, spread):
    band = PSF_R + 4
    spacing = jnp.arange(-band, band + 1, dtype=jnp.float32)
    tap = jnp.arange(-PSF_R, PSF_R + 1, dtype=jnp.float32)
    tap_weight = jnp.exp(-spread[..., None] * (tap * tap))
    weight_total = jnp.sum(tap_weight, axis=-1)
    taps = lanczos_tap(spacing + (shift[..., None, None] + tap[:, None]))
    summed = jnp.sum(tap_weight[..., None] * taps, axis=-2)
    return (summed / weight_total[..., None]).astype(jnp.bfloat16)


def toeplitz(values, side):
    band = PSF_R + 4
    position = jnp.arange(side, dtype=jnp.int32)
    lag = position[:, None] - position[None, :]
    matrix = jnp.zeros(values.shape[:-1] + (side, side), jnp.bfloat16)
    for index in range(2 * band + 1):
        matrix = jnp.where(lag == index - band, values[..., index, None, None], matrix)
    return matrix


def gain_pieces(gain):
    high = lax.reduce_precision(gain, exponent_bits=8, mantissa_bits=7)
    rest = gain - high
    middle = lax.reduce_precision(rest, exponent_bits=8, mantissa_bits=7)
    low = lax.reduce_precision(rest - middle, exponent_bits=8, mantissa_bits=7)
    return jnp.stack([high, middle, low]).astype(jnp.bfloat16)


def filter_taps():
    values = [
        math.exp(-float(tap * tap) / (2.0 * det_sigma * det_sigma))
        for tap in range(-DET_R, DET_R + 1)
    ]
    whole = sum(values)
    return [value / whole for value in values]


def smooth_columns(padded, width):
    taps = filter_taps()
    total = jnp.zeros((padded.shape[0], width), jnp.float32)
    for index, tap in enumerate(range(-DET_R, DET_R + 1)):
        total = total + taps[index] * padded[:, DET_R + tap : DET_R + tap + width]
    return total


def smooth_rows_valid(framed, height):
    taps = filter_taps()
    total = jnp.zeros((height, framed.shape[1]), jnp.float32)
    for index, tap in enumerate(range(-DET_R, DET_R + 1)):
        total = total + taps[index] * framed[DET_R + tap : DET_R + tap + height, :]
    return total


def local(images, offsets, widths, weights, dest, cells, band_gain):
    side = images.shape[-1]
    count = images.shape[1]
    sect_count = lax.axis_size("sect")
    sub_count = lax.axis_size("sub")
    owners = sect_count * sub_count
    capacity = max(2, -(-2 * count // owners))
    slot_count = owners * capacity
    values = band_values(offsets[0], widths[0])
    row_kernel = toeplitz(values[:, 0], side)
    col_kernel = toeplitz(values[:, 1], side)
    section = jnp.einsum(
        "bij,bjk->bik", row_kernel, images[0], preferred_element_type=jnp.float32
    ).astype(jnp.bfloat16)
    warped = jnp.einsum(
        "bij,bkj->bik", section, col_kernel, preferred_element_type=jnp.float32
    ).astype(jnp.bfloat16)
    target = dest[0]
    same_owner = target[:, None] == target[None, :]
    block_order = jnp.arange(count, dtype=jnp.int32)
    earlier = block_order[None, :] < block_order[:, None]
    rank_within = jnp.sum(jnp.logical_and(same_owner, earlier), axis=1)
    slot_index = target * capacity + rank_within
    matching = jnp.arange(slot_count, dtype=jnp.int32)[:, None] == slot_index[None, :]
    source = jnp.sum(jnp.where(matching, block_order[None, :], 0), axis=1)
    placing = matching.astype(jnp.bfloat16)
    packed = jnp.take(warped, source, axis=0, mode="clip")
    cell_weight = jnp.where(
        cells[0][:, None] == jnp.arange(CELL_DEV, dtype=jnp.int32)[None, :],
        weights[0][:, None],
        jnp.zeros((), jnp.bfloat16),
    )
    packed_weight = jnp.dot(placing, cell_weight, preferred_element_type=jnp.float32).astype(
        jnp.bfloat16
    )
    received, received_weight = (
        lax.all_to_all(
            packed.reshape(owners, capacity * side, side),
            ("sect", "sub"),
            split_axis=0,
            concat_axis=0,
            tiled=True,
        ),
        lax.all_to_all(
            packed_weight.reshape(owners, capacity, CELL_DEV),
            ("sect", "sub"),
            split_axis=0,
            concat_axis=0,
            tiled=True,
        ),
    )
    received = received.reshape(slot_count, side, side)
    received_weight = received_weight.reshape(slot_count, CELL_DEV)
    numerator = jnp.einsum(
        "sc,sij->cij", received_weight, received, preferred_element_type=jnp.float32
    )
    denominator = jnp.sum(received_weight.astype(jnp.float32), axis=0)
    cell_mean = (numerator / jnp.maximum(denominator, 1.0)[:, None, None]).astype(jnp.bfloat16)
    coadd = (
        cell_mean.reshape(CELL_DEV, side, side).transpose(1, 0, 2).reshape(side, CELL_DEV * side)
    )
    padded = extended(coadd, ((("sect", "sub"), 1),), DET_R)
    band_count = lax.axis_size("band")
    height = side // band_count
    framed = jnp.pad(padded, ((DET_R, DET_R), (0, 0)))
    gain_row = jnp.zeros((1, padded.shape[1]), jnp.bfloat16).at[0, :3].set(gain_pieces(band_gain[0]))
    span = height + 2 * DET_R
    me = lax.axis_index("band")
    own = lax.dynamic_slice_in_dim(framed, me * height, span, axis=0)
    combined = band_gain[0] * own.astype(jnp.float32)
    for shift in range(1, band_count):
        outgoing = jnp.concatenate(
            [lax.dynamic_slice_in_dim(framed, ((me + shift) % band_count) * height, span, axis=0), gain_row]
        )
        incoming = lax.ppermute(
            outgoing, "band", [(i, (i + shift) % band_count) for i in range(band_count)]
        )
        gain = jnp.sum(incoming[span, :3].astype(jnp.float32))
        combined = combined + gain * incoming[:span].astype(jnp.float32)
    detection = smooth_rows_valid(smooth_columns(combined, CELL_DEV * side), height)
    return (coadd[None], detection)


def solution(mesh):
    return jax.shard_map(
        local,
        mesh=mesh,
        in_specs=(
            P("band", ("groups", "sect", "sub"), None, None),
            P("band", ("groups", "sect", "sub"), None),
            P("band", ("groups", "sect", "sub"), None),
            P("band", ("groups", "sect", "sub")),
            P("band", ("groups", "sect", "sub")),
            P("band", ("groups", "sect", "sub")),
            P("band"),
        ),
        out_specs=(
            P("band", None, ("groups", "sect", "sub")),
            P("band", ("groups", "sect", "sub")),
        ),
        check_vma=False,
    )
```

```python
import math

import jax
import jax.numpy as jnp
from jax import lax
from jax.sharding import PartitionSpec as P

CELL_DEV = 4
PSF_R = 8
DET_R = 4


det_sigma = 3.0


def extended(array, sides, width):
    for axis, dim in sides:
        size, length = (lax.axis_size(axis), array.shape[dim])
        up = [(i, (i + 1) % size) for i in range(size - 1)]
        down = [(j, i) for i, j in up]
        last = lax.slice_in_dim(array, length - width, length, axis=dim)
        initial = lax.slice_in_dim(array, 0, width, axis=dim)
        before = lax.ppermute(last, axis, up)
        after = lax.ppermute(initial, axis, down)
        array = jnp.concatenate([before, array, after], axis=dim)
    return array


def lanczos_tap(spacing):
    return jnp.where(jnp.abs(spacing) < 3.0, jnp.sinc(spacing) * jnp.sinc(spacing / 3.0), 0.0)


def band_values(shift, spread):
    band = PSF_R + 4
    spacing = jnp.arange(-band, band + 1, dtype=jnp.float32)
    tap = jnp.arange(-PSF_R, PSF_R + 1, dtype=jnp.float32)
    tap_weight = jnp.exp(-spread[..., None] * (tap * tap))
    taps = lanczos_tap(spacing + (shift[..., None, None] + tap[:, None]))
    taps = jnp.concatenate([taps, jnp.ones(taps.shape[:-1] + (1,), jnp.float32)], axis=-1)
    summed = jnp.sum(tap_weight[..., None] * taps, axis=-2)
    return (summed[..., :-1] / summed[..., -1:]).astype(jnp.bfloat16)


def toeplitz(values, side):
    band = PSF_R + 4
    position = jnp.arange(side, dtype=jnp.int32)
    lag = position[:, None] - position[None, :]
    matrix = jnp.zeros(values.shape[:-1] + (side, side), jnp.bfloat16)
    for index in range(2 * band + 1):
        matrix = jnp.where(lag == index - band, values[..., index, None, None], matrix)
    return matrix


def gain_pieces(gain):
    high = lax.reduce_precision(gain, exponent_bits=8, mantissa_bits=7)
    rest = gain - high
    middle = lax.reduce_precision(rest, exponent_bits=8, mantissa_bits=7)
    low = lax.reduce_precision(rest - middle, exponent_bits=8, mantissa_bits=7)
    return jnp.stack([high, middle, low]).astype(jnp.bfloat16)


def filter_taps():
    values = [
        math.exp(-float(tap * tap) / (2.0 * det_sigma * det_sigma))
        for tap in range(-DET_R, DET_R + 1)
    ]
    whole = sum(values)
    return [value / whole for value in values]


def smooth_columns(padded, width):
    taps = filter_taps()
    total = jnp.zeros((padded.shape[0], width), jnp.float32)
    for index, tap in enumerate(range(-DET_R, DET_R + 1)):
        total = total + taps[index] * padded[:, DET_R + tap : DET_R + tap + width]
    return total


def smooth_rows_valid(framed, height):
    taps = filter_taps()
    total = jnp.zeros((height, framed.shape[1]), jnp.float32)
    for index, tap in enumerate(range(-DET_R, DET_R + 1)):
        total = total + taps[index] * framed[DET_R + tap : DET_R + tap + height, :]
    return total


def local(images, offsets, widths, weights, dest, cells, band_gain):
    side = images.shape[-1]
    count = images.shape[1]
    sect_count = lax.axis_size("sect")
    sub_count = lax.axis_size("sub")
    owners = sect_count * sub_count
    capacity = max(2, -(-2 * count // owners))
    slot_count = owners * capacity
    values = band_values(offsets[0], widths[0])
    row_kernel = toeplitz(values[:, 0], side)
    col_kernel = toeplitz(values[:, 1], side)
    section = jnp.einsum(
        "bij,bjk->bik", row_kernel, images[0], preferred_element_type=jnp.float32
    ).astype(jnp.bfloat16)
    warped = jnp.einsum(
        "bij,bkj->bik", section, col_kernel, preferred_element_type=jnp.float32
    ).astype(jnp.bfloat16)
    target = dest[0]
    same_owner = target[:, None] == target[None, :]
    block_order = jnp.arange(count, dtype=jnp.int32)
    earlier = block_order[None, :] < block_order[:, None]
    rank_within = jnp.sum(jnp.logical_and(same_owner, earlier), axis=1)
    slot_index = target * capacity + rank_within
    matching = jnp.arange(slot_count, dtype=jnp.int32)[:, None] == slot_index[None, :]
    source = jnp.sum(jnp.where(matching, block_order[None, :], 0), axis=1)
    placing = matching.astype(jnp.bfloat16)
    packed = jnp.take(warped, source, axis=0, mode="clip")
    cell_weight = jnp.where(
        cells[0][:, None] == jnp.arange(CELL_DEV, dtype=jnp.int32)[None, :],
        weights[0][:, None],
        jnp.zeros((), jnp.bfloat16),
    )
    packed_weight = jnp.dot(placing, cell_weight, preferred_element_type=jnp.float32).astype(
        jnp.bfloat16
    )
    received, received_weight = (
        lax.all_to_all(
            packed.reshape(owners, capacity * side, side),
            ("sect", "sub"),
            split_axis=0,
            concat_axis=0,
            tiled=True,
        ),
        lax.all_to_all(
            packed_weight.reshape(owners, capacity, CELL_DEV),
            ("sect", "sub"),
            split_axis=0,
            concat_axis=0,
            tiled=True,
        ),
    )
    received = received.reshape(slot_count, side, side)
    received_weight = received_weight.reshape(slot_count, CELL_DEV)
    numerator = jnp.einsum(
        "sc,sij->icj", received_weight, received, preferred_element_type=jnp.float32
    )
    denominator = jnp.sum(received_weight.astype(jnp.float32), axis=0)
    cell_mean = (numerator / jnp.maximum(denominator, 1.0)[None, :, None]).astype(jnp.bfloat16)
    coadd = cell_mean.reshape(side, CELL_DEV * side)
    padded = extended(coadd, ((("sect", "sub"), 1),), DET_R)
    band_count = lax.axis_size("band")
    height = side // band_count
    framed = jnp.pad(padded, ((DET_R, DET_R), (0, 0)))
    gain_row = jnp.zeros((1, padded.shape[1]), jnp.bfloat16).at[0, :3].set(gain_pieces(band_gain[0]))
    span = height + 2 * DET_R
    me = lax.axis_index("band")
    own = lax.dynamic_slice_in_dim(framed, me * height, span, axis=0)
    combined = band_gain[0] * own.astype(jnp.float32)
    for shift in range(1, band_count):
        outgoing = jnp.concatenate(
            [lax.dynamic_slice_in_dim(framed, ((me + shift) % band_count) * height, span, axis=0), gain_row]
        )
        incoming = lax.ppermute(
            outgoing, "band", [(i, (i + shift) % band_count) for i in range(band_count)]
        )
        gain = jnp.sum(incoming[span, :3].astype(jnp.float32))
        combined = combined + gain * incoming[:span].astype(jnp.float32)
    detection = smooth_rows_valid(smooth_columns(combined, CELL_DEV * side), height)
    return (coadd[None], detection)


def solution(mesh):
    return jax.shard_map(
        local,
        mesh=mesh,
        in_specs=(
            P("band", ("groups", "sect", "sub"), None, None),
            P("band", ("groups", "sect", "sub"), None),
            P("band", ("groups", "sect", "sub"), None),
            P("band", ("groups", "sect", "sub")),
            P("band", ("groups", "sect", "sub")),
            P("band", ("groups", "sect", "sub")),
            P("band"),
        ),
        out_specs=(
            P("band", None, ("groups", "sect", "sub")),
            P("band", ("groups", "sect", "sub")),
        ),
        check_vma=False,
    )
```

```python
import math

import jax
import jax.numpy as jnp
from jax import lax
from jax.experimental import pallas as pl
from jax.experimental.pallas import tpu as pltpu
from jax.sharding import PartitionSpec as P

CELL_DEV = 4
PSF_R = 8
DET_R = 4


det_sigma = 3.0


def extended(array, sides, width):
    for axis, dim in sides:
        size, length = (lax.axis_size(axis), array.shape[dim])
        up = [(i, (i + 1) % size) for i in range(size - 1)]
        down = [(j, i) for i, j in up]
        last = lax.slice_in_dim(array, length - width, length, axis=dim)
        initial = lax.slice_in_dim(array, 0, width, axis=dim)
        before = lax.ppermute(last, axis, up)
        after = lax.ppermute(initial, axis, down)
        array = jnp.concatenate([before, array, after], axis=dim)
    return array


def lanczos_tap(spacing):
    return jnp.where(jnp.abs(spacing) < 3.0, jnp.sinc(spacing) * jnp.sinc(spacing / 3.0), 0.0)


def band_values(shift, spread):
    band = PSF_R + 4
    spacing = jnp.arange(-band, band + 1, dtype=jnp.float32)
    tap = jnp.arange(-PSF_R, PSF_R + 1, dtype=jnp.float32)
    tap_weight = jnp.exp(-spread[..., None] * (tap * tap))
    taps = lanczos_tap(spacing + (shift[..., None, None] + tap[:, None]))
    taps = jnp.concatenate([taps, jnp.ones(taps.shape[:-1] + (1,), jnp.float32)], axis=-1)
    summed = jnp.sum(tap_weight[..., None] * taps, axis=-2)
    return (summed[..., :-1] / summed[..., -1:]).astype(jnp.bfloat16)


def toeplitz(values, side):
    band = PSF_R + 4
    position = jnp.arange(side, dtype=jnp.int32)
    lag = position[:, None] - position[None, :]
    matrix = jnp.zeros(values.shape[:-1] + (side, side), jnp.bfloat16)
    for index in range(2 * band + 1):
        matrix = jnp.where(lag == index - band, values[..., index, None, None], matrix)
    return matrix


def base_rows(values, side):
    band = PSF_R + 4
    gap = jnp.zeros((values.shape[0], side - 2 * band - 1), jnp.float32)
    values = values.astype(jnp.float32)
    rows = jnp.concatenate([values[:, 0, band::-1], gap, values[:, 0, : band : -1]], axis=-1)
    cols = jnp.concatenate([values[:, 1, band:], gap, values[:, 1, :band]], axis=-1)
    return rows[:, None, :], cols[:, None, :]


def warp_kernel(source_ref, rows_ref, cols_ref, image_ref, out_ref):
    side = image_ref.shape[-1]
    row_base = jnp.broadcast_to(rows_ref[0], (side, side))
    col_base = jnp.broadcast_to(cols_ref[0], (side, side))
    lag = lax.broadcasted_iota(jnp.int32, (side, side), 0) - lax.broadcasted_iota(
        jnp.int32, (side, side), 1
    )
    inside = jnp.abs(lag) <= PSF_R + 4
    row_kernel = jnp.where(
        inside, pltpu.roll(row_base, 0, 1, stride=1, stride_axis=0), 0.0
    ).astype(jnp.bfloat16)
    col_kernel_t = jnp.where(
        inside, pltpu.roll(col_base, 0, 1, stride=1, stride_axis=0), 0.0
    ).astype(jnp.bfloat16)
    section = jnp.dot(row_kernel, image_ref[0], preferred_element_type=jnp.float32)
    out_ref[0] = jnp.dot(
        section.astype(jnp.bfloat16), col_kernel_t, preferred_element_type=jnp.float32
    ).astype(jnp.bfloat16)


def warp_slots(images, values, source, interpret=False):
    count, side = images.shape[0], images.shape[-1]
    slot_count = source.shape[0]
    rows, cols = base_rows(values, side)
    vector_spec = pl.BlockSpec((1, 1, side), lambda s, src: (src[s], 0, 0))
    return pl.pallas_call(
        warp_kernel,
        grid_spec=pltpu.PrefetchScalarGridSpec(
            num_scalar_prefetch=1,
            grid=(slot_count,),
            in_specs=[
                vector_spec,
                vector_spec,
                pl.BlockSpec((1, side, side), lambda s, src: (src[s], 0, 0)),
            ],
            out_specs=pl.BlockSpec((1, side, side), lambda s, src: (s, 0, 0)),
        ),
        out_shape=jax.ShapeDtypeStruct((slot_count, side, side), jnp.bfloat16),
        cost_estimate=pl.CostEstimate(
            flops=4 * slot_count * side**3,
            transcendentals=0,
            bytes_accessed=4 * slot_count * side * side,
        ),
        interpret=interpret,
    )(source, rows, cols, images)


def gain_pieces(gain):
    high = lax.reduce_precision(gain, exponent_bits=8, mantissa_bits=7)
    rest = gain - high
    middle = lax.reduce_precision(rest, exponent_bits=8, mantissa_bits=7)
    low = lax.reduce_precision(rest - middle, exponent_bits=8, mantissa_bits=7)
    return jnp.stack([high, middle, low]).astype(jnp.bfloat16)


def filter_taps():
    values = [
        math.exp(-float(tap * tap) / (2.0 * det_sigma * det_sigma))
        for tap in range(-DET_R, DET_R + 1)
    ]
    whole = sum(values)
    return [value / whole for value in values]


def smooth_columns(padded, width):
    taps = filter_taps()
    total = jnp.zeros((padded.shape[0], width), jnp.float32)
    for index, tap in enumerate(range(-DET_R, DET_R + 1)):
        total = total + taps[index] * padded[:, DET_R + tap : DET_R + tap + width]
    return total


def smooth_rows_valid(framed, height):
    taps = filter_taps()
    total = jnp.zeros((height, framed.shape[1]), jnp.float32)
    for index, tap in enumerate(range(-DET_R, DET_R + 1)):
        total = total + taps[index] * framed[DET_R + tap : DET_R + tap + height, :]
    return total


def local(images, offsets, widths, weights, dest, cells, band_gain):
    side = images.shape[-1]
    count = images.shape[1]
    sect_count = lax.axis_size("sect")
    sub_count = lax.axis_size("sub")
    owners = sect_count * sub_count
    capacity = max(2, -(-2 * count // owners))
    slot_count = owners * capacity
    values = band_values(offsets[0], widths[0])
    target = dest[0]
    same_owner = target[:, None] == target[None, :]
    block_order = jnp.arange(count, dtype=jnp.int32)
    earlier = block_order[None, :] < block_order[:, None]
    rank_within = jnp.sum(jnp.logical_and(same_owner, earlier), axis=1)
    slot_index = target * capacity + rank_within
    matching = jnp.arange(slot_count, dtype=jnp.int32)[:, None] == slot_index[None, :]
    source = jnp.sum(jnp.where(matching, block_order[None, :], 0), axis=1)
    placing = matching.astype(jnp.bfloat16)
    packed = warp_slots(images[0], values, source)
    cell_weight = jnp.where(
        cells[0][:, None] == jnp.arange(CELL_DEV, dtype=jnp.int32)[None, :],
        weights[0][:, None],
        jnp.zeros((), jnp.bfloat16),
    )
    packed_weight = jnp.dot(placing, cell_weight, preferred_element_type=jnp.float32).astype(
        jnp.bfloat16
    )
    received, received_weight = (
        lax.all_to_all(
            packed.reshape(owners, capacity * side, side),
            ("sect", "sub"),
            split_axis=0,
            concat_axis=0,
            tiled=True,
        ),
        lax.all_to_all(
            packed_weight.reshape(owners, capacity, CELL_DEV),
            ("sect", "sub"),
            split_axis=0,
            concat_axis=0,
            tiled=True,
        ),
    )
    received = received.reshape(slot_count, side, side)
    received_weight = received_weight.reshape(slot_count, CELL_DEV)
    numerator = jnp.einsum(
        "sc,sij->icj", received_weight, received, preferred_element_type=jnp.float32
    )
    denominator = jnp.sum(received_weight.astype(jnp.float32), axis=0)
    cell_mean = (numerator / jnp.maximum(denominator, 1.0)[None, :, None]).astype(jnp.bfloat16)
    coadd = cell_mean.reshape(side, CELL_DEV * side)
    padded = extended(coadd, ((("sect", "sub"), 1),), DET_R)
    band_count = lax.axis_size("band")
    height = side // band_count
    framed = jnp.pad(padded, ((DET_R, DET_R), (0, 0)))
    gain_row = jnp.zeros((1, padded.shape[1]), jnp.bfloat16).at[0, :3].set(gain_pieces(band_gain[0]))
    span = height + 2 * DET_R
    me = lax.axis_index("band")
    own = lax.dynamic_slice_in_dim(framed, me * height, span, axis=0)
    combined = band_gain[0] * own.astype(jnp.float32)
    for shift in range(1, band_count):
        outgoing = jnp.concatenate(
            [lax.dynamic_slice_in_dim(framed, ((me + shift) % band_count) * height, span, axis=0), gain_row]
        )
        incoming = lax.ppermute(
            outgoing, "band", [(i, (i + shift) % band_count) for i in range(band_count)]
        )
        gain = jnp.sum(incoming[span, :3].astype(jnp.float32))
        combined = combined + gain * incoming[:span].astype(jnp.float32)
    detection = smooth_rows_valid(smooth_columns(combined, CELL_DEV * side), height)
    return (coadd[None], detection)


def solution(mesh):
    return jax.shard_map(
        local,
        mesh=mesh,
        in_specs=(
            P("band", ("groups", "sect", "sub"), None, None),
            P("band", ("groups", "sect", "sub"), None),
            P("band", ("groups", "sect", "sub"), None),
            P("band", ("groups", "sect", "sub")),
            P("band", ("groups", "sect", "sub")),
            P("band", ("groups", "sect", "sub")),
            P("band"),
        ),
        out_specs=(
            P("band", None, ("groups", "sect", "sub")),
            P("band", ("groups", "sect", "sub")),
        ),
        check_vma=False,
    )
```

```python
import math

import jax
import jax.numpy as jnp
from jax import lax
from jax.experimental import pallas as pl
from jax.experimental.pallas import tpu as pltpu
from jax.sharding import PartitionSpec as P

CELL_DEV = 4
PSF_R = 8
DET_R = 4


det_sigma = 3.0


def extended(array, sides, width):
    for axis, dim in sides:
        size, length = (lax.axis_size(axis), array.shape[dim])
        up = [(i, (i + 1) % size) for i in range(size - 1)]
        down = [(j, i) for i, j in up]
        last = lax.slice_in_dim(array, length - width, length, axis=dim)
        initial = lax.slice_in_dim(array, 0, width, axis=dim)
        before = lax.ppermute(last, axis, up)
        after = lax.ppermute(initial, axis, down)
        array = jnp.concatenate([before, array, after], axis=dim)
    return array


def lanczos_tap(spacing):
    return jnp.where(jnp.abs(spacing) < 3.0, jnp.sinc(spacing) * jnp.sinc(spacing / 3.0), 0.0)


def band_values(shift, spread):
    band = PSF_R + 4
    spacing = jnp.arange(-band, band + 1, dtype=jnp.float32)
    tap = jnp.arange(-PSF_R, PSF_R + 1, dtype=jnp.float32)
    tap_weight = jnp.exp(-spread[..., None] * (tap * tap))
    taps = lanczos_tap(spacing + (shift[..., None, None] + tap[:, None]))
    taps = jnp.concatenate([taps, jnp.ones(taps.shape[:-1] + (1,), jnp.float32)], axis=-1)
    summed = jnp.sum(tap_weight[..., None] * taps, axis=-2)
    return (summed[..., :-1] / summed[..., -1:]).astype(jnp.bfloat16)


def toeplitz(values, side):
    band = PSF_R + 4
    position = jnp.arange(side, dtype=jnp.int32)
    lag = position[:, None] - position[None, :]
    matrix = jnp.zeros(values.shape[:-1] + (side, side), jnp.bfloat16)
    for index in range(2 * band + 1):
        matrix = jnp.where(lag == index - band, values[..., index, None, None], matrix)
    return matrix


def base_rows(values, side):
    band = PSF_R + 4
    gap = jnp.zeros((values.shape[0], side - 2 * band - 1), jnp.float32)
    values = values.astype(jnp.float32)
    rows = jnp.concatenate([values[:, 0, band::-1], gap, values[:, 0, : band : -1]], axis=-1)
    cols = jnp.concatenate([values[:, 1, band:], gap, values[:, 1, :band]], axis=-1)
    return rows[:, None, :], cols[:, None, :]


def warp_kernel(slot_ref, rows_ref, cols_ref, image_ref, blank_ref, out_ref):
    side = image_ref.shape[-1]
    row_base = jnp.broadcast_to(rows_ref[0], (side, side))
    col_base = jnp.broadcast_to(cols_ref[0], (side, side))
    lag = lax.broadcasted_iota(jnp.int32, (side, side), 0) - lax.broadcasted_iota(
        jnp.int32, (side, side), 1
    )
    inside = jnp.abs(lag) <= PSF_R + 4
    row_kernel = jnp.where(
        inside, pltpu.roll(row_base, 0, 1, stride=1, stride_axis=0), 0.0
    ).astype(jnp.bfloat16)
    col_kernel_t = jnp.where(
        inside, pltpu.roll(col_base, 0, 1, stride=1, stride_axis=0), 0.0
    ).astype(jnp.bfloat16)
    section = jnp.dot(row_kernel, image_ref[0], preferred_element_type=jnp.float32)
    out_ref[0] = jnp.dot(
        section.astype(jnp.bfloat16), col_kernel_t, preferred_element_type=jnp.float32
    ).astype(jnp.bfloat16)


def warp_slots(images, values, slot_index, slot_count, interpret=False):
    count, side = images.shape[0], images.shape[-1]
    rows, cols = base_rows(values, side)
    blank = jnp.zeros((slot_count, side, side), jnp.bfloat16)
    vector_spec = pl.BlockSpec((1, 1, side), lambda b, slots: (b, 0, 0))
    return pl.pallas_call(
        warp_kernel,
        grid_spec=pltpu.PrefetchScalarGridSpec(
            num_scalar_prefetch=1,
            grid=(count,),
            in_specs=[
                vector_spec,
                vector_spec,
                pl.BlockSpec((1, side, side), lambda b, slots: (b, 0, 0)),
                pl.BlockSpec(memory_space=pl.ANY),
            ],
            out_specs=pl.BlockSpec((1, side, side), lambda b, slots: (slots[b], 0, 0)),
        ),
        out_shape=jax.ShapeDtypeStruct((slot_count, side, side), jnp.bfloat16),
        input_output_aliases={4: 0},
        cost_estimate=pl.CostEstimate(
            flops=4 * count * side**3,
            transcendentals=0,
            bytes_accessed=2 * (2 * count + slot_count) * side * side,
        ),
        interpret=interpret,
    )(slot_index, rows, cols, images, blank)


def gain_pieces(gain):
    high = lax.reduce_precision(gain, exponent_bits=8, mantissa_bits=7)
    rest = gain - high
    middle = lax.reduce_precision(rest, exponent_bits=8, mantissa_bits=7)
    low = lax.reduce_precision(rest - middle, exponent_bits=8, mantissa_bits=7)
    return jnp.stack([high, middle, low]).astype(jnp.bfloat16)


def filter_taps():
    values = [
        math.exp(-float(tap * tap) / (2.0 * det_sigma * det_sigma))
        for tap in range(-DET_R, DET_R + 1)
    ]
    whole = sum(values)
    return [value / whole for value in values]


def smooth_columns(padded, width):
    taps = filter_taps()
    total = jnp.zeros((padded.shape[0], width), jnp.float32)
    for index, tap in enumerate(range(-DET_R, DET_R + 1)):
        total = total + taps[index] * padded[:, DET_R + tap : DET_R + tap + width]
    return total


def smooth_rows_valid(framed, height):
    taps = filter_taps()
    total = jnp.zeros((height, framed.shape[1]), jnp.float32)
    for index, tap in enumerate(range(-DET_R, DET_R + 1)):
        total = total + taps[index] * framed[DET_R + tap : DET_R + tap + height, :]
    return total


def local(images, offsets, widths, weights, dest, cells, band_gain):
    side = images.shape[-1]
    count = images.shape[1]
    sect_count = lax.axis_size("sect")
    sub_count = lax.axis_size("sub")
    owners = sect_count * sub_count
    capacity = max(2, -(-2 * count // owners))
    slot_count = owners * capacity
    values = band_values(offsets[0], widths[0])
    target = dest[0]
    same_owner = target[:, None] == target[None, :]
    block_order = jnp.arange(count, dtype=jnp.int32)
    earlier = block_order[None, :] < block_order[:, None]
    rank_within = jnp.sum(jnp.logical_and(same_owner, earlier), axis=1)
    slot_index = target * capacity + rank_within
    matching = jnp.arange(slot_count, dtype=jnp.int32)[:, None] == slot_index[None, :]
    source = jnp.sum(jnp.where(matching, block_order[None, :], 0), axis=1)
    placing = matching.astype(jnp.bfloat16)
    packed = warp_slots(
        images[0], values, jnp.minimum(slot_index, slot_count - 1).astype(jnp.int32), slot_count
    )
    cell_weight = jnp.where(
        cells[0][:, None] == jnp.arange(CELL_DEV, dtype=jnp.int32)[None, :],
        weights[0][:, None],
        jnp.zeros((), jnp.bfloat16),
    )
    packed_weight = jnp.dot(placing, cell_weight, preferred_element_type=jnp.float32).astype(
        jnp.bfloat16
    )
    received, received_weight = (
        lax.all_to_all(
            packed.reshape(owners, capacity * side, side),
            ("sect", "sub"),
            split_axis=0,
            concat_axis=0,
            tiled=True,
        ),
        lax.all_to_all(
            packed_weight.reshape(owners, capacity, CELL_DEV),
            ("sect", "sub"),
            split_axis=0,
            concat_axis=0,
            tiled=True,
        ),
    )
    received = received.reshape(slot_count, side, side)
    received_weight = received_weight.reshape(slot_count, CELL_DEV)
    numerator = jnp.einsum(
        "sc,sij->icj", received_weight, received, preferred_element_type=jnp.float32
    )
    denominator = jnp.sum(received_weight.astype(jnp.float32), axis=0)
    cell_mean = (numerator / jnp.maximum(denominator, 1.0)[None, :, None]).astype(jnp.bfloat16)
    coadd = cell_mean.reshape(side, CELL_DEV * side)
    padded = extended(coadd, ((("sect", "sub"), 1),), DET_R)
    band_count = lax.axis_size("band")
    height = side // band_count
    framed = jnp.pad(padded, ((DET_R, DET_R), (0, 0)))
    gain_row = jnp.zeros((1, padded.shape[1]), jnp.bfloat16).at[0, :3].set(gain_pieces(band_gain[0]))
    span = height + 2 * DET_R
    me = lax.axis_index("band")
    own = lax.dynamic_slice_in_dim(framed, me * height, span, axis=0)
    combined = band_gain[0] * own.astype(jnp.float32)
    for shift in range(1, band_count):
        outgoing = jnp.concatenate(
            [lax.dynamic_slice_in_dim(framed, ((me + shift) % band_count) * height, span, axis=0), gain_row]
        )
        incoming = lax.ppermute(
            outgoing, "band", [(i, (i + shift) % band_count) for i in range(band_count)]
        )
        gain = jnp.sum(incoming[span, :3].astype(jnp.float32))
        combined = combined + gain * incoming[:span].astype(jnp.float32)
    detection = smooth_rows_valid(smooth_columns(combined, CELL_DEV * side), height)
    return (coadd[None], detection)


def solution(mesh):
    return jax.shard_map(
        local,
        mesh=mesh,
        in_specs=(
            P("band", ("groups", "sect", "sub"), None, None),
            P("band", ("groups", "sect", "sub"), None),
            P("band", ("groups", "sect", "sub"), None),
            P("band", ("groups", "sect", "sub")),
            P("band", ("groups", "sect", "sub")),
            P("band", ("groups", "sect", "sub")),
            P("band"),
        ),
        out_specs=(
            P("band", None, ("groups", "sect", "sub")),
            P("band", ("groups", "sect", "sub")),
        ),
        check_vma=False,
    )
```

```python
import math

import jax
import jax.numpy as jnp
from jax import lax
from jax.experimental import pallas as pl
from jax.experimental.pallas import tpu as pltpu
from jax.sharding import PartitionSpec as P

CELL_DEV = 4
PSF_R = 8
DET_R = 4


det_sigma = 3.0


def extended(array, sides, width):
    for axis, dim in sides:
        size, length = (lax.axis_size(axis), array.shape[dim])
        up = [(i, (i + 1) % size) for i in range(size - 1)]
        down = [(j, i) for i, j in up]
        last = lax.slice_in_dim(array, length - width, length, axis=dim)
        initial = lax.slice_in_dim(array, 0, width, axis=dim)
        before = lax.ppermute(last, axis, up)
        after = lax.ppermute(initial, axis, down)
        array = jnp.concatenate([before, array, after], axis=dim)
    return array


def lanczos_tap(spacing):
    return jnp.where(jnp.abs(spacing) < 3.0, jnp.sinc(spacing) * jnp.sinc(spacing / 3.0), 0.0)


def band_values(shift, spread):
    band = PSF_R + 4
    spacing = jnp.arange(-band, band + 1, dtype=jnp.float32)
    tap = jnp.arange(-PSF_R, PSF_R + 1, dtype=jnp.float32)
    tap_weight = jnp.exp(-spread[..., None] * (tap * tap))
    taps = lanczos_tap(spacing + (shift[..., None, None] + tap[:, None]))
    taps = jnp.concatenate([taps, jnp.ones(taps.shape[:-1] + (1,), jnp.float32)], axis=-1)
    summed = jnp.sum(tap_weight[..., None] * taps, axis=-2)
    return (summed[..., :-1] / summed[..., -1:]).astype(jnp.bfloat16)


def toeplitz(values, side):
    band = PSF_R + 4
    position = jnp.arange(side, dtype=jnp.int32)
    lag = position[:, None] - position[None, :]
    matrix = jnp.zeros(values.shape[:-1] + (side, side), jnp.bfloat16)
    for index in range(2 * band + 1):
        matrix = jnp.where(lag == index - band, values[..., index, None, None], matrix)
    return matrix


def base_rows(values, side):
    band = PSF_R + 4
    gap = jnp.zeros((values.shape[0], side - 2 * band - 1), jnp.float32)
    values = values.astype(jnp.float32)
    rows = jnp.concatenate([values[:, 0, band::-1], gap, values[:, 0, : band : -1]], axis=-1)
    cols = jnp.concatenate([values[:, 1, band:], gap, values[:, 1, :band]], axis=-1)
    return rows[:, None, :], cols[:, None, :]


def warp_kernel(slot_ref, rows_ref, cols_ref, inside_ref, image_ref, blank_ref, out_ref):
    side = image_ref.shape[-1]
    row_base = jnp.broadcast_to(rows_ref[0], (side, side))
    col_base = jnp.broadcast_to(cols_ref[0], (side, side))
    inside = inside_ref[...]
    row_kernel = (pltpu.roll(row_base, 0, 1, stride=1, stride_axis=0) * inside).astype(
        jnp.bfloat16
    )
    col_kernel_t = (pltpu.roll(col_base, 0, 1, stride=1, stride_axis=0) * inside).astype(
        jnp.bfloat16
    )
    section = jnp.dot(row_kernel, image_ref[0], preferred_element_type=jnp.float32)
    out_ref[0] = jnp.dot(
        section.astype(jnp.bfloat16), col_kernel_t, preferred_element_type=jnp.float32
    ).astype(jnp.bfloat16)


def warp_slots(images, values, slot_index, slot_count, interpret=False):
    count, side = images.shape[0], images.shape[-1]
    rows, cols = base_rows(values, side)
    blank = jnp.zeros((slot_count, side, side), jnp.bfloat16)
    position = jnp.arange(side, dtype=jnp.int32)
    inside = (jnp.abs(position[:, None] - position[None, :]) <= PSF_R + 4).astype(jnp.float32)
    vector_spec = pl.BlockSpec((1, 1, side), lambda b, slots: (b, 0, 0))
    return pl.pallas_call(
        warp_kernel,
        grid_spec=pltpu.PrefetchScalarGridSpec(
            num_scalar_prefetch=1,
            grid=(count,),
            in_specs=[
                vector_spec,
                vector_spec,
                pl.BlockSpec((side, side), lambda b, slots: (0, 0)),
                pl.BlockSpec((1, side, side), lambda b, slots: (b, 0, 0)),
                pl.BlockSpec(memory_space=pl.ANY),
            ],
            out_specs=pl.BlockSpec((1, side, side), lambda b, slots: (slots[b], 0, 0)),
        ),
        out_shape=jax.ShapeDtypeStruct((slot_count, side, side), jnp.bfloat16),
        input_output_aliases={5: 0},
        cost_estimate=pl.CostEstimate(
            flops=4 * count * side**3,
            transcendentals=0,
            bytes_accessed=2 * (2 * count + slot_count) * side * side,
        ),
        interpret=interpret,
    )(slot_index, rows, cols, inside, images, blank)


def gain_pieces(gain):
    high = lax.reduce_precision(gain, exponent_bits=8, mantissa_bits=7)
    rest = gain - high
    middle = lax.reduce_precision(rest, exponent_bits=8, mantissa_bits=7)
    low = lax.reduce_precision(rest - middle, exponent_bits=8, mantissa_bits=7)
    return jnp.stack([high, middle, low]).astype(jnp.bfloat16)


def filter_taps():
    values = [
        math.exp(-float(tap * tap) / (2.0 * det_sigma * det_sigma))
        for tap in range(-DET_R, DET_R + 1)
    ]
    whole = sum(values)
    return [value / whole for value in values]


def smooth_columns(padded, width):
    taps = filter_taps()
    total = jnp.zeros((padded.shape[0], width), jnp.float32)
    for index, tap in enumerate(range(-DET_R, DET_R + 1)):
        total = total + taps[index] * padded[:, DET_R + tap : DET_R + tap + width]
    return total


def smooth_rows_valid(framed, height):
    taps = filter_taps()
    total = jnp.zeros((height, framed.shape[1]), jnp.float32)
    for index, tap in enumerate(range(-DET_R, DET_R + 1)):
        total = total + taps[index] * framed[DET_R + tap : DET_R + tap + height, :]
    return total


def local(images, offsets, widths, weights, dest, cells, band_gain):
    side = images.shape[-1]
    count = images.shape[1]
    sect_count = lax.axis_size("sect")
    sub_count = lax.axis_size("sub")
    owners = sect_count * sub_count
    capacity = max(2, -(-2 * count // owners))
    slot_count = owners * capacity
    values = band_values(offsets[0], widths[0])
    target = dest[0]
    same_owner = target[:, None] == target[None, :]
    block_order = jnp.arange(count, dtype=jnp.int32)
    earlier = block_order[None, :] < block_order[:, None]
    rank_within = jnp.sum(jnp.logical_and(same_owner, earlier), axis=1)
    slot_index = target * capacity + rank_within
    matching = jnp.arange(slot_count, dtype=jnp.int32)[:, None] == slot_index[None, :]
    source = jnp.sum(jnp.where(matching, block_order[None, :], 0), axis=1)
    placing = matching.astype(jnp.bfloat16)
    packed = warp_slots(
        images[0], values, jnp.minimum(slot_index, slot_count - 1).astype(jnp.int32), slot_count
    )
    cell_weight = jnp.where(
        cells[0][:, None] == jnp.arange(CELL_DEV, dtype=jnp.int32)[None, :],
        weights[0][:, None],
        jnp.zeros((), jnp.bfloat16),
    )
    packed_weight = jnp.dot(placing, cell_weight, preferred_element_type=jnp.float32).astype(
        jnp.bfloat16
    )
    received, received_weight = (
        lax.all_to_all(
            packed.reshape(owners, capacity * side, side),
            ("sect", "sub"),
            split_axis=0,
            concat_axis=0,
            tiled=True,
        ),
        lax.all_to_all(
            packed_weight.reshape(owners, capacity, CELL_DEV),
            ("sect", "sub"),
            split_axis=0,
            concat_axis=0,
            tiled=True,
        ),
    )
    received = received.reshape(slot_count, side, side)
    received_weight = received_weight.reshape(slot_count, CELL_DEV)
    numerator = jnp.einsum(
        "sc,sij->icj", received_weight, received, preferred_element_type=jnp.float32
    )
    denominator = jnp.sum(received_weight.astype(jnp.float32), axis=0)
    cell_mean = (numerator / jnp.maximum(denominator, 1.0)[None, :, None]).astype(jnp.bfloat16)
    coadd = cell_mean.reshape(side, CELL_DEV * side)
    padded = extended(coadd, ((("sect", "sub"), 1),), DET_R)
    band_count = lax.axis_size("band")
    height = side // band_count
    framed = jnp.pad(padded, ((DET_R, DET_R), (0, 0)))
    gain_row = jnp.zeros((1, padded.shape[1]), jnp.bfloat16).at[0, :3].set(gain_pieces(band_gain[0]))
    span = height + 2 * DET_R
    me = lax.axis_index("band")
    own = lax.dynamic_slice_in_dim(framed, me * height, span, axis=0)
    combined = band_gain[0] * own.astype(jnp.float32)
    for shift in range(1, band_count):
        outgoing = jnp.concatenate(
            [lax.dynamic_slice_in_dim(framed, ((me + shift) % band_count) * height, span, axis=0), gain_row]
        )
        incoming = lax.ppermute(
            outgoing, "band", [(i, (i + shift) % band_count) for i in range(band_count)]
        )
        gain = jnp.sum(incoming[span, :3].astype(jnp.float32))
        combined = combined + gain * incoming[:span].astype(jnp.float32)
    detection = smooth_rows_valid(smooth_columns(combined, CELL_DEV * side), height)
    return (coadd[None], detection)


def solution(mesh):
    return jax.shard_map(
        local,
        mesh=mesh,
        in_specs=(
            P("band", ("groups", "sect", "sub"), None, None),
            P("band", ("groups", "sect", "sub"), None),
            P("band", ("groups", "sect", "sub"), None),
            P("band", ("groups", "sect", "sub")),
            P("band", ("groups", "sect", "sub")),
            P("band", ("groups", "sect", "sub")),
            P("band"),
        ),
        out_specs=(
            P("band", None, ("groups", "sect", "sub")),
            P("band", ("groups", "sect", "sub")),
        ),
        check_vma=False,
    )
```

```python
import math

import jax
import jax.numpy as jnp
from jax import lax
from jax.experimental import pallas as pl
from jax.experimental.pallas import tpu as pltpu
from jax.sharding import PartitionSpec as P

CELL_DEV = 4
PSF_R = 8
DET_R = 4


det_sigma = 3.0


def extended(array, sides, width):
    for axis, dim in sides:
        size, length = (lax.axis_size(axis), array.shape[dim])
        up = [(i, (i + 1) % size) for i in range(size - 1)]
        down = [(j, i) for i, j in up]
        last = lax.slice_in_dim(array, length - width, length, axis=dim)
        initial = lax.slice_in_dim(array, 0, width, axis=dim)
        before = lax.ppermute(last, axis, up)
        after = lax.ppermute(initial, axis, down)
        array = jnp.concatenate([before, array, after], axis=dim)
    return array


def lanczos_tap(spacing):
    return jnp.where(jnp.abs(spacing) < 3.0, jnp.sinc(spacing) * jnp.sinc(spacing / 3.0), 0.0)


def band_values(shift, spread):
    band = PSF_R + 4
    spacing = jnp.arange(-band, band + 1, dtype=jnp.float32)
    tap = jnp.arange(-PSF_R, PSF_R + 1, dtype=jnp.float32)
    tap_weight = jnp.exp(-spread[..., None] * (tap * tap))
    taps = lanczos_tap(spacing + (shift[..., None, None] + tap[:, None]))
    taps = jnp.concatenate([taps, jnp.ones(taps.shape[:-1] + (1,), jnp.float32)], axis=-1)
    summed = jnp.sum(tap_weight[..., None] * taps, axis=-2)
    return (summed[..., :-1] / summed[..., -1:]).astype(jnp.bfloat16)


def toeplitz(values, side):
    band = PSF_R + 4
    position = jnp.arange(side, dtype=jnp.int32)
    lag = position[:, None] - position[None, :]
    matrix = jnp.zeros(values.shape[:-1] + (side, side), jnp.bfloat16)
    for index in range(2 * band + 1):
        matrix = jnp.where(lag == index - band, values[..., index, None, None], matrix)
    return matrix


def base_rows(values, side):
    band = PSF_R + 4
    gap = jnp.zeros((values.shape[0], side - 2 * band - 1), jnp.float32)
    values = values.astype(jnp.float32)
    rows = jnp.concatenate([values[:, 0, band::-1], gap, values[:, 0, : band : -1]], axis=-1)
    cols = jnp.concatenate([values[:, 1, band:], gap, values[:, 1, :band]], axis=-1)
    return rows[:, None, :], cols[:, None, :]


def warp_kernel(slot_ref, rows_ref, cols_ref, inside_ref, image_ref, blank_ref, out_ref, done_ref, sems):
    side = image_ref.shape[-1]
    group = image_ref.shape[0]
    step = pl.program_id(0)
    inside = inside_ref[...]
    copies = []
    for member in range(group):
        row_base = jnp.broadcast_to(rows_ref[member], (side, side))
        col_base = jnp.broadcast_to(cols_ref[member], (side, side))
        row_kernel = (pltpu.roll(row_base, 0, 1, stride=1, stride_axis=0) * inside).astype(
            jnp.bfloat16
        )
        col_kernel_t = (pltpu.roll(col_base, 0, 1, stride=1, stride_axis=0) * inside).astype(
            jnp.bfloat16
        )
        section = jnp.dot(row_kernel, image_ref[member], preferred_element_type=jnp.float32)
        done_ref[member] = jnp.dot(
            section.astype(jnp.bfloat16), col_kernel_t, preferred_element_type=jnp.float32
        ).astype(jnp.bfloat16)
        copy = pltpu.make_async_copy(
            done_ref.at[member], out_ref.at[slot_ref[step * group + member]], sems.at[member]
        )
        copy.start()
        copies.append(copy)
    for copy in copies:
        copy.wait()


def warp_slots(images, values, slot_index, slot_count, interpret=False):
    count, side = images.shape[0], images.shape[-1]
    group = 2 if count % 2 == 0 else 1
    rows, cols = base_rows(values, side)
    blank = jnp.zeros((slot_count, side, side), jnp.bfloat16)
    position = jnp.arange(side, dtype=jnp.int32)
    inside = (jnp.abs(position[:, None] - position[None, :]) <= PSF_R + 4).astype(jnp.float32)
    vector_spec = pl.BlockSpec((group, 1, side), lambda b, slots: (b, 0, 0))
    return pl.pallas_call(
        warp_kernel,
        grid_spec=pltpu.PrefetchScalarGridSpec(
            num_scalar_prefetch=1,
            grid=(count // group,),
            in_specs=[
                vector_spec,
                vector_spec,
                pl.BlockSpec((side, side), lambda b, slots: (0, 0)),
                pl.BlockSpec((group, side, side), lambda b, slots: (b, 0, 0)),
                pl.BlockSpec(memory_space=pl.ANY),
            ],
            out_specs=pl.BlockSpec(memory_space=pl.ANY),
            scratch_shapes=[
                pltpu.VMEM((group, side, side), jnp.bfloat16),
                pltpu.SemaphoreType.DMA((group,)),
            ],
        ),
        out_shape=jax.ShapeDtypeStruct((slot_count, side, side), jnp.bfloat16),
        input_output_aliases={5: 0},
        cost_estimate=pl.CostEstimate(
            flops=4 * count * side**3,
            transcendentals=0,
            bytes_accessed=2 * (2 * count + slot_count) * side * side,
        ),
        interpret=interpret,
    )(slot_index, rows, cols, inside, images, blank)


def gain_pieces(gain):
    high = lax.reduce_precision(gain, exponent_bits=8, mantissa_bits=7)
    rest = gain - high
    middle = lax.reduce_precision(rest, exponent_bits=8, mantissa_bits=7)
    low = lax.reduce_precision(rest - middle, exponent_bits=8, mantissa_bits=7)
    return jnp.stack([high, middle, low]).astype(jnp.bfloat16)


def filter_taps():
    values = [
        math.exp(-float(tap * tap) / (2.0 * det_sigma * det_sigma))
        for tap in range(-DET_R, DET_R + 1)
    ]
    whole = sum(values)
    return [value / whole for value in values]


def smooth_columns(padded, width):
    taps = filter_taps()
    total = jnp.zeros((padded.shape[0], width), jnp.float32)
    for index, tap in enumerate(range(-DET_R, DET_R + 1)):
        total = total + taps[index] * padded[:, DET_R + tap : DET_R + tap + width]
    return total


def smooth_rows_valid(framed, height):
    taps = filter_taps()
    total = jnp.zeros((height, framed.shape[1]), jnp.float32)
    for index, tap in enumerate(range(-DET_R, DET_R + 1)):
        total = total + taps[index] * framed[DET_R + tap : DET_R + tap + height, :]
    return total


def local(images, offsets, widths, weights, dest, cells, band_gain):
    side = images.shape[-1]
    count = images.shape[1]
    sect_count = lax.axis_size("sect")
    sub_count = lax.axis_size("sub")
    owners = sect_count * sub_count
    capacity = max(2, -(-2 * count // owners))
    slot_count = owners * capacity
    values = band_values(offsets[0], widths[0])
    target = dest[0]
    same_owner = target[:, None] == target[None, :]
    block_order = jnp.arange(count, dtype=jnp.int32)
    earlier = block_order[None, :] < block_order[:, None]
    rank_within = jnp.sum(jnp.logical_and(same_owner, earlier), axis=1)
    slot_index = target * capacity + rank_within
    matching = jnp.arange(slot_count, dtype=jnp.int32)[:, None] == slot_index[None, :]
    source = jnp.sum(jnp.where(matching, block_order[None, :], 0), axis=1)
    placing = matching.astype(jnp.bfloat16)
    packed = warp_slots(
        images[0], values, jnp.minimum(slot_index, slot_count - 1).astype(jnp.int32), slot_count
    )
    cell_weight = jnp.where(
        cells[0][:, None] == jnp.arange(CELL_DEV, dtype=jnp.int32)[None, :],
        weights[0][:, None],
        jnp.zeros((), jnp.bfloat16),
    )
    packed_weight = jnp.dot(placing, cell_weight, preferred_element_type=jnp.float32).astype(
        jnp.bfloat16
    )
    received, received_weight = (
        lax.all_to_all(
            packed.reshape(owners, capacity * side, side),
            ("sect", "sub"),
            split_axis=0,
            concat_axis=0,
            tiled=True,
        ),
        lax.all_to_all(
            packed_weight.reshape(owners, capacity, CELL_DEV),
            ("sect", "sub"),
            split_axis=0,
            concat_axis=0,
            tiled=True,
        ),
    )
    received = received.reshape(slot_count, side, side)
    received_weight = received_weight.reshape(slot_count, CELL_DEV)
    numerator = jnp.einsum(
        "sc,sij->icj", received_weight, received, preferred_element_type=jnp.float32
    )
    denominator = jnp.sum(received_weight.astype(jnp.float32), axis=0)
    cell_mean = (numerator / jnp.maximum(denominator, 1.0)[None, :, None]).astype(jnp.bfloat16)
    coadd = cell_mean.reshape(side, CELL_DEV * side)
    padded = extended(coadd, ((("sect", "sub"), 1),), DET_R)
    band_count = lax.axis_size("band")
    height = side // band_count
    framed = jnp.pad(padded, ((DET_R, DET_R), (0, 0)))
    gain_row = jnp.zeros((1, padded.shape[1]), jnp.bfloat16).at[0, :3].set(gain_pieces(band_gain[0]))
    span = height + 2 * DET_R
    me = lax.axis_index("band")
    own = lax.dynamic_slice_in_dim(framed, me * height, span, axis=0)
    combined = band_gain[0] * own.astype(jnp.float32)
    for shift in range(1, band_count):
        outgoing = jnp.concatenate(
            [lax.dynamic_slice_in_dim(framed, ((me + shift) % band_count) * height, span, axis=0), gain_row]
        )
        incoming = lax.ppermute(
            outgoing, "band", [(i, (i + shift) % band_count) for i in range(band_count)]
        )
        gain = jnp.sum(incoming[span, :3].astype(jnp.float32))
        combined = combined + gain * incoming[:span].astype(jnp.float32)
    detection = smooth_rows_valid(smooth_columns(combined, CELL_DEV * side), height)
    return (coadd[None], detection)


def solution(mesh):
    return jax.shard_map(
        local,
        mesh=mesh,
        in_specs=(
            P("band", ("groups", "sect", "sub"), None, None),
            P("band", ("groups", "sect", "sub"), None),
            P("band", ("groups", "sect", "sub"), None),
            P("band", ("groups", "sect", "sub")),
            P("band", ("groups", "sect", "sub")),
            P("band", ("groups", "sect", "sub")),
            P("band"),
        ),
        out_specs=(
            P("band", None, ("groups", "sect", "sub")),
            P("band", ("groups", "sect", "sub")),
        ),
        check_vma=False,
    )
```

```python
import math

import jax
import jax.numpy as jnp
from jax import lax
from jax.experimental import pallas as pl
from jax.experimental.pallas import tpu as pltpu
from jax.sharding import PartitionSpec as P

CELL_DEV = 4
PSF_R = 8
DET_R = 4


det_sigma = 3.0


def extended(array, sides, width):
    for axis, dim in sides:
        size, length = (lax.axis_size(axis), array.shape[dim])
        up = [(i, (i + 1) % size) for i in range(size - 1)]
        down = [(j, i) for i, j in up]
        last = lax.slice_in_dim(array, length - width, length, axis=dim)
        initial = lax.slice_in_dim(array, 0, width, axis=dim)
        before = lax.ppermute(last, axis, up)
        after = lax.ppermute(initial, axis, down)
        array = jnp.concatenate([before, array, after], axis=dim)
    return array


def lanczos_tap(spacing):
    return jnp.where(jnp.abs(spacing) < 3.0, jnp.sinc(spacing) * jnp.sinc(spacing / 3.0), 0.0)


def band_values(shift, spread):
    band = PSF_R + 4
    spacing = jnp.arange(-band, band + 1, dtype=jnp.float32)
    tap = jnp.arange(-PSF_R, PSF_R + 1, dtype=jnp.float32)
    tap_weight = jnp.exp(-spread[..., None] * (tap * tap))
    taps = lanczos_tap(spacing + (shift[..., None, None] + tap[:, None]))
    taps = jnp.concatenate([taps, jnp.ones(taps.shape[:-1] + (1,), jnp.float32)], axis=-1)
    summed = jnp.sum(tap_weight[..., None] * taps, axis=-2)
    return (summed[..., :-1] / summed[..., -1:]).astype(jnp.bfloat16)


def toeplitz(values, side):
    band = PSF_R + 4
    position = jnp.arange(side, dtype=jnp.int32)
    lag = position[:, None] - position[None, :]
    matrix = jnp.zeros(values.shape[:-1] + (side, side), jnp.bfloat16)
    for index in range(2 * band + 1):
        matrix = jnp.where(lag == index - band, values[..., index, None, None], matrix)
    return matrix


def base_rows(values, side):
    band = PSF_R + 4
    gap = jnp.zeros((values.shape[0], side - 2 * band - 1), jnp.float32)
    values = values.astype(jnp.float32)
    rows = jnp.concatenate([values[:, 0, band::-1], gap, values[:, 0, : band : -1]], axis=-1)
    cols = jnp.concatenate([values[:, 1, band:], gap, values[:, 1, :band]], axis=-1)
    return rows[:, None, :], cols[:, None, :]


def warp_kernel(slot_ref, rows_ref, cols_ref, inside_ref, image_ref, blank_ref, out_ref, done_ref, sems):
    side = image_ref.shape[-1]
    group = image_ref.shape[0]
    step = pl.program_id(0)
    inside = inside_ref[...]
    copies = []
    for member in range(group):
        row_base = jnp.broadcast_to(rows_ref[member], (side, side))
        col_base = jnp.broadcast_to(cols_ref[member], (side, side))
        row_kernel = (pltpu.roll(row_base, 0, 1, stride=1, stride_axis=0) * inside).astype(
            jnp.bfloat16
        )
        col_kernel_t = (pltpu.roll(col_base, 0, 1, stride=1, stride_axis=0) * inside).astype(
            jnp.bfloat16
        )
        section = jnp.dot(row_kernel, image_ref[member], preferred_element_type=jnp.float32)
        done_ref[member] = jnp.dot(
            section.astype(jnp.bfloat16), col_kernel_t, preferred_element_type=jnp.float32
        ).astype(jnp.bfloat16)
        slot = slot_ref[step * group + member]
        capacity = (out_ref.shape[1] - 16) // side
        target = out_ref.at[slot // capacity, pl.ds((slot % capacity) * side, side), :]
        copy = pltpu.make_async_copy(done_ref.at[member], target, sems.at[member])
        copy.start()
        copies.append(copy)
    for copy in copies:
        copy.wait()


def warp_slots(images, values, slot_index, slot_weight, interpret=False):
    count, side = images.shape[0], images.shape[-1]
    owners, capacity, cell_count = slot_weight.shape
    group = 2 if count % 2 == 0 else 1
    rows, cols = base_rows(values, side)
    blank = (
        jnp.zeros((owners, capacity * side + 16, side), jnp.bfloat16)
        .at[:, capacity * side, : capacity * cell_count]
        .set(slot_weight.reshape(owners, capacity * cell_count))
    )
    position = jnp.arange(side, dtype=jnp.int32)
    inside = (jnp.abs(position[:, None] - position[None, :]) <= PSF_R + 4).astype(jnp.float32)
    vector_spec = pl.BlockSpec((group, 1, side), lambda b, slots: (b, 0, 0))
    return pl.pallas_call(
        warp_kernel,
        grid_spec=pltpu.PrefetchScalarGridSpec(
            num_scalar_prefetch=1,
            grid=(count // group,),
            in_specs=[
                vector_spec,
                vector_spec,
                pl.BlockSpec((side, side), lambda b, slots: (0, 0)),
                pl.BlockSpec((group, side, side), lambda b, slots: (b, 0, 0)),
                pl.BlockSpec(memory_space=pl.ANY),
            ],
            out_specs=pl.BlockSpec(memory_space=pl.ANY),
            scratch_shapes=[
                pltpu.VMEM((group, side, side), jnp.bfloat16),
                pltpu.SemaphoreType.DMA((group,)),
            ],
        ),
        out_shape=jax.ShapeDtypeStruct(blank.shape, jnp.bfloat16),
        input_output_aliases={5: 0},
        cost_estimate=pl.CostEstimate(
            flops=4 * count * side**3,
            transcendentals=0,
            bytes_accessed=2 * (2 * count * side * side + blank.size),
        ),
        interpret=interpret,
    )(slot_index, rows, cols, inside, images, blank)


def gain_pieces(gain):
    high = lax.reduce_precision(gain, exponent_bits=8, mantissa_bits=7)
    rest = gain - high
    middle = lax.reduce_precision(rest, exponent_bits=8, mantissa_bits=7)
    low = lax.reduce_precision(rest - middle, exponent_bits=8, mantissa_bits=7)
    return jnp.stack([high, middle, low]).astype(jnp.bfloat16)


def filter_taps():
    values = [
        math.exp(-float(tap * tap) / (2.0 * det_sigma * det_sigma))
        for tap in range(-DET_R, DET_R + 1)
    ]
    whole = sum(values)
    return [value / whole for value in values]


def smooth_columns(padded, width):
    taps = filter_taps()
    total = jnp.zeros((padded.shape[0], width), jnp.float32)
    for index, tap in enumerate(range(-DET_R, DET_R + 1)):
        total = total + taps[index] * padded[:, DET_R + tap : DET_R + tap + width]
    return total


def smooth_rows_valid(framed, height):
    taps = filter_taps()
    total = jnp.zeros((height, framed.shape[1]), jnp.float32)
    for index, tap in enumerate(range(-DET_R, DET_R + 1)):
        total = total + taps[index] * framed[DET_R + tap : DET_R + tap + height, :]
    return total


def local(images, offsets, widths, weights, dest, cells, band_gain):
    side = images.shape[-1]
    count = images.shape[1]
    sect_count = lax.axis_size("sect")
    sub_count = lax.axis_size("sub")
    owners = sect_count * sub_count
    capacity = max(2, -(-2 * count // owners))
    slot_count = owners * capacity
    values = band_values(offsets[0], widths[0])
    target = dest[0]
    same_owner = target[:, None] == target[None, :]
    block_order = jnp.arange(count, dtype=jnp.int32)
    earlier = block_order[None, :] < block_order[:, None]
    rank_within = jnp.sum(jnp.logical_and(same_owner, earlier), axis=1)
    slot_index = target * capacity + rank_within
    matching = jnp.arange(slot_count, dtype=jnp.int32)[:, None] == slot_index[None, :]
    source = jnp.sum(jnp.where(matching, block_order[None, :], 0), axis=1)
    placing = matching.astype(jnp.bfloat16)
    cell_weight = jnp.where(
        cells[0][:, None] == jnp.arange(CELL_DEV, dtype=jnp.int32)[None, :],
        weights[0][:, None],
        jnp.zeros((), jnp.bfloat16),
    )
    packed_weight = jnp.dot(placing, cell_weight, preferred_element_type=jnp.float32).astype(
        jnp.bfloat16
    )
    packed = warp_slots(
        images[0],
        values,
        jnp.minimum(slot_index, slot_count - 1).astype(jnp.int32),
        packed_weight.reshape(owners, capacity, CELL_DEV),
    )
    received = lax.all_to_all(packed, ("sect", "sub"), split_axis=0, concat_axis=0, tiled=True)
    received_weight = received[:, capacity * side, : capacity * CELL_DEV].reshape(
        slot_count, CELL_DEV
    )
    received = received[:, : capacity * side].reshape(slot_count, side, side)
    numerator = jnp.einsum(
        "sc,sij->icj", received_weight, received, preferred_element_type=jnp.float32
    )
    denominator = jnp.sum(received_weight.astype(jnp.float32), axis=0)
    cell_mean = (numerator / jnp.maximum(denominator, 1.0)[None, :, None]).astype(jnp.bfloat16)
    coadd = cell_mean.reshape(side, CELL_DEV * side)
    padded = extended(coadd, ((("sect", "sub"), 1),), DET_R)
    band_count = lax.axis_size("band")
    height = side // band_count
    framed = jnp.pad(padded, ((DET_R, DET_R), (0, 0)))
    gain_row = jnp.zeros((1, padded.shape[1]), jnp.bfloat16).at[0, :3].set(gain_pieces(band_gain[0]))
    span = height + 2 * DET_R
    me = lax.axis_index("band")
    own = lax.dynamic_slice_in_dim(framed, me * height, span, axis=0)
    combined = band_gain[0] * own.astype(jnp.float32)
    for shift in range(1, band_count):
        outgoing = jnp.concatenate(
            [lax.dynamic_slice_in_dim(framed, ((me + shift) % band_count) * height, span, axis=0), gain_row]
        )
        incoming = lax.ppermute(
            outgoing, "band", [(i, (i + shift) % band_count) for i in range(band_count)]
        )
        gain = jnp.sum(incoming[span, :3].astype(jnp.float32))
        combined = combined + gain * incoming[:span].astype(jnp.float32)
    detection = smooth_rows_valid(smooth_columns(combined, CELL_DEV * side), height)
    return (coadd[None], detection)


def solution(mesh):
    return jax.shard_map(
        local,
        mesh=mesh,
        in_specs=(
            P("band", ("groups", "sect", "sub"), None, None),
            P("band", ("groups", "sect", "sub"), None),
            P("band", ("groups", "sect", "sub"), None),
            P("band", ("groups", "sect", "sub")),
            P("band", ("groups", "sect", "sub")),
            P("band", ("groups", "sect", "sub")),
            P("band"),
        ),
        out_specs=(
            P("band", None, ("groups", "sect", "sub")),
            P("band", ("groups", "sect", "sub")),
        ),
        check_vma=False,
    )
```

```python
import math

import jax
import jax.numpy as jnp
from jax import lax
from jax.experimental import pallas as pl
from jax.experimental.pallas import tpu as pltpu
from jax.sharding import PartitionSpec as P

CELL_DEV = 4
PSF_R = 8
DET_R = 4


det_sigma = 3.0


def extended(array, sides, width):
    for axis, dim in sides:
        size, length = (lax.axis_size(axis), array.shape[dim])
        up = [(i, (i + 1) % size) for i in range(size - 1)]
        down = [(j, i) for i, j in up]
        last = lax.slice_in_dim(array, length - width, length, axis=dim)
        initial = lax.slice_in_dim(array, 0, width, axis=dim)
        before = lax.ppermute(last, axis, up)
        after = lax.ppermute(initial, axis, down)
        array = jnp.concatenate([before, array, after], axis=dim)
    return array


def lanczos_tap(spacing):
    return jnp.where(jnp.abs(spacing) < 3.0, jnp.sinc(spacing) * jnp.sinc(spacing / 3.0), 0.0)


def band_values(shift, spread):
    band = PSF_R + 4
    spacing = jnp.arange(-band, band + 1, dtype=jnp.float32)
    tap = jnp.arange(-PSF_R, PSF_R + 1, dtype=jnp.float32)
    tap_weight = jnp.exp(-spread[..., None] * (tap * tap))
    taps = lanczos_tap(spacing + (shift[..., None, None] + tap[:, None]))
    taps = jnp.concatenate([taps, jnp.ones(taps.shape[:-1] + (1,), jnp.float32)], axis=-1)
    summed = jnp.sum(tap_weight[..., None] * taps, axis=-2)
    return (summed[..., :-1] / summed[..., -1:]).astype(jnp.bfloat16)


def toeplitz(values, side):
    band = PSF_R + 4
    position = jnp.arange(side, dtype=jnp.int32)
    lag = position[:, None] - position[None, :]
    matrix = jnp.zeros(values.shape[:-1] + (side, side), jnp.bfloat16)
    for index in range(2 * band + 1):
        matrix = jnp.where(lag == index - band, values[..., index, None, None], matrix)
    return matrix


def base_rows(values, side):
    band = PSF_R + 4
    gap = jnp.zeros((values.shape[0], side - 2 * band - 1), jnp.float32)
    values = values.astype(jnp.float32)
    rows = jnp.concatenate([values[:, 0, band::-1], gap, values[:, 0, : band : -1]], axis=-1)
    cols = jnp.concatenate([values[:, 1, band:], gap, values[:, 1, :band]], axis=-1)
    return rows[:, None, :], cols[:, None, :]


def warp_kernel(slot_ref, rows_ref, cols_ref, inside_ref, image_ref, blank_ref, out_ref, done_ref, sems):
    side = image_ref.shape[-1]
    group = image_ref.shape[0]
    step = pl.program_id(0)
    inside = inside_ref[...]
    copies = []
    for member in range(group):
        row_base = jnp.broadcast_to(rows_ref[member], (side, side))
        col_base = jnp.broadcast_to(cols_ref[member], (side, side))
        row_kernel = (pltpu.roll(row_base, 0, 1, stride=1, stride_axis=0) * inside).astype(
            jnp.bfloat16
        )
        col_kernel_t = (pltpu.roll(col_base, 0, 1, stride=1, stride_axis=0) * inside).astype(
            jnp.bfloat16
        )
        section = jnp.dot(row_kernel, image_ref[member], preferred_element_type=jnp.float32)
        done_ref[member] = jnp.dot(
            section.astype(jnp.bfloat16), col_kernel_t, preferred_element_type=jnp.float32
        ).astype(jnp.bfloat16)
        slot = slot_ref[step * group + member]
        capacity = (out_ref.shape[1] - 16) // side
        target = out_ref.at[slot // capacity, pl.ds((slot % capacity) * side, side), :]
        copy = pltpu.make_async_copy(done_ref.at[member], target, sems.at[member])
        copy.start()
        copies.append(copy)
    for copy in copies:
        copy.wait()


def warp_slots(images, values, slot_index, slot_weight, interpret=False):
    count, side = images.shape[0], images.shape[-1]
    owners, capacity, cell_count = slot_weight.shape
    group = 4 if count % 4 == 0 else 1
    rows, cols = base_rows(values, side)
    blank = (
        jnp.zeros((owners, capacity * side + 16, side), jnp.bfloat16)
        .at[:, capacity * side, : capacity * cell_count]
        .set(slot_weight.reshape(owners, capacity * cell_count))
    )
    position = jnp.arange(side, dtype=jnp.int32)
    inside = (jnp.abs(position[:, None] - position[None, :]) <= PSF_R + 4).astype(jnp.float32)
    vector_spec = pl.BlockSpec((group, 1, side), lambda b, slots: (b, 0, 0))
    return pl.pallas_call(
        warp_kernel,
        grid_spec=pltpu.PrefetchScalarGridSpec(
            num_scalar_prefetch=1,
            grid=(count // group,),
            in_specs=[
                vector_spec,
                vector_spec,
                pl.BlockSpec((side, side), lambda b, slots: (0, 0)),
                pl.BlockSpec((group, side, side), lambda b, slots: (b, 0, 0)),
                pl.BlockSpec(memory_space=pl.ANY),
            ],
            out_specs=pl.BlockSpec(memory_space=pl.ANY),
            scratch_shapes=[
                pltpu.VMEM((group, side, side), jnp.bfloat16),
                pltpu.SemaphoreType.DMA((group,)),
            ],
        ),
        out_shape=jax.ShapeDtypeStruct(blank.shape, jnp.bfloat16),
        input_output_aliases={5: 0},
        cost_estimate=pl.CostEstimate(
            flops=4 * count * side**3,
            transcendentals=0,
            bytes_accessed=2 * (2 * count * side * side + blank.size),
        ),
        interpret=interpret,
    )(slot_index, rows, cols, inside, images, blank)


def gain_pieces(gain):
    high = lax.reduce_precision(gain, exponent_bits=8, mantissa_bits=7)
    rest = gain - high
    middle = lax.reduce_precision(rest, exponent_bits=8, mantissa_bits=7)
    low = lax.reduce_precision(rest - middle, exponent_bits=8, mantissa_bits=7)
    return jnp.stack([high, middle, low]).astype(jnp.bfloat16)


def filter_taps():
    values = [
        math.exp(-float(tap * tap) / (2.0 * det_sigma * det_sigma))
        for tap in range(-DET_R, DET_R + 1)
    ]
    whole = sum(values)
    return [value / whole for value in values]


def smooth_columns(padded, width):
    taps = filter_taps()
    total = jnp.zeros((padded.shape[0], width), jnp.float32)
    for index, tap in enumerate(range(-DET_R, DET_R + 1)):
        total = total + taps[index] * padded[:, DET_R + tap : DET_R + tap + width]
    return total


def smooth_rows_valid(framed, height):
    taps = filter_taps()
    total = jnp.zeros((height, framed.shape[1]), jnp.float32)
    for index, tap in enumerate(range(-DET_R, DET_R + 1)):
        total = total + taps[index] * framed[DET_R + tap : DET_R + tap + height, :]
    return total


def local(images, offsets, widths, weights, dest, cells, band_gain):
    side = images.shape[-1]
    count = images.shape[1]
    sect_count = lax.axis_size("sect")
    sub_count = lax.axis_size("sub")
    owners = sect_count * sub_count
    capacity = max(2, -(-2 * count // owners))
    slot_count = owners * capacity
    values = band_values(offsets[0], widths[0])
    target = dest[0]
    same_owner = target[:, None] == target[None, :]
    block_order = jnp.arange(count, dtype=jnp.int32)
    earlier = block_order[None, :] < block_order[:, None]
    rank_within = jnp.sum(jnp.logical_and(same_owner, earlier), axis=1)
    slot_index = target * capacity + rank_within
    matching = jnp.arange(slot_count, dtype=jnp.int32)[:, None] == slot_index[None, :]
    source = jnp.sum(jnp.where(matching, block_order[None, :], 0), axis=1)
    placing = matching.astype(jnp.bfloat16)
    cell_weight = jnp.where(
        cells[0][:, None] == jnp.arange(CELL_DEV, dtype=jnp.int32)[None, :],
        weights[0][:, None],
        jnp.zeros((), jnp.bfloat16),
    )
    packed_weight = jnp.dot(placing, cell_weight, preferred_element_type=jnp.float32).astype(
        jnp.bfloat16
    )
    packed = warp_slots(
        images[0],
        values,
        jnp.minimum(slot_index, slot_count - 1).astype(jnp.int32),
        packed_weight.reshape(owners, capacity, CELL_DEV),
    )
    received = lax.all_to_all(packed, ("sect", "sub"), split_axis=0, concat_axis=0, tiled=True)
    received_weight = received[:, capacity * side, : capacity * CELL_DEV].reshape(
        slot_count, CELL_DEV
    )
    received = received[:, : capacity * side].reshape(slot_count, side, side)
    numerator = jnp.einsum(
        "sc,sij->icj", received_weight, received, preferred_element_type=jnp.float32
    )
    denominator = jnp.sum(received_weight.astype(jnp.float32), axis=0)
    cell_mean = (numerator / jnp.maximum(denominator, 1.0)[None, :, None]).astype(jnp.bfloat16)
    coadd = cell_mean.reshape(side, CELL_DEV * side)
    padded = extended(coadd, ((("sect", "sub"), 1),), DET_R)
    band_count = lax.axis_size("band")
    height = side // band_count
    framed = jnp.pad(padded, ((DET_R, DET_R), (0, 0)))
    gain_row = jnp.zeros((1, padded.shape[1]), jnp.bfloat16).at[0, :3].set(gain_pieces(band_gain[0]))
    span = height + 2 * DET_R
    me = lax.axis_index("band")
    own = lax.dynamic_slice_in_dim(framed, me * height, span, axis=0)
    combined = band_gain[0] * own.astype(jnp.float32)
    for shift in range(1, band_count):
        outgoing = jnp.concatenate(
            [lax.dynamic_slice_in_dim(framed, ((me + shift) % band_count) * height, span, axis=0), gain_row]
        )
        incoming = lax.ppermute(
            outgoing, "band", [(i, (i + shift) % band_count) for i in range(band_count)]
        )
        gain = jnp.sum(incoming[span, :3].astype(jnp.float32))
        combined = combined + gain * incoming[:span].astype(jnp.float32)
    detection = smooth_rows_valid(smooth_columns(combined, CELL_DEV * side), height)
    return (coadd[None], detection)


def solution(mesh):
    return jax.shard_map(
        local,
        mesh=mesh,
        in_specs=(
            P("band", ("groups", "sect", "sub"), None, None),
            P("band", ("groups", "sect", "sub"), None),
            P("band", ("groups", "sect", "sub"), None),
            P("band", ("groups", "sect", "sub")),
            P("band", ("groups", "sect", "sub")),
            P("band", ("groups", "sect", "sub")),
            P("band"),
        ),
        out_specs=(
            P("band", None, ("groups", "sect", "sub")),
            P("band", ("groups", "sect", "sub")),
        ),
        check_vma=False,
    )
```

```python
import math

import jax
import jax.numpy as jnp
from jax import lax
from jax.experimental import pallas as pl
from jax.experimental.pallas import tpu as pltpu
from jax.sharding import PartitionSpec as P

CELL_DEV = 4
PSF_R = 8
DET_R = 4


det_sigma = 3.0


def extended(array, sides, width):
    for axis, dim in sides:
        size, length = (lax.axis_size(axis), array.shape[dim])
        up = [(i, (i + 1) % size) for i in range(size - 1)]
        down = [(j, i) for i, j in up]
        last = lax.slice_in_dim(array, length - width, length, axis=dim)
        initial = lax.slice_in_dim(array, 0, width, axis=dim)
        before = lax.ppermute(last, axis, up)
        after = lax.ppermute(initial, axis, down)
        array = jnp.concatenate([before, array, after], axis=dim)
    return array


def lanczos_tap(spacing):
    return jnp.where(jnp.abs(spacing) < 3.0, jnp.sinc(spacing) * jnp.sinc(spacing / 3.0), 0.0)


def band_values(shift, spread):
    band = PSF_R + 4
    spacing = jnp.arange(-band, band + 1, dtype=jnp.float32)
    tap = jnp.arange(-PSF_R, PSF_R + 1, dtype=jnp.float32)
    tap_weight = jnp.exp(-spread[..., None] * (tap * tap))
    taps = lanczos_tap(spacing + (shift[..., None, None] + tap[:, None]))
    taps = jnp.concatenate([taps, jnp.ones(taps.shape[:-1] + (1,), jnp.float32)], axis=-1)
    summed = jnp.sum(tap_weight[..., None] * taps, axis=-2)
    return (summed[..., :-1] / summed[..., -1:]).astype(jnp.bfloat16)


def toeplitz(values, side):
    band = PSF_R + 4
    position = jnp.arange(side, dtype=jnp.int32)
    lag = position[:, None] - position[None, :]
    matrix = jnp.zeros(values.shape[:-1] + (side, side), jnp.bfloat16)
    for index in range(2 * band + 1):
        matrix = jnp.where(lag == index - band, values[..., index, None, None], matrix)
    return matrix


def base_rows(values, side):
    band = PSF_R + 4
    gap = jnp.zeros((values.shape[0], side - 2 * band - 1), jnp.float32)
    values = values.astype(jnp.float32)
    rows = jnp.concatenate([values[:, 0, band::-1], gap, values[:, 0, : band : -1]], axis=-1)
    cols = jnp.concatenate([values[:, 1, band:], gap, values[:, 1, :band]], axis=-1)
    return rows[:, None, :], cols[:, None, :]


def warp_kernel(slot_ref, rows_ref, cols_ref, inside_ref, image_ref, blank_ref, out_ref, done_ref, sems):
    side = image_ref.shape[-1]
    group = image_ref.shape[0]
    step = pl.program_id(0)
    inside = inside_ref[...]
    copies = []
    for member in range(group):
        row_base = jnp.broadcast_to(rows_ref[member], (side, side))
        col_base = jnp.broadcast_to(cols_ref[member], (side, side))
        row_kernel = (pltpu.roll(row_base, 0, 1, stride=1, stride_axis=0) * inside).astype(
            jnp.bfloat16
        )
        col_kernel_t = (pltpu.roll(col_base, 0, 1, stride=1, stride_axis=0) * inside).astype(
            jnp.bfloat16
        )
        section = jnp.dot(row_kernel, image_ref[member], preferred_element_type=jnp.float32)
        done_ref[member] = jnp.dot(
            section.astype(jnp.bfloat16), col_kernel_t, preferred_element_type=jnp.float32
        ).astype(jnp.bfloat16)
        slot = slot_ref[step * group + member]
        capacity = (out_ref.shape[1] - 16) // side
        target = out_ref.at[slot // capacity, pl.ds((slot % capacity) * side, side), :]
        copy = pltpu.make_async_copy(done_ref.at[member], target, sems.at[member])
        copy.start()
        copies.append(copy)
    for copy in copies:
        copy.wait()


def warp_slots(images, values, slot_index, slot_weight, interpret=False):
    count, side = images.shape[0], images.shape[-1]
    owners, capacity, cell_count = slot_weight.shape
    group = next(size for size in (8, 4, 2, 1) if count % size == 0)
    rows, cols = base_rows(values, side)
    blank = (
        jnp.zeros((owners, capacity * side + 16, side), jnp.bfloat16)
        .at[:, capacity * side, : capacity * cell_count]
        .set(slot_weight.reshape(owners, capacity * cell_count))
    )
    position = jnp.arange(side, dtype=jnp.int32)
    inside = (jnp.abs(position[:, None] - position[None, :]) <= PSF_R + 4).astype(jnp.float32)
    vector_spec = pl.BlockSpec((group, 1, side), lambda b, slots: (b, 0, 0))
    return pl.pallas_call(
        warp_kernel,
        grid_spec=pltpu.PrefetchScalarGridSpec(
            num_scalar_prefetch=1,
            grid=(count // group,),
            in_specs=[
                vector_spec,
                vector_spec,
                pl.BlockSpec((side, side), lambda b, slots: (0, 0)),
                pl.BlockSpec((group, side, side), lambda b, slots: (b, 0, 0)),
                pl.BlockSpec(memory_space=pl.ANY),
            ],
            out_specs=pl.BlockSpec(memory_space=pl.ANY),
            scratch_shapes=[
                pltpu.VMEM((group, side, side), jnp.bfloat16),
                pltpu.SemaphoreType.DMA((group,)),
            ],
        ),
        out_shape=jax.ShapeDtypeStruct(blank.shape, jnp.bfloat16),
        input_output_aliases={5: 0},
        cost_estimate=pl.CostEstimate(
            flops=4 * count * side**3,
            transcendentals=0,
            bytes_accessed=2 * (2 * count * side * side + blank.size),
        ),
        interpret=interpret,
    )(slot_index, rows, cols, inside, images, blank)


def gain_pieces(gain):
    high = lax.reduce_precision(gain, exponent_bits=8, mantissa_bits=7)
    rest = gain - high
    middle = lax.reduce_precision(rest, exponent_bits=8, mantissa_bits=7)
    low = lax.reduce_precision(rest - middle, exponent_bits=8, mantissa_bits=7)
    return jnp.stack([high, middle, low]).astype(jnp.bfloat16)


def filter_taps():
    values = [
        math.exp(-float(tap * tap) / (2.0 * det_sigma * det_sigma))
        for tap in range(-DET_R, DET_R + 1)
    ]
    whole = sum(values)
    return [value / whole for value in values]


def smooth_columns(padded, width):
    taps = filter_taps()
    total = jnp.zeros((padded.shape[0], width), jnp.float32)
    for index, tap in enumerate(range(-DET_R, DET_R + 1)):
        total = total + taps[index] * padded[:, DET_R + tap : DET_R + tap + width]
    return total


def smooth_rows_valid(framed, height):
    taps = filter_taps()
    total = jnp.zeros((height, framed.shape[1]), jnp.float32)
    for index, tap in enumerate(range(-DET_R, DET_R + 1)):
        total = total + taps[index] * framed[DET_R + tap : DET_R + tap + height, :]
    return total


def local(images, offsets, widths, weights, dest, cells, band_gain):
    side = images.shape[-1]
    count = images.shape[1]
    sect_count = lax.axis_size("sect")
    sub_count = lax.axis_size("sub")
    owners = sect_count * sub_count
    capacity = max(2, -(-2 * count // owners))
    slot_count = owners * capacity
    values = band_values(offsets[0], widths[0])
    target = dest[0]
    same_owner = target[:, None] == target[None, :]
    block_order = jnp.arange(count, dtype=jnp.int32)
    earlier = block_order[None, :] < block_order[:, None]
    rank_within = jnp.sum(jnp.logical_and(same_owner, earlier), axis=1)
    slot_index = target * capacity + rank_within
    matching = jnp.arange(slot_count, dtype=jnp.int32)[:, None] == slot_index[None, :]
    source = jnp.sum(jnp.where(matching, block_order[None, :], 0), axis=1)
    placing = matching.astype(jnp.bfloat16)
    cell_weight = jnp.where(
        cells[0][:, None] == jnp.arange(CELL_DEV, dtype=jnp.int32)[None, :],
        weights[0][:, None],
        jnp.zeros((), jnp.bfloat16),
    )
    packed_weight = jnp.dot(placing, cell_weight, preferred_element_type=jnp.float32).astype(
        jnp.bfloat16
    )
    packed = warp_slots(
        images[0],
        values,
        jnp.minimum(slot_index, slot_count - 1).astype(jnp.int32),
        packed_weight.reshape(owners, capacity, CELL_DEV),
    )
    received = lax.all_to_all(packed, ("sect", "sub"), split_axis=0, concat_axis=0, tiled=True)
    received_weight = received[:, capacity * side, : capacity * CELL_DEV].reshape(
        slot_count, CELL_DEV
    )
    received = received[:, : capacity * side].reshape(slot_count, side, side)
    numerator = jnp.einsum(
        "sc,sij->icj", received_weight, received, preferred_element_type=jnp.float32
    )
    denominator = jnp.sum(received_weight.astype(jnp.float32), axis=0)
    cell_mean = (numerator / jnp.maximum(denominator, 1.0)[None, :, None]).astype(jnp.bfloat16)
    coadd = cell_mean.reshape(side, CELL_DEV * side)
    padded = extended(coadd, ((("sect", "sub"), 1),), DET_R)
    band_count = lax.axis_size("band")
    height = side // band_count
    framed = jnp.pad(padded, ((DET_R, DET_R), (0, 0)))
    gain_row = jnp.zeros((1, padded.shape[1]), jnp.bfloat16).at[0, :3].set(gain_pieces(band_gain[0]))
    span = height + 2 * DET_R
    me = lax.axis_index("band")
    own = lax.dynamic_slice_in_dim(framed, me * height, span, axis=0)
    combined = band_gain[0] * own.astype(jnp.float32)
    for shift in range(1, band_count):
        outgoing = jnp.concatenate(
            [lax.dynamic_slice_in_dim(framed, ((me + shift) % band_count) * height, span, axis=0), gain_row]
        )
        incoming = lax.ppermute(
            outgoing, "band", [(i, (i + shift) % band_count) for i in range(band_count)]
        )
        gain = jnp.sum(incoming[span, :3].astype(jnp.float32))
        combined = combined + gain * incoming[:span].astype(jnp.float32)
    detection = smooth_rows_valid(smooth_columns(combined, CELL_DEV * side), height)
    return (coadd[None], detection)


def solution(mesh):
    return jax.shard_map(
        local,
        mesh=mesh,
        in_specs=(
            P("band", ("groups", "sect", "sub"), None, None),
            P("band", ("groups", "sect", "sub"), None),
            P("band", ("groups", "sect", "sub"), None),
            P("band", ("groups", "sect", "sub")),
            P("band", ("groups", "sect", "sub")),
            P("band", ("groups", "sect", "sub")),
            P("band"),
        ),
        out_specs=(
            P("band", None, ("groups", "sect", "sub")),
            P("band", ("groups", "sect", "sub")),
        ),
        check_vma=False,
    )
```

```python
import math

import jax
import jax.numpy as jnp
from jax import lax
from jax.experimental import pallas as pl
from jax.experimental.pallas import tpu as pltpu
from jax.sharding import PartitionSpec as P

CELL_DEV = 4
PSF_R = 8
DET_R = 4


det_sigma = 3.0


def extended(array, sides, width):
    for axis, dim in sides:
        size, length = (lax.axis_size(axis), array.shape[dim])
        up = [(i, (i + 1) % size) for i in range(size - 1)]
        down = [(j, i) for i, j in up]
        last = lax.slice_in_dim(array, length - width, length, axis=dim)
        initial = lax.slice_in_dim(array, 0, width, axis=dim)
        before = lax.ppermute(last, axis, up)
        after = lax.ppermute(initial, axis, down)
        array = jnp.concatenate([before, array, after], axis=dim)
    return array


def lanczos_tap(spacing):
    return jnp.where(jnp.abs(spacing) < 3.0, jnp.sinc(spacing) * jnp.sinc(spacing / 3.0), 0.0)


def band_values(shift, spread):
    band = PSF_R + 4
    spacing = jnp.arange(-band, band + 1, dtype=jnp.float32)
    tap = jnp.arange(-PSF_R, PSF_R + 1, dtype=jnp.float32)
    tap_weight = jnp.exp(-spread[..., None] * (tap * tap))
    taps = lanczos_tap(spacing + (shift[..., None, None] + tap[:, None]))
    taps = jnp.concatenate([taps, jnp.ones(taps.shape[:-1] + (1,), jnp.float32)], axis=-1)
    summed = jnp.sum(tap_weight[..., None] * taps, axis=-2)
    return (summed[..., :-1] / summed[..., -1:]).astype(jnp.bfloat16)


def toeplitz(values, side):
    band = PSF_R + 4
    position = jnp.arange(side, dtype=jnp.int32)
    lag = position[:, None] - position[None, :]
    matrix = jnp.zeros(values.shape[:-1] + (side, side), jnp.bfloat16)
    for index in range(2 * band + 1):
        matrix = jnp.where(lag == index - band, values[..., index, None, None], matrix)
    return matrix


def base_rows(values, side):
    band = PSF_R + 4
    gap = jnp.zeros((values.shape[0], side - 2 * band - 1), jnp.float32)
    values = values.astype(jnp.float32)
    rows = jnp.concatenate([values[:, 0, band::-1], gap, values[:, 0, : band : -1]], axis=-1)
    cols = jnp.concatenate([values[:, 1, band:], gap, values[:, 1, :band]], axis=-1)
    return jnp.stack([rows, cols], axis=1)


def warp_kernel(slot_ref, bases_ref, image_ref, blank_ref, out_ref, done_ref, sems):
    side = image_ref.shape[-1]
    group = image_ref.shape[0]
    step = pl.program_id(0)
    lag = lax.broadcasted_iota(jnp.int32, (side, side), 0) - lax.broadcasted_iota(
        jnp.int32, (side, side), 1
    )
    inside = (jnp.abs(lag) <= PSF_R + 4).astype(jnp.float32)
    copies = []
    for member in range(group):
        bases = bases_ref[member]
        row_base = jnp.broadcast_to(bases[0:1], (side, side))
        col_base = jnp.broadcast_to(bases[1:2], (side, side))
        row_kernel = (pltpu.roll(row_base, 0, 1, stride=1, stride_axis=0) * inside).astype(
            jnp.bfloat16
        )
        col_kernel_t = (pltpu.roll(col_base, 0, 1, stride=1, stride_axis=0) * inside).astype(
            jnp.bfloat16
        )
        section = jnp.dot(row_kernel, image_ref[member], preferred_element_type=jnp.float32)
        done_ref[member] = jnp.dot(
            section.astype(jnp.bfloat16), col_kernel_t, preferred_element_type=jnp.float32
        ).astype(jnp.bfloat16)
        slot = slot_ref[step * group + member]
        capacity = (out_ref.shape[1] - 16) // side
        target = out_ref.at[slot // capacity, pl.ds((slot % capacity) * side, side), :]
        copy = pltpu.make_async_copy(done_ref.at[member], target, sems.at[member])
        copy.start()
        copies.append(copy)
    for copy in copies:
        copy.wait()


def warp_slots(images, values, slot_index, slot_weight, interpret=False):
    count, side = images.shape[0], images.shape[-1]
    owners, capacity, cell_count = slot_weight.shape
    group = next(size for size in (8, 4, 2, 1) if count % size == 0)
    bases = base_rows(values, side)
    blank = (
        jnp.zeros((owners, capacity * side + 16, side), jnp.bfloat16)
        .at[:, capacity * side, : capacity * cell_count]
        .set(slot_weight.reshape(owners, capacity * cell_count))
    )
    return pl.pallas_call(
        warp_kernel,
        grid_spec=pltpu.PrefetchScalarGridSpec(
            num_scalar_prefetch=1,
            grid=(count // group,),
            in_specs=[
                pl.BlockSpec((group, 2, side), lambda b, slots: (b, 0, 0)),
                pl.BlockSpec((group, side, side), lambda b, slots: (b, 0, 0)),
                pl.BlockSpec(memory_space=pl.ANY),
            ],
            out_specs=pl.BlockSpec(memory_space=pl.ANY),
            scratch_shapes=[
                pltpu.VMEM((group, side, side), jnp.bfloat16),
                pltpu.SemaphoreType.DMA((group,)),
            ],
        ),
        out_shape=jax.ShapeDtypeStruct(blank.shape, jnp.bfloat16),
        input_output_aliases={3: 0},
        cost_estimate=pl.CostEstimate(
            flops=4 * count * side**3,
            transcendentals=0,
            bytes_accessed=2 * (2 * count * side * side + blank.size),
        ),
        interpret=interpret,
    )(slot_index, bases, images, blank)


def gain_pieces(gain):
    high = lax.reduce_precision(gain, exponent_bits=8, mantissa_bits=7)
    rest = gain - high
    middle = lax.reduce_precision(rest, exponent_bits=8, mantissa_bits=7)
    low = lax.reduce_precision(rest - middle, exponent_bits=8, mantissa_bits=7)
    return jnp.stack([high, middle, low]).astype(jnp.bfloat16)


def filter_taps():
    values = [
        math.exp(-float(tap * tap) / (2.0 * det_sigma * det_sigma))
        for tap in range(-DET_R, DET_R + 1)
    ]
    whole = sum(values)
    return [value / whole for value in values]


def smooth_columns(padded, width):
    taps = filter_taps()
    total = jnp.zeros((padded.shape[0], width), jnp.float32)
    for index, tap in enumerate(range(-DET_R, DET_R + 1)):
        total = total + taps[index] * padded[:, DET_R + tap : DET_R + tap + width]
    return total


def smooth_rows_valid(framed, height):
    taps = filter_taps()
    total = jnp.zeros((height, framed.shape[1]), jnp.float32)
    for index, tap in enumerate(range(-DET_R, DET_R + 1)):
        total = total + taps[index] * framed[DET_R + tap : DET_R + tap + height, :]
    return total


def local(images, offsets, widths, weights, dest, cells, band_gain):
    side = images.shape[-1]
    count = images.shape[1]
    sect_count = lax.axis_size("sect")
    sub_count = lax.axis_size("sub")
    owners = sect_count * sub_count
    capacity = max(2, -(-2 * count // owners))
    slot_count = owners * capacity
    values = band_values(offsets[0], widths[0])
    target = dest[0]
    same_owner = target[:, None] == target[None, :]
    block_order = jnp.arange(count, dtype=jnp.int32)
    earlier = block_order[None, :] < block_order[:, None]
    rank_within = jnp.sum(jnp.logical_and(same_owner, earlier), axis=1)
    slot_index = target * capacity + rank_within
    matching = jnp.arange(slot_count, dtype=jnp.int32)[:, None] == slot_index[None, :]
    source = jnp.sum(jnp.where(matching, block_order[None, :], 0), axis=1)
    placing = matching.astype(jnp.bfloat16)
    cell_weight = jnp.where(
        cells[0][:, None] == jnp.arange(CELL_DEV, dtype=jnp.int32)[None, :],
        weights[0][:, None],
        jnp.zeros((), jnp.bfloat16),
    )
    packed_weight = jnp.dot(placing, cell_weight, preferred_element_type=jnp.float32).astype(
        jnp.bfloat16
    )
    packed = warp_slots(
        images[0],
        values,
        jnp.minimum(slot_index, slot_count - 1).astype(jnp.int32),
        packed_weight.reshape(owners, capacity, CELL_DEV),
    )
    received = lax.all_to_all(packed, ("sect", "sub"), split_axis=0, concat_axis=0, tiled=True)
    received_weight = received[:, capacity * side, : capacity * CELL_DEV].reshape(
        slot_count, CELL_DEV
    )
    received = received[:, : capacity * side].reshape(slot_count, side, side)
    numerator = jnp.einsum(
        "sc,sij->icj", received_weight, received, preferred_element_type=jnp.float32
    )
    denominator = jnp.sum(received_weight.astype(jnp.float32), axis=0)
    cell_mean = (numerator / jnp.maximum(denominator, 1.0)[None, :, None]).astype(jnp.bfloat16)
    coadd = cell_mean.reshape(side, CELL_DEV * side)
    padded = extended(coadd, ((("sect", "sub"), 1),), DET_R)
    band_count = lax.axis_size("band")
    height = side // band_count
    framed = jnp.pad(padded, ((DET_R, DET_R), (0, 0)))
    gain_row = jnp.zeros((1, padded.shape[1]), jnp.bfloat16).at[0, :3].set(gain_pieces(band_gain[0]))
    span = height + 2 * DET_R
    me = lax.axis_index("band")
    own = lax.dynamic_slice_in_dim(framed, me * height, span, axis=0)
    combined = band_gain[0] * own.astype(jnp.float32)
    for shift in range(1, band_count):
        outgoing = jnp.concatenate(
            [lax.dynamic_slice_in_dim(framed, ((me + shift) % band_count) * height, span, axis=0), gain_row]
        )
        incoming = lax.ppermute(
            outgoing, "band", [(i, (i + shift) % band_count) for i in range(band_count)]
        )
        gain = jnp.sum(incoming[span, :3].astype(jnp.float32))
        combined = combined + gain * incoming[:span].astype(jnp.float32)
    detection = smooth_rows_valid(smooth_columns(combined, CELL_DEV * side), height)
    return (coadd[None], detection)


def solution(mesh):
    return jax.shard_map(
        local,
        mesh=mesh,
        in_specs=(
            P("band", ("groups", "sect", "sub"), None, None),
            P("band", ("groups", "sect", "sub"), None),
            P("band", ("groups", "sect", "sub"), None),
            P("band", ("groups", "sect", "sub")),
            P("band", ("groups", "sect", "sub")),
            P("band", ("groups", "sect", "sub")),
            P("band"),
        ),
        out_specs=(
            P("band", None, ("groups", "sect", "sub")),
            P("band", ("groups", "sect", "sub")),
        ),
        check_vma=False,
    )
```

```python
import math

import jax
import jax.numpy as jnp
from jax import lax
from jax.experimental import pallas as pl
from jax.experimental.pallas import tpu as pltpu
from jax.sharding import PartitionSpec as P

CELL_DEV = 4
PSF_R = 8
DET_R = 4


det_sigma = 3.0


def extended(array, sides, width):
    for axis, dim in sides:
        size, length = (lax.axis_size(axis), array.shape[dim])
        up = [(i, (i + 1) % size) for i in range(size - 1)]
        down = [(j, i) for i, j in up]
        last = lax.slice_in_dim(array, length - width, length, axis=dim)
        initial = lax.slice_in_dim(array, 0, width, axis=dim)
        before = lax.ppermute(last, axis, up)
        after = lax.ppermute(initial, axis, down)
        array = jnp.concatenate([before, array, after], axis=dim)
    return array


def lanczos_tap(spacing):
    return jnp.where(jnp.abs(spacing) < 3.0, jnp.sinc(spacing) * jnp.sinc(spacing / 3.0), 0.0)


def band_values(shift, spread):
    band = PSF_R + 4
    spacing = jnp.arange(-band, band + 1, dtype=jnp.float32)
    tap = jnp.arange(-PSF_R, PSF_R + 1, dtype=jnp.float32)
    tap_weight = jnp.exp(-spread[..., None] * (tap * tap))
    taps = lanczos_tap(spacing + (shift[..., None, None] + tap[:, None]))
    taps = jnp.concatenate([taps, jnp.ones(taps.shape[:-1] + (1,), jnp.float32)], axis=-1)
    summed = jnp.sum(tap_weight[..., None] * taps, axis=-2)
    return (summed[..., :-1] / summed[..., -1:]).astype(jnp.bfloat16)


def toeplitz(values, side):
    band = PSF_R + 4
    position = jnp.arange(side, dtype=jnp.int32)
    lag = position[:, None] - position[None, :]
    matrix = jnp.zeros(values.shape[:-1] + (side, side), jnp.bfloat16)
    for index in range(2 * band + 1):
        matrix = jnp.where(lag == index - band, values[..., index, None, None], matrix)
    return matrix


def base_rows(values, side):
    band = PSF_R + 4
    gap = jnp.zeros((values.shape[0], side - 2 * band - 1), jnp.float32)
    values = values.astype(jnp.float32)
    rows = jnp.concatenate([values[:, 0, band::-1], gap, values[:, 0, : band : -1]], axis=-1)
    cols = jnp.concatenate([values[:, 1, band:], gap, values[:, 1, :band]], axis=-1)
    return jnp.stack([rows, cols], axis=1)


def warp_kernel(slot_ref, bases_ref, image_ref, blank_ref, out_ref, done_ref, sems):
    side = image_ref.shape[-1]
    group = image_ref.shape[0]
    step = pl.program_id(0)
    lag = lax.broadcasted_iota(jnp.int32, (side, side), 0) - lax.broadcasted_iota(
        jnp.int32, (side, side), 1
    )
    inside = (jnp.abs(lag) <= PSF_R + 4).astype(jnp.float32)
    copies = []
    for member in range(group):
        bases = bases_ref[member]
        row_base = jnp.broadcast_to(bases[0:1], (side, side))
        col_base = jnp.broadcast_to(bases[1:2], (side, side))
        row_kernel = (pltpu.roll(row_base, 0, 1, stride=1, stride_axis=0) * inside).astype(
            jnp.bfloat16
        )
        col_kernel_t = (pltpu.roll(col_base, 0, 1, stride=1, stride_axis=0) * inside).astype(
            jnp.bfloat16
        )
        section = jnp.dot(row_kernel, image_ref[member], preferred_element_type=jnp.float32)
        done_ref[member] = jnp.dot(
            section.astype(jnp.bfloat16), col_kernel_t, preferred_element_type=jnp.float32
        ).astype(jnp.bfloat16)
        slot = slot_ref[step * group + member]
        capacity = (out_ref.shape[1] - 16) // side
        target = out_ref.at[slot // capacity, pl.ds((slot % capacity) * side, side), :]
        copy = pltpu.make_async_copy(done_ref.at[member], target, sems.at[member])
        copy.start()
        copies.append(copy)
    for copy in copies:
        copy.wait()


def warp_slots(images, values, slot_index, slot_weight, interpret=False):
    count, side = images.shape[0], images.shape[-1]
    owners, capacity, cell_count = slot_weight.shape
    group = next(size for size in (16, 8, 4, 2, 1) if count % size == 0)
    bases = base_rows(values, side)
    blank = (
        jnp.zeros((owners, capacity * side + 16, side), jnp.bfloat16)
        .at[:, capacity * side, : capacity * cell_count]
        .set(slot_weight.reshape(owners, capacity * cell_count))
    )
    return pl.pallas_call(
        warp_kernel,
        grid_spec=pltpu.PrefetchScalarGridSpec(
            num_scalar_prefetch=1,
            grid=(count // group,),
            in_specs=[
                pl.BlockSpec((group, 2, side), lambda b, slots: (b, 0, 0)),
                pl.BlockSpec((group, side, side), lambda b, slots: (b, 0, 0)),
                pl.BlockSpec(memory_space=pl.ANY),
            ],
            out_specs=pl.BlockSpec(memory_space=pl.ANY),
            scratch_shapes=[
                pltpu.VMEM((group, side, side), jnp.bfloat16),
                pltpu.SemaphoreType.DMA((group,)),
            ],
        ),
        out_shape=jax.ShapeDtypeStruct(blank.shape, jnp.bfloat16),
        input_output_aliases={3: 0},
        cost_estimate=pl.CostEstimate(
            flops=4 * count * side**3,
            transcendentals=0,
            bytes_accessed=2 * (2 * count * side * side + blank.size),
        ),
        interpret=interpret,
    )(slot_index, bases, images, blank)


def gain_pieces(gain):
    high = lax.reduce_precision(gain, exponent_bits=8, mantissa_bits=7)
    rest = gain - high
    middle = lax.reduce_precision(rest, exponent_bits=8, mantissa_bits=7)
    low = lax.reduce_precision(rest - middle, exponent_bits=8, mantissa_bits=7)
    return jnp.stack([high, middle, low]).astype(jnp.bfloat16)


def filter_taps():
    values = [
        math.exp(-float(tap * tap) / (2.0 * det_sigma * det_sigma))
        for tap in range(-DET_R, DET_R + 1)
    ]
    whole = sum(values)
    return [value / whole for value in values]


def smooth_columns(padded, width):
    taps = filter_taps()
    total = jnp.zeros((padded.shape[0], width), jnp.float32)
    for index, tap in enumerate(range(-DET_R, DET_R + 1)):
        total = total + taps[index] * padded[:, DET_R + tap : DET_R + tap + width]
    return total


def smooth_rows_valid(framed, height):
    taps = filter_taps()
    total = jnp.zeros((height, framed.shape[1]), jnp.float32)
    for index, tap in enumerate(range(-DET_R, DET_R + 1)):
        total = total + taps[index] * framed[DET_R + tap : DET_R + tap + height, :]
    return total


def local(images, offsets, widths, weights, dest, cells, band_gain):
    side = images.shape[-1]
    count = images.shape[1]
    sect_count = lax.axis_size("sect")
    sub_count = lax.axis_size("sub")
    owners = sect_count * sub_count
    capacity = max(2, -(-2 * count // owners))
    slot_count = owners * capacity
    values = band_values(offsets[0], widths[0])
    target = dest[0]
    same_owner = target[:, None] == target[None, :]
    block_order = jnp.arange(count, dtype=jnp.int32)
    earlier = block_order[None, :] < block_order[:, None]
    rank_within = jnp.sum(jnp.logical_and(same_owner, earlier), axis=1)
    slot_index = target * capacity + rank_within
    matching = jnp.arange(slot_count, dtype=jnp.int32)[:, None] == slot_index[None, :]
    source = jnp.sum(jnp.where(matching, block_order[None, :], 0), axis=1)
    placing = matching.astype(jnp.bfloat16)
    cell_weight = jnp.where(
        cells[0][:, None] == jnp.arange(CELL_DEV, dtype=jnp.int32)[None, :],
        weights[0][:, None],
        jnp.zeros((), jnp.bfloat16),
    )
    packed_weight = jnp.dot(placing, cell_weight, preferred_element_type=jnp.float32).astype(
        jnp.bfloat16
    )
    packed = warp_slots(
        images[0],
        values,
        jnp.minimum(slot_index, slot_count - 1).astype(jnp.int32),
        packed_weight.reshape(owners, capacity, CELL_DEV),
    )
    received = lax.all_to_all(packed, ("sect", "sub"), split_axis=0, concat_axis=0, tiled=True)
    received_weight = received[:, capacity * side, : capacity * CELL_DEV].reshape(
        slot_count, CELL_DEV
    )
    received = received[:, : capacity * side].reshape(slot_count, side, side)
    numerator = jnp.einsum(
        "sc,sij->icj", received_weight, received, preferred_element_type=jnp.float32
    )
    denominator = jnp.sum(received_weight.astype(jnp.float32), axis=0)
    cell_mean = (numerator / jnp.maximum(denominator, 1.0)[None, :, None]).astype(jnp.bfloat16)
    coadd = cell_mean.reshape(side, CELL_DEV * side)
    padded = extended(coadd, ((("sect", "sub"), 1),), DET_R)
    band_count = lax.axis_size("band")
    height = side // band_count
    framed = jnp.pad(padded, ((DET_R, DET_R), (0, 0)))
    gain_row = jnp.zeros((1, padded.shape[1]), jnp.bfloat16).at[0, :3].set(gain_pieces(band_gain[0]))
    span = height + 2 * DET_R
    me = lax.axis_index("band")
    own = lax.dynamic_slice_in_dim(framed, me * height, span, axis=0)
    combined = band_gain[0] * own.astype(jnp.float32)
    for shift in range(1, band_count):
        outgoing = jnp.concatenate(
            [lax.dynamic_slice_in_dim(framed, ((me + shift) % band_count) * height, span, axis=0), gain_row]
        )
        incoming = lax.ppermute(
            outgoing, "band", [(i, (i + shift) % band_count) for i in range(band_count)]
        )
        gain = jnp.sum(incoming[span, :3].astype(jnp.float32))
        combined = combined + gain * incoming[:span].astype(jnp.float32)
    detection = smooth_rows_valid(smooth_columns(combined, CELL_DEV * side), height)
    return (coadd[None], detection)


def solution(mesh):
    return jax.shard_map(
        local,
        mesh=mesh,
        in_specs=(
            P("band", ("groups", "sect", "sub"), None, None),
            P("band", ("groups", "sect", "sub"), None),
            P("band", ("groups", "sect", "sub"), None),
            P("band", ("groups", "sect", "sub")),
            P("band", ("groups", "sect", "sub")),
            P("band", ("groups", "sect", "sub")),
            P("band"),
        ),
        out_specs=(
            P("band", None, ("groups", "sect", "sub")),
            P("band", ("groups", "sect", "sub")),
        ),
        check_vma=False,
    )
```

```python
import math

import jax
import jax.numpy as jnp
from jax import lax
from jax.experimental import pallas as pl
from jax.experimental.pallas import tpu as pltpu
from jax.sharding import PartitionSpec as P

CELL_DEV = 4
PSF_R = 8
DET_R = 4


det_sigma = 3.0


def extended(array, sides, width):
    for axis, dim in sides:
        size, length = (lax.axis_size(axis), array.shape[dim])
        up = [(i, (i + 1) % size) for i in range(size - 1)]
        down = [(j, i) for i, j in up]
        last = lax.slice_in_dim(array, length - width, length, axis=dim)
        initial = lax.slice_in_dim(array, 0, width, axis=dim)
        before = lax.ppermute(last, axis, up)
        after = lax.ppermute(initial, axis, down)
        array = jnp.concatenate([before, array, after], axis=dim)
    return array


def lanczos_tap(spacing):
    return jnp.where(jnp.abs(spacing) < 3.0, jnp.sinc(spacing) * jnp.sinc(spacing / 3.0), 0.0)


def band_values(shift, spread):
    band = PSF_R + 4
    spacing = jnp.arange(-band, band + 1, dtype=jnp.float32)
    tap = jnp.arange(-PSF_R, PSF_R + 1, dtype=jnp.float32)
    tap_weight = jnp.exp(-spread[..., None] * (tap * tap))
    taps = lanczos_tap(spacing + (shift[..., None, None] + tap[:, None]))
    taps = jnp.concatenate([taps, jnp.ones(taps.shape[:-1] + (1,), jnp.float32)], axis=-1)
    summed = jnp.sum(tap_weight[..., None] * taps, axis=-2)
    return (summed[..., :-1] / summed[..., -1:]).astype(jnp.bfloat16)


def toeplitz(values, side):
    band = PSF_R + 4
    position = jnp.arange(side, dtype=jnp.int32)
    lag = position[:, None] - position[None, :]
    matrix = jnp.zeros(values.shape[:-1] + (side, side), jnp.bfloat16)
    for index in range(2 * band + 1):
        matrix = jnp.where(lag == index - band, values[..., index, None, None], matrix)
    return matrix


def base_rows(values, side):
    band = PSF_R + 4
    gap = jnp.zeros((values.shape[0], side - 2 * band - 1), jnp.float32)
    values = values.astype(jnp.float32)
    rows = jnp.concatenate([values[:, 0, band::-1], gap, values[:, 0, : band : -1]], axis=-1)
    cols = jnp.concatenate([values[:, 1, band:], gap, values[:, 1, :band]], axis=-1)
    return jnp.stack([rows, cols], axis=1)


def warp_kernel(slot_ref, bases_ref, image_ref, blank_ref, out_ref, done_ref, sems):
    side = image_ref.shape[-1]
    group = image_ref.shape[0]
    step = pl.program_id(0)
    lag = lax.broadcasted_iota(jnp.int32, (side, side), 0) - lax.broadcasted_iota(
        jnp.int32, (side, side), 1
    )
    inside = (jnp.abs(lag) <= PSF_R + 4).astype(jnp.float32)
    copies = []
    for member in range(group):
        bases = bases_ref[member]
        row_base = jnp.broadcast_to(bases[0:1], (side, side))
        col_base = jnp.broadcast_to(bases[1:2], (side, side))
        row_kernel = (pltpu.roll(row_base, 0, 1, stride=1, stride_axis=0) * inside).astype(
            jnp.bfloat16
        )
        col_kernel_t = (pltpu.roll(col_base, 0, 1, stride=1, stride_axis=0) * inside).astype(
            jnp.bfloat16
        )
        section = jnp.dot(row_kernel, image_ref[member], preferred_element_type=jnp.float32)
        done_ref[member] = jnp.dot(
            section.astype(jnp.bfloat16), col_kernel_t, preferred_element_type=jnp.float32
        ).astype(jnp.bfloat16)
        slot = slot_ref[step * group + member]
        capacity = (out_ref.shape[1] - 16) // side
        target = out_ref.at[slot // capacity, pl.ds((slot % capacity) * side, side), :]
        copy = pltpu.make_async_copy(done_ref.at[member], target, sems.at[member])
        copy.start()
        copies.append(copy)
    for copy in copies:
        copy.wait()


def warp_slots(images, values, slot_index, slot_weight, interpret=False):
    count, side = images.shape[0], images.shape[-1]
    owners, capacity, cell_count = slot_weight.shape
    group = next(size for size in (16, 8, 4, 2, 1) if count % size == 0)
    bases = base_rows(values, side)
    blank = (
        jnp.zeros((owners, capacity * side + 16, side), jnp.bfloat16)
        .at[:, capacity * side, : capacity * cell_count]
        .set(slot_weight.reshape(owners, capacity * cell_count))
    )
    return pl.pallas_call(
        warp_kernel,
        grid_spec=pltpu.PrefetchScalarGridSpec(
            num_scalar_prefetch=1,
            grid=(count // group,),
            in_specs=[
                pl.BlockSpec((group, 2, side), lambda b, slots: (b, 0, 0)),
                pl.BlockSpec((group, side, side), lambda b, slots: (b, 0, 0)),
                pl.BlockSpec(memory_space=pl.ANY),
            ],
            out_specs=pl.BlockSpec(memory_space=pl.ANY),
            scratch_shapes=[
                pltpu.VMEM((group, side, side), jnp.bfloat16),
                pltpu.SemaphoreType.DMA((group,)),
            ],
        ),
        out_shape=jax.ShapeDtypeStruct(blank.shape, jnp.bfloat16),
        input_output_aliases={3: 0},
        cost_estimate=pl.CostEstimate(
            flops=4 * count * side**3,
            transcendentals=0,
            bytes_accessed=2 * (2 * count * side * side + blank.size),
        ),
        interpret=interpret,
    )(slot_index, bases, images, blank)


def gain_pieces(gain):
    high = lax.reduce_precision(gain, exponent_bits=8, mantissa_bits=7)
    rest = gain - high
    middle = lax.reduce_precision(rest, exponent_bits=8, mantissa_bits=7)
    low = lax.reduce_precision(rest - middle, exponent_bits=8, mantissa_bits=7)
    return jnp.stack([high, middle, low]).astype(jnp.bfloat16)


def filter_taps():
    values = [
        math.exp(-float(tap * tap) / (2.0 * det_sigma * det_sigma))
        for tap in range(-DET_R, DET_R + 1)
    ]
    whole = sum(values)
    return [value / whole for value in values]


def smooth_columns(padded, width):
    taps = filter_taps()
    total = jnp.zeros((padded.shape[0], width), jnp.float32)
    for index, tap in enumerate(range(-DET_R, DET_R + 1)):
        total = total + taps[index] * padded[:, DET_R + tap : DET_R + tap + width]
    return total


def smooth_rows_valid(framed, height):
    taps = filter_taps()
    total = jnp.zeros((height, framed.shape[1]), jnp.float32)
    for index, tap in enumerate(range(-DET_R, DET_R + 1)):
        total = total + taps[index] * framed[DET_R + tap : DET_R + tap + height, :]
    return total


def local(images, offsets, widths, weights, dest, cells, band_gain):
    side = images.shape[-1]
    count = images.shape[1]
    sect_count = lax.axis_size("sect")
    sub_count = lax.axis_size("sub")
    owners = sect_count * sub_count
    capacity = max(2, -(-2 * count // owners))
    slot_count = owners * capacity
    values = band_values(offsets[0], widths[0])
    target = dest[0]
    same_owner = target[:, None] == target[None, :]
    block_order = jnp.arange(count, dtype=jnp.int32)
    earlier = block_order[None, :] < block_order[:, None]
    rank_within = jnp.sum(jnp.logical_and(same_owner, earlier), axis=1)
    slot_index = target * capacity + rank_within
    matching = jnp.arange(slot_count, dtype=jnp.int32)[:, None] == slot_index[None, :]
    source = jnp.sum(jnp.where(matching, block_order[None, :], 0), axis=1)
    placing = matching.astype(jnp.bfloat16)
    cell_weight = jnp.where(
        cells[0][:, None] == jnp.arange(CELL_DEV, dtype=jnp.int32)[None, :],
        weights[0][:, None],
        jnp.zeros((), jnp.bfloat16),
    )
    packed_weight = jnp.dot(placing, cell_weight, preferred_element_type=jnp.float32).astype(
        jnp.bfloat16
    )
    packed = warp_slots(
        images[0],
        values,
        jnp.minimum(slot_index, slot_count - 1).astype(jnp.int32),
        packed_weight.reshape(owners, capacity, CELL_DEV),
    )
    received = lax.all_to_all(packed, ("sect", "sub"), split_axis=0, concat_axis=0, tiled=True)
    received_weight = received[:, capacity * side, : capacity * CELL_DEV].reshape(
        owners, capacity, CELL_DEV
    )
    numerator = sum(
        jnp.einsum(
            "oc,oij->icj",
            received_weight[:, rank],
            received[:, rank * side : (rank + 1) * side],
            preferred_element_type=jnp.float32,
        )
        for rank in range(capacity)
    )
    denominator = jnp.sum(received_weight.astype(jnp.float32), axis=(0, 1))
    cell_mean = (numerator / jnp.maximum(denominator, 1.0)[None, :, None]).astype(jnp.bfloat16)
    coadd = cell_mean.reshape(side, CELL_DEV * side)
    padded = extended(coadd, ((("sect", "sub"), 1),), DET_R)
    band_count = lax.axis_size("band")
    height = side // band_count
    framed = jnp.pad(padded, ((DET_R, DET_R), (0, 0)))
    gain_row = jnp.zeros((1, padded.shape[1]), jnp.bfloat16).at[0, :3].set(gain_pieces(band_gain[0]))
    span = height + 2 * DET_R
    me = lax.axis_index("band")
    own = lax.dynamic_slice_in_dim(framed, me * height, span, axis=0)
    combined = band_gain[0] * own.astype(jnp.float32)
    for shift in range(1, band_count):
        outgoing = jnp.concatenate(
            [lax.dynamic_slice_in_dim(framed, ((me + shift) % band_count) * height, span, axis=0), gain_row]
        )
        incoming = lax.ppermute(
            outgoing, "band", [(i, (i + shift) % band_count) for i in range(band_count)]
        )
        gain = jnp.sum(incoming[span, :3].astype(jnp.float32))
        combined = combined + gain * incoming[:span].astype(jnp.float32)
    detection = smooth_rows_valid(smooth_columns(combined, CELL_DEV * side), height)
    return (coadd[None], detection)


def solution(mesh):
    return jax.shard_map(
        local,
        mesh=mesh,
        in_specs=(
            P("band", ("groups", "sect", "sub"), None, None),
            P("band", ("groups", "sect", "sub"), None),
            P("band", ("groups", "sect", "sub"), None),
            P("band", ("groups", "sect", "sub")),
            P("band", ("groups", "sect", "sub")),
            P("band", ("groups", "sect", "sub")),
            P("band"),
        ),
        out_specs=(
            P("band", None, ("groups", "sect", "sub")),
            P("band", ("groups", "sect", "sub")),
        ),
        check_vma=False,
    )
```

```python
import math

import jax
import jax.numpy as jnp
from jax import lax
from jax.experimental import pallas as pl
from jax.experimental.pallas import tpu as pltpu
from jax.sharding import PartitionSpec as P

CELL_DEV = 4
PSF_R = 8
DET_R = 4


det_sigma = 3.0


def extended(array, sides, width):
    for axis, dim in sides:
        size, length = (lax.axis_size(axis), array.shape[dim])
        up = [(i, (i + 1) % size) for i in range(size - 1)]
        down = [(j, i) for i, j in up]
        last = lax.slice_in_dim(array, length - width, length, axis=dim)
        initial = lax.slice_in_dim(array, 0, width, axis=dim)
        before = lax.ppermute(last, axis, up)
        after = lax.ppermute(initial, axis, down)
        array = jnp.concatenate([before, array, after], axis=dim)
    return array


def lanczos_tap(spacing):
    return jnp.where(jnp.abs(spacing) < 3.0, jnp.sinc(spacing) * jnp.sinc(spacing / 3.0), 0.0)


def band_values(shift, spread):
    band = PSF_R + 4
    spacing = jnp.arange(-band, band + 1, dtype=jnp.float32)
    tap = jnp.arange(-PSF_R, PSF_R + 1, dtype=jnp.float32)
    tap_weight = jnp.exp(-spread[..., None] * (tap * tap))
    taps = lanczos_tap(spacing + (shift[..., None, None] + tap[:, None]))
    taps = jnp.concatenate([taps, jnp.ones(taps.shape[:-1] + (1,), jnp.float32)], axis=-1)
    summed = jnp.sum(tap_weight[..., None] * taps, axis=-2)
    return (summed[..., :-1] / summed[..., -1:]).astype(jnp.bfloat16)


def toeplitz(values, side):
    band = PSF_R + 4
    position = jnp.arange(side, dtype=jnp.int32)
    lag = position[:, None] - position[None, :]
    matrix = jnp.zeros(values.shape[:-1] + (side, side), jnp.bfloat16)
    for index in range(2 * band + 1):
        matrix = jnp.where(lag == index - band, values[..., index, None, None], matrix)
    return matrix


def base_rows(values, side):
    band = PSF_R + 4
    gap = jnp.zeros((values.shape[0], side - 2 * band - 1), jnp.float32)
    values = values.astype(jnp.float32)
    rows = jnp.concatenate([values[:, 0, band::-1], gap, values[:, 0, : band : -1]], axis=-1)
    cols = jnp.concatenate([values[:, 1, band:], gap, values[:, 1, :band]], axis=-1)
    return jnp.stack([rows, cols], axis=1)


def warp_kernel(slot_ref, bases_ref, image_ref, blank_ref, out_ref, done_ref, sems):
    side = image_ref.shape[-1]
    group = image_ref.shape[0]
    step = pl.program_id(0)
    lag = lax.broadcasted_iota(jnp.int32, (side, side), 0) - lax.broadcasted_iota(
        jnp.int32, (side, side), 1
    )
    inside = (jnp.abs(lag) <= PSF_R + 4).astype(jnp.float32)
    copies = []
    for member in range(group):
        bases = bases_ref[member]
        row_base = jnp.broadcast_to(bases[0:1], (side, side))
        col_base = jnp.broadcast_to(bases[1:2], (side, side))
        row_kernel = (pltpu.roll(row_base, 0, 1, stride=1, stride_axis=0) * inside).astype(
            jnp.bfloat16
        )
        col_kernel_t = (pltpu.roll(col_base, 0, 1, stride=1, stride_axis=0) * inside).astype(
            jnp.bfloat16
        )
        section = jnp.dot(row_kernel, image_ref[member], preferred_element_type=jnp.float32)
        done_ref[member] = jnp.dot(
            section.astype(jnp.bfloat16), col_kernel_t, preferred_element_type=jnp.float32
        ).astype(jnp.bfloat16)
        slot = slot_ref[step * group + member]
        capacity = (out_ref.shape[1] - 16) // side
        target = out_ref.at[slot // capacity, pl.ds((slot % capacity) * side, side), :]
        copy = pltpu.make_async_copy(done_ref.at[member], target, sems.at[member])
        copy.start()
        copies.append(copy)
    for copy in copies:
        copy.wait()


def warp_slots(images, values, slot_index, slot_weight, interpret=False):
    count, side = images.shape[0], images.shape[-1]
    owners, capacity, cell_count = slot_weight.shape
    group = next(size for size in (16, 8, 4, 2, 1) if count % size == 0)
    bases = base_rows(values, side)
    blank = (
        jnp.zeros((owners, capacity * side + 16, side), jnp.bfloat16)
        .at[:, capacity * side, : capacity * cell_count]
        .set(slot_weight.reshape(owners, capacity * cell_count))
    )
    return pl.pallas_call(
        warp_kernel,
        grid_spec=pltpu.PrefetchScalarGridSpec(
            num_scalar_prefetch=1,
            grid=(count // group,),
            in_specs=[
                pl.BlockSpec((group, 2, side), lambda b, slots: (b, 0, 0)),
                pl.BlockSpec((group, side, side), lambda b, slots: (b, 0, 0)),
                pl.BlockSpec(memory_space=pl.ANY),
            ],
            out_specs=pl.BlockSpec(memory_space=pl.ANY),
            scratch_shapes=[
                pltpu.VMEM((group, side, side), jnp.bfloat16),
                pltpu.SemaphoreType.DMA((group,)),
            ],
        ),
        out_shape=jax.ShapeDtypeStruct(blank.shape, jnp.bfloat16),
        input_output_aliases={3: 0},
        cost_estimate=pl.CostEstimate(
            flops=4 * count * side**3,
            transcendentals=0,
            bytes_accessed=2 * (2 * count * side * side + blank.size),
        ),
        interpret=interpret,
    )(slot_index, bases, images, blank)


def gain_pieces(gain):
    high = lax.reduce_precision(gain, exponent_bits=8, mantissa_bits=7)
    rest = gain - high
    middle = lax.reduce_precision(rest, exponent_bits=8, mantissa_bits=7)
    low = lax.reduce_precision(rest - middle, exponent_bits=8, mantissa_bits=7)
    return jnp.stack([high, middle, low]).astype(jnp.bfloat16)


def filter_taps():
    values = [
        math.exp(-float(tap * tap) / (2.0 * det_sigma * det_sigma))
        for tap in range(-DET_R, DET_R + 1)
    ]
    whole = sum(values)
    return [value / whole for value in values]


def smooth_columns(padded, width):
    taps = filter_taps()
    total = jnp.zeros((padded.shape[0], width), jnp.float32)
    for index, tap in enumerate(range(-DET_R, DET_R + 1)):
        total = total + taps[index] * padded[:, DET_R + tap : DET_R + tap + width]
    return total


def smooth_rows_valid(framed, height):
    taps = filter_taps()
    total = jnp.zeros((height, framed.shape[1]), jnp.float32)
    for index, tap in enumerate(range(-DET_R, DET_R + 1)):
        total = total + taps[index] * framed[DET_R + tap : DET_R + tap + height, :]
    return total


def local(images, offsets, widths, weights, dest, cells, band_gain):
    side = images.shape[-1]
    count = images.shape[1]
    sect_count = lax.axis_size("sect")
    sub_count = lax.axis_size("sub")
    owners = sect_count * sub_count
    capacity = max(2, -(-2 * count // owners))
    slot_count = owners * capacity
    values = band_values(offsets[0], widths[0])
    target = dest[0]
    same_owner = target[:, None] == target[None, :]
    block_order = jnp.arange(count, dtype=jnp.int32)
    earlier = block_order[None, :] < block_order[:, None]
    rank_within = jnp.sum(jnp.logical_and(same_owner, earlier), axis=1)
    slot_index = target * capacity + rank_within
    matching = jnp.arange(slot_count, dtype=jnp.int32)[:, None] == slot_index[None, :]
    source = jnp.sum(jnp.where(matching, block_order[None, :], 0), axis=1)
    cell_weight = jnp.where(
        cells[0][:, None] == jnp.arange(CELL_DEV, dtype=jnp.int32)[None, :],
        weights[0][:, None],
        jnp.zeros((), jnp.bfloat16),
    )
    packed_weight = jnp.sum(
        jnp.where(matching[:, :, None], cell_weight[None].astype(jnp.float32), 0.0), axis=1
    ).astype(jnp.bfloat16)
    packed = warp_slots(
        images[0],
        values,
        jnp.minimum(slot_index, slot_count - 1).astype(jnp.int32),
        packed_weight.reshape(owners, capacity, CELL_DEV),
    )
    received = lax.all_to_all(packed, ("sect", "sub"), split_axis=0, concat_axis=0, tiled=True)
    received_weight = received[:, capacity * side, : capacity * CELL_DEV].reshape(
        slot_count, CELL_DEV
    )
    received = received[:, : capacity * side].reshape(slot_count, side, side)
    numerator = jnp.einsum(
        "sc,sij->icj", received_weight, received, preferred_element_type=jnp.float32
    )
    denominator = jnp.sum(received_weight.astype(jnp.float32), axis=0)
    cell_mean = (numerator / jnp.maximum(denominator, 1.0)[None, :, None]).astype(jnp.bfloat16)
    coadd = cell_mean.reshape(side, CELL_DEV * side)
    padded = extended(coadd, ((("sect", "sub"), 1),), DET_R)
    band_count = lax.axis_size("band")
    height = side // band_count
    framed = jnp.pad(padded, ((DET_R, DET_R), (0, 0)))
    gain_row = jnp.zeros((1, padded.shape[1]), jnp.bfloat16).at[0, :3].set(gain_pieces(band_gain[0]))
    span = height + 2 * DET_R
    me = lax.axis_index("band")
    own = lax.dynamic_slice_in_dim(framed, me * height, span, axis=0)
    combined = band_gain[0] * own.astype(jnp.float32)
    for shift in range(1, band_count):
        outgoing = jnp.concatenate(
            [lax.dynamic_slice_in_dim(framed, ((me + shift) % band_count) * height, span, axis=0), gain_row]
        )
        incoming = lax.ppermute(
            outgoing, "band", [(i, (i + shift) % band_count) for i in range(band_count)]
        )
        gain = jnp.sum(incoming[span, :3].astype(jnp.float32))
        combined = combined + gain * incoming[:span].astype(jnp.float32)
    detection = smooth_rows_valid(smooth_columns(combined, CELL_DEV * side), height)
    return (coadd[None], detection)


def solution(mesh):
    return jax.shard_map(
        local,
        mesh=mesh,
        in_specs=(
            P("band", ("groups", "sect", "sub"), None, None),
            P("band", ("groups", "sect", "sub"), None),
            P("band", ("groups", "sect", "sub"), None),
            P("band", ("groups", "sect", "sub")),
            P("band", ("groups", "sect", "sub")),
            P("band", ("groups", "sect", "sub")),
            P("band"),
        ),
        out_specs=(
            P("band", None, ("groups", "sect", "sub")),
            P("band", ("groups", "sect", "sub")),
        ),
        check_vma=False,
    )
```

```python
import math

import jax
import jax.numpy as jnp
from jax import lax
from jax.experimental import pallas as pl
from jax.experimental.pallas import tpu as pltpu
from jax.sharding import PartitionSpec as P

CELL_DEV = 4
PSF_R = 8
DET_R = 4


det_sigma = 3.0


def extended(array, sides, width):
    for axis, dim in sides:
        size, length = (lax.axis_size(axis), array.shape[dim])
        up = [(i, (i + 1) % size) for i in range(size - 1)]
        down = [(j, i) for i, j in up]
        last = lax.slice_in_dim(array, length - width, length, axis=dim)
        initial = lax.slice_in_dim(array, 0, width, axis=dim)
        before = lax.ppermute(last, axis, up)
        after = lax.ppermute(initial, axis, down)
        array = jnp.concatenate([before, array, after], axis=dim)
    return array


def lanczos_tap(spacing):
    return jnp.where(jnp.abs(spacing) < 3.0, jnp.sinc(spacing) * jnp.sinc(spacing / 3.0), 0.0)


def band_values(shift, spread):
    band = PSF_R + 4
    spacing = jnp.arange(-band, band + 1, dtype=jnp.float32)
    tap = jnp.arange(-PSF_R, PSF_R + 1, dtype=jnp.float32)
    tap_weight = jnp.exp(-spread[..., None] * (tap * tap))
    taps = lanczos_tap(spacing + (shift[..., None, None] + tap[:, None]))
    taps = jnp.concatenate([taps, jnp.ones(taps.shape[:-1] + (1,), jnp.float32)], axis=-1)
    summed = jnp.sum(tap_weight[..., None] * taps, axis=-2)
    return (summed[..., :-1] / summed[..., -1:]).astype(jnp.bfloat16)


def toeplitz(values, side):
    band = PSF_R + 4
    position = jnp.arange(side, dtype=jnp.int32)
    lag = position[:, None] - position[None, :]
    matrix = jnp.zeros(values.shape[:-1] + (side, side), jnp.bfloat16)
    for index in range(2 * band + 1):
        matrix = jnp.where(lag == index - band, values[..., index, None, None], matrix)
    return matrix


def base_rows(values, side):
    band = PSF_R + 4
    gap = jnp.zeros((values.shape[0], side - 2 * band - 1), jnp.float32)
    values = values.astype(jnp.float32)
    rows = jnp.concatenate([values[:, 0, band::-1], gap, values[:, 0, : band : -1]], axis=-1)
    cols = jnp.concatenate([values[:, 1, band:], gap, values[:, 1, :band]], axis=-1)
    return jnp.stack([rows, cols], axis=1)


def warp_kernel(slot_ref, bases_ref, image_ref, blank_ref, out_ref, done_ref, sems):
    side = image_ref.shape[-1]
    group = image_ref.shape[0]
    step = pl.program_id(0)
    lag = lax.broadcasted_iota(jnp.int32, (side, side), 0) - lax.broadcasted_iota(
        jnp.int32, (side, side), 1
    )
    inside = (jnp.abs(lag) <= PSF_R + 4).astype(jnp.float32)
    copies = []
    for member in range(group):
        bases = bases_ref[member]
        row_base = jnp.broadcast_to(bases[0:1], (side, side))
        col_base = jnp.broadcast_to(bases[1:2], (side, side))
        row_kernel = (pltpu.roll(row_base, 0, 1, stride=1, stride_axis=0) * inside).astype(
            jnp.bfloat16
        )
        col_kernel_t = (pltpu.roll(col_base, 0, 1, stride=1, stride_axis=0) * inside).astype(
            jnp.bfloat16
        )
        section = jnp.dot(row_kernel, image_ref[member], preferred_element_type=jnp.float32)
        done_ref[member] = jnp.dot(
            section.astype(jnp.bfloat16), col_kernel_t, preferred_element_type=jnp.float32
        ).astype(jnp.bfloat16)
        slot = slot_ref[step * group + member]
        capacity = (out_ref.shape[1] - 16) // side
        target = out_ref.at[slot // capacity, pl.ds((slot % capacity) * side, side), :]
        copy = pltpu.make_async_copy(done_ref.at[member], target, sems.at[member])
        copy.start()
        copies.append(copy)
    for copy in copies:
        copy.wait()


def warp_slots(images, values, slot_index, slot_weight, interpret=False):
    count, side = images.shape[0], images.shape[-1]
    owners, capacity, cell_count = slot_weight.shape
    group = next(size for size in (16, 8, 4, 2, 1) if count % size == 0)
    bases = base_rows(values, side)
    blank = (
        jnp.zeros((owners, capacity * side + 16, side), jnp.bfloat16)
        .at[:, capacity * side, : capacity * cell_count]
        .set(slot_weight.reshape(owners, capacity * cell_count))
    )
    return pl.pallas_call(
        warp_kernel,
        grid_spec=pltpu.PrefetchScalarGridSpec(
            num_scalar_prefetch=1,
            grid=(count // group,),
            in_specs=[
                pl.BlockSpec((group, 2, side), lambda b, slots: (b, 0, 0)),
                pl.BlockSpec((group, side, side), lambda b, slots: (b, 0, 0)),
                pl.BlockSpec(memory_space=pl.ANY),
            ],
            out_specs=pl.BlockSpec(memory_space=pl.ANY),
            scratch_shapes=[
                pltpu.VMEM((group, side, side), jnp.bfloat16),
                pltpu.SemaphoreType.DMA((group,)),
            ],
        ),
        out_shape=jax.ShapeDtypeStruct(blank.shape, jnp.bfloat16),
        input_output_aliases={3: 0},
        cost_estimate=pl.CostEstimate(
            flops=4 * count * side**3,
            transcendentals=0,
            bytes_accessed=2 * (2 * count * side * side + blank.size),
        ),
        interpret=interpret,
    )(slot_index, bases, images, blank)


def gain_pieces(gain):
    high = lax.reduce_precision(gain, exponent_bits=8, mantissa_bits=7)
    rest = gain - high
    middle = lax.reduce_precision(rest, exponent_bits=8, mantissa_bits=7)
    low = lax.reduce_precision(rest - middle, exponent_bits=8, mantissa_bits=7)
    return jnp.stack([high, middle, low]).astype(jnp.bfloat16)


def filter_taps():
    values = [
        math.exp(-float(tap * tap) / (2.0 * det_sigma * det_sigma))
        for tap in range(-DET_R, DET_R + 1)
    ]
    whole = sum(values)
    return [value / whole for value in values]


def smooth_columns(padded, width):
    taps = filter_taps()
    total = jnp.zeros((padded.shape[0], width), jnp.float32)
    for index, tap in enumerate(range(-DET_R, DET_R + 1)):
        total = total + taps[index] * padded[:, DET_R + tap : DET_R + tap + width]
    return total


def smooth_rows_valid(framed, height):
    taps = filter_taps()
    total = jnp.zeros((height, framed.shape[1]), jnp.float32)
    for index, tap in enumerate(range(-DET_R, DET_R + 1)):
        total = total + taps[index] * framed[DET_R + tap : DET_R + tap + height, :]
    return total


def local(images, offsets, widths, weights, dest, cells, band_gain):
    side = images.shape[-1]
    count = images.shape[1]
    sect_count = lax.axis_size("sect")
    sub_count = lax.axis_size("sub")
    owners = sect_count * sub_count
    capacity = max(2, -(-2 * count // owners))
    slot_count = owners * capacity
    values = band_values(offsets[0], widths[0])
    target = dest[0]
    same_owner = target[:, None] == target[None, :]
    block_order = jnp.arange(count, dtype=jnp.int32)
    earlier = block_order[None, :] < block_order[:, None]
    rank_within = jnp.sum(jnp.logical_and(same_owner, earlier), axis=1)
    slot_index = target * capacity + rank_within
    matching = jnp.arange(slot_count, dtype=jnp.int32)[:, None] == slot_index[None, :]
    source = jnp.sum(jnp.where(matching, block_order[None, :], 0), axis=1)
    cell_weight = jnp.where(
        cells[0][:, None] == jnp.arange(CELL_DEV, dtype=jnp.int32)[None, :],
        weights[0][:, None],
        jnp.zeros((), jnp.bfloat16),
    )
    packed_weight = jnp.sum(
        jnp.where(matching[:, :, None], cell_weight[None].astype(jnp.float32), 0.0), axis=1
    ).astype(jnp.bfloat16)
    packed = warp_slots(
        images[0],
        values,
        jnp.minimum(slot_index, slot_count - 1).astype(jnp.int32),
        packed_weight.reshape(owners, capacity, CELL_DEV),
    )
    received = lax.all_to_all(packed, ("sect", "sub"), split_axis=0, concat_axis=0, tiled=True)
    received_weight = received[:, capacity * side, : capacity * CELL_DEV].reshape(
        slot_count, CELL_DEV
    )
    received = received[:, : capacity * side].reshape(slot_count, side, side)
    numerator = jnp.einsum(
        "sc,sij->icj", received_weight, received, preferred_element_type=jnp.float32
    )
    denominator = jnp.sum(received_weight.astype(jnp.float32), axis=0)
    cell_mean = (numerator / jnp.maximum(denominator, 1.0)[None, :, None]).astype(jnp.bfloat16)
    coadd = cell_mean.reshape(side, CELL_DEV * side)
    scale = jnp.maximum(denominator, 1.0)
    first = jnp.einsum(
        "s,sij->ij",
        received_weight[:, 0],
        received[:, :, :DET_R],
        preferred_element_type=jnp.float32,
    )
    last = jnp.einsum(
        "s,sij->ij",
        received_weight[:, CELL_DEV - 1],
        received[:, :, side - DET_R :],
        preferred_element_type=jnp.float32,
    )
    first = (first / scale[0]).astype(jnp.bfloat16)
    last = (last / scale[CELL_DEV - 1]).astype(jnp.bfloat16)
    size = lax.axis_size(("sect", "sub"))
    up = [(i, (i + 1) % size) for i in range(size - 1)]
    down = [(j, i) for i, j in up]
    before = lax.ppermute(last, ("sect", "sub"), up)
    after = lax.ppermute(first, ("sect", "sub"), down)
    padded = jnp.concatenate([before, coadd, after], axis=1)
    band_count = lax.axis_size("band")
    height = side // band_count
    framed = jnp.pad(padded, ((DET_R, DET_R), (0, 0)))
    gain_row = jnp.zeros((1, padded.shape[1]), jnp.bfloat16).at[0, :3].set(gain_pieces(band_gain[0]))
    span = height + 2 * DET_R
    me = lax.axis_index("band")
    own = lax.dynamic_slice_in_dim(framed, me * height, span, axis=0)
    combined = band_gain[0] * own.astype(jnp.float32)
    for shift in range(1, band_count):
        outgoing = jnp.concatenate(
            [lax.dynamic_slice_in_dim(framed, ((me + shift) % band_count) * height, span, axis=0), gain_row]
        )
        incoming = lax.ppermute(
            outgoing, "band", [(i, (i + shift) % band_count) for i in range(band_count)]
        )
        gain = jnp.sum(incoming[span, :3].astype(jnp.float32))
        combined = combined + gain * incoming[:span].astype(jnp.float32)
    detection = smooth_rows_valid(smooth_columns(combined, CELL_DEV * side), height)
    return (coadd[None], detection)


def solution(mesh):
    return jax.shard_map(
        local,
        mesh=mesh,
        in_specs=(
            P("band", ("groups", "sect", "sub"), None, None),
            P("band", ("groups", "sect", "sub"), None),
            P("band", ("groups", "sect", "sub"), None),
            P("band", ("groups", "sect", "sub")),
            P("band", ("groups", "sect", "sub")),
            P("band", ("groups", "sect", "sub")),
            P("band"),
        ),
        out_specs=(
            P("band", None, ("groups", "sect", "sub")),
            P("band", ("groups", "sect", "sub")),
        ),
        check_vma=False,
    )
```

```python
import math

import jax
import jax.numpy as jnp
from jax import lax
from jax.experimental import pallas as pl
from jax.experimental.pallas import tpu as pltpu
from jax.sharding import PartitionSpec as P

CELL_DEV = 4
PSF_R = 8
DET_R = 4


det_sigma = 3.0


def extended(array, sides, width):
    for axis, dim in sides:
        size, length = (lax.axis_size(axis), array.shape[dim])
        up = [(i, (i + 1) % size) for i in range(size - 1)]
        down = [(j, i) for i, j in up]
        last = lax.slice_in_dim(array, length - width, length, axis=dim)
        initial = lax.slice_in_dim(array, 0, width, axis=dim)
        before = lax.ppermute(last, axis, up)
        after = lax.ppermute(initial, axis, down)
        array = jnp.concatenate([before, array, after], axis=dim)
    return array


def lanczos_tap(spacing):
    return jnp.where(jnp.abs(spacing) < 3.0, jnp.sinc(spacing) * jnp.sinc(spacing / 3.0), 0.0)


def band_values(shift, spread):
    band = PSF_R + 4
    spacing = jnp.arange(-band, band + 1, dtype=jnp.float32)
    tap = jnp.arange(-PSF_R, PSF_R + 1, dtype=jnp.float32)
    tap_weight = jnp.exp(-spread[..., None] * (tap * tap))
    taps = lanczos_tap(spacing + (shift[..., None, None] + tap[:, None]))
    taps = jnp.concatenate([taps, jnp.ones(taps.shape[:-1] + (1,), jnp.float32)], axis=-1)
    summed = jnp.sum(tap_weight[..., None] * taps, axis=-2)
    return (summed[..., :-1] / summed[..., -1:]).astype(jnp.bfloat16)


def toeplitz(values, side):
    band = PSF_R + 4
    position = jnp.arange(side, dtype=jnp.int32)
    lag = position[:, None] - position[None, :]
    matrix = jnp.zeros(values.shape[:-1] + (side, side), jnp.bfloat16)
    for index in range(2 * band + 1):
        matrix = jnp.where(lag == index - band, values[..., index, None, None], matrix)
    return matrix


def base_rows(values, side):
    band = PSF_R + 4
    gap = jnp.zeros((values.shape[0], side - 2 * band - 1), jnp.float32)
    values = values.astype(jnp.float32)
    rows = jnp.concatenate([values[:, 0, band::-1], gap, values[:, 0, : band : -1]], axis=-1)
    cols = jnp.concatenate([values[:, 1, band:], gap, values[:, 1, :band]], axis=-1)
    return jnp.stack([rows, cols], axis=1)


def warp_kernel(slot_ref, bases_ref, image_ref, blank_ref, out_ref, done_ref, sems):
    side = image_ref.shape[-1]
    group = image_ref.shape[0]
    step = pl.program_id(0)
    lag = lax.broadcasted_iota(jnp.int32, (side, side), 0) - lax.broadcasted_iota(
        jnp.int32, (side, side), 1
    )
    inside = (jnp.abs(lag) <= PSF_R + 4).astype(jnp.float32)
    copies = []
    for member in range(group):
        bases = bases_ref[member]
        row_base = jnp.broadcast_to(bases[0:1], (side, side))
        col_base = jnp.broadcast_to(bases[1:2], (side, side))
        row_kernel = (pltpu.roll(row_base, 0, 1, stride=1, stride_axis=0) * inside).astype(
            jnp.bfloat16
        )
        col_kernel_t = (pltpu.roll(col_base, 0, 1, stride=1, stride_axis=0) * inside).astype(
            jnp.bfloat16
        )
        section = jnp.dot(row_kernel, image_ref[member], preferred_element_type=jnp.float32)
        done_ref[member] = jnp.dot(
            section.astype(jnp.bfloat16), col_kernel_t, preferred_element_type=jnp.float32
        ).astype(jnp.bfloat16)
        slot = slot_ref[step * group + member]
        capacity = (out_ref.shape[1] - 16) // side
        target = out_ref.at[slot // capacity, pl.ds((slot % capacity) * side, side), :]
        copy = pltpu.make_async_copy(done_ref.at[member], target, sems.at[member])
        copy.start()
        copies.append(copy)
    for copy in copies:
        copy.wait()


def warp_slots(images, values, slot_index, slot_weight, interpret=False):
    count, side = images.shape[0], images.shape[-1]
    owners, capacity, cell_count = slot_weight.shape
    group = next(size for size in (16, 8, 4, 2, 1) if count % size == 0)
    bases = base_rows(values, side)
    blank = (
        jnp.zeros((owners, capacity * side + 16, side), jnp.bfloat16)
        .at[:, capacity * side, : capacity * cell_count]
        .set(slot_weight.reshape(owners, capacity * cell_count))
    )
    return pl.pallas_call(
        warp_kernel,
        grid_spec=pltpu.PrefetchScalarGridSpec(
            num_scalar_prefetch=1,
            grid=(count // group,),
            in_specs=[
                pl.BlockSpec((group, 2, side), lambda b, slots: (b, 0, 0)),
                pl.BlockSpec((group, side, side), lambda b, slots: (b, 0, 0)),
                pl.BlockSpec(memory_space=pl.ANY),
            ],
            out_specs=pl.BlockSpec(memory_space=pl.ANY),
            scratch_shapes=[
                pltpu.VMEM((group, side, side), jnp.bfloat16),
                pltpu.SemaphoreType.DMA((group,)),
            ],
        ),
        out_shape=jax.ShapeDtypeStruct(blank.shape, jnp.bfloat16),
        input_output_aliases={3: 0},
        cost_estimate=pl.CostEstimate(
            flops=4 * count * side**3,
            transcendentals=0,
            bytes_accessed=2 * (2 * count * side * side + blank.size),
        ),
        interpret=interpret,
    )(slot_index, bases, images, blank)


def gain_pieces(gain):
    high = lax.reduce_precision(gain, exponent_bits=8, mantissa_bits=7)
    rest = gain - high
    middle = lax.reduce_precision(rest, exponent_bits=8, mantissa_bits=7)
    low = lax.reduce_precision(rest - middle, exponent_bits=8, mantissa_bits=7)
    return jnp.stack([high, middle, low]).astype(jnp.bfloat16)


def filter_taps():
    values = [
        math.exp(-float(tap * tap) / (2.0 * det_sigma * det_sigma))
        for tap in range(-DET_R, DET_R + 1)
    ]
    whole = sum(values)
    return [value / whole for value in values]


def smooth_columns(padded, width):
    taps = filter_taps()
    total = jnp.zeros((padded.shape[0], width), jnp.float32)
    for index, tap in enumerate(range(-DET_R, DET_R + 1)):
        total = total + taps[index] * padded[:, DET_R + tap : DET_R + tap + width]
    return total


def smooth_rows_valid(framed, height):
    taps = filter_taps()
    total = jnp.zeros((height, framed.shape[1]), jnp.float32)
    for index, tap in enumerate(range(-DET_R, DET_R + 1)):
        total = total + taps[index] * framed[DET_R + tap : DET_R + tap + height, :]
    return total


def local(images, offsets, widths, weights, dest, cells, band_gain):
    side = images.shape[-1]
    count = images.shape[1]
    sect_count = lax.axis_size("sect")
    sub_count = lax.axis_size("sub")
    owners = sect_count * sub_count
    capacity = max(2, -(-2 * count // owners))
    slot_count = owners * capacity
    values = band_values(offsets[0], widths[0])
    target = dest[0]
    same_owner = target[:, None] == target[None, :]
    block_order = jnp.arange(count, dtype=jnp.int32)
    earlier = block_order[None, :] < block_order[:, None]
    rank_within = jnp.sum(jnp.logical_and(same_owner, earlier), axis=1)
    slot_index = target * capacity + rank_within
    matching = jnp.arange(slot_count, dtype=jnp.int32)[:, None] == slot_index[None, :]
    source = jnp.sum(jnp.where(matching, block_order[None, :], 0), axis=1)
    cell_weight = jnp.where(
        cells[0][:, None] == jnp.arange(CELL_DEV, dtype=jnp.int32)[None, :],
        weights[0][:, None],
        jnp.zeros((), jnp.bfloat16),
    )
    packed_weight = jnp.sum(
        jnp.where(matching[:, :, None], cell_weight[None].astype(jnp.float32), 0.0), axis=1
    ).astype(jnp.bfloat16)
    packed = warp_slots(
        images[0],
        values,
        jnp.minimum(slot_index, slot_count - 1).astype(jnp.int32),
        packed_weight.reshape(owners, capacity, CELL_DEV),
    )
    received = lax.all_to_all(packed, ("sect", "sub"), split_axis=0, concat_axis=0, tiled=True)
    received_weight = received[:, capacity * side, : capacity * CELL_DEV].reshape(
        slot_count, CELL_DEV
    )
    received = received[:, : capacity * side].reshape(slot_count, side, side)
    numerator = jnp.einsum(
        "sc,sij->icj", received_weight, received, preferred_element_type=jnp.float32
    )
    denominator = jnp.sum(received_weight.astype(jnp.float32), axis=0)
    cell_mean = (numerator / jnp.maximum(denominator, 1.0)[None, :, None]).astype(jnp.bfloat16)
    coadd = cell_mean.reshape(side, CELL_DEV * side)
    padded = extended(coadd, ((("sect", "sub"), 1),), DET_R)
    band_count = lax.axis_size("band")
    height = side // band_count
    framed = jnp.pad(padded, ((DET_R, DET_R), (0, 0)))
    gain_row = jnp.zeros((1, padded.shape[1]), jnp.bfloat16).at[0, :3].set(gain_pieces(band_gain[0]))
    span = height + 2 * DET_R
    me = lax.axis_index("band")
    own = lax.dynamic_slice_in_dim(framed, me * height, span, axis=0)
    width = CELL_DEV * side
    detection = smooth_rows_valid(smooth_columns(band_gain[0] * own.astype(jnp.float32), width), height)
    for shift in range(1, band_count):
        outgoing = jnp.concatenate(
            [lax.dynamic_slice_in_dim(framed, ((me + shift) % band_count) * height, span, axis=0), gain_row]
        )
        incoming = lax.ppermute(
            outgoing, "band", [(i, (i + shift) % band_count) for i in range(band_count)]
        )
        gain = jnp.sum(incoming[span, :3].astype(jnp.float32))
        detection = detection + smooth_rows_valid(
            smooth_columns(gain * incoming[:span].astype(jnp.float32), width), height
        )
    return (coadd[None], detection)


def solution(mesh):
    return jax.shard_map(
        local,
        mesh=mesh,
        in_specs=(
            P("band", ("groups", "sect", "sub"), None, None),
            P("band", ("groups", "sect", "sub"), None),
            P("band", ("groups", "sect", "sub"), None),
            P("band", ("groups", "sect", "sub")),
            P("band", ("groups", "sect", "sub")),
            P("band", ("groups", "sect", "sub")),
            P("band"),
        ),
        out_specs=(
            P("band", None, ("groups", "sect", "sub")),
            P("band", ("groups", "sect", "sub")),
        ),
        check_vma=False,
    )
```

```python
import math

import jax
import jax.numpy as jnp
from jax import lax
from jax.experimental import pallas as pl
from jax.experimental.pallas import tpu as pltpu
from jax.sharding import PartitionSpec as P

CELL_DEV = 4
PSF_R = 8
DET_R = 4


det_sigma = 3.0


def extended(array, sides, width):
    for axis, dim in sides:
        size, length = (lax.axis_size(axis), array.shape[dim])
        up = [(i, (i + 1) % size) for i in range(size - 1)]
        down = [(j, i) for i, j in up]
        last = lax.slice_in_dim(array, length - width, length, axis=dim)
        initial = lax.slice_in_dim(array, 0, width, axis=dim)
        before = lax.ppermute(last, axis, up)
        after = lax.ppermute(initial, axis, down)
        array = jnp.concatenate([before, array, after], axis=dim)
    return array


def lanczos_tap(spacing):
    return jnp.where(jnp.abs(spacing) < 3.0, jnp.sinc(spacing) * jnp.sinc(spacing / 3.0), 0.0)


def band_values(shift, spread):
    band = PSF_R + 4
    spacing = jnp.arange(-band, band + 1, dtype=jnp.float32)
    tap = jnp.arange(-PSF_R, PSF_R + 1, dtype=jnp.float32)
    tap_weight = jnp.exp(-spread[..., None] * (tap * tap))
    taps = lanczos_tap(spacing + (shift[..., None, None] + tap[:, None]))
    taps = jnp.concatenate([taps, jnp.ones(taps.shape[:-1] + (1,), jnp.float32)], axis=-1)
    summed = jnp.sum(tap_weight[..., None] * taps, axis=-2)
    return (summed[..., :-1] / summed[..., -1:]).astype(jnp.bfloat16)


def toeplitz(values, side):
    band = PSF_R + 4
    position = jnp.arange(side, dtype=jnp.int32)
    lag = position[:, None] - position[None, :]
    matrix = jnp.zeros(values.shape[:-1] + (side, side), jnp.bfloat16)
    for index in range(2 * band + 1):
        matrix = jnp.where(lag == index - band, values[..., index, None, None], matrix)
    return matrix


def base_rows(values, side):
    band = PSF_R + 4
    gap = jnp.zeros((values.shape[0], side - 2 * band - 1), jnp.float32)
    values = values.astype(jnp.float32)
    rows = jnp.concatenate([values[:, 0, band::-1], gap, values[:, 0, : band : -1]], axis=-1)
    cols = jnp.concatenate([values[:, 1, band:], gap, values[:, 1, :band]], axis=-1)
    return jnp.stack([rows, cols], axis=1)


def warp_kernel(
    slot_ref, source_ref, bases_ref, image_ref, weight_ref, out_ref, done_ref, zero_ref, sems, fill_sems
):
    side = image_ref.shape[-1]
    group = image_ref.shape[0]
    capacity = (out_ref.shape[1] - 16) // side
    slot_total = source_ref.shape[0]
    zero_ref[...] = jnp.zeros((side, side), jnp.bfloat16)

    def target(slot):
        return out_ref.at[slot // capacity, pl.ds((slot % capacity) * side, side), :]

    for slot in range(slot_total):

        @pl.when(source_ref[slot] >= group)
        def _():
            pltpu.make_async_copy(zero_ref, target(slot), fill_sems.at[slot]).start()

    weight_copy = pltpu.make_async_copy(
        weight_ref, out_ref.at[:, pl.ds(capacity * side, 16), :], fill_sems.at[slot_total]
    )
    weight_copy.start()
    lag = lax.broadcasted_iota(jnp.int32, (side, side), 0) - lax.broadcasted_iota(
        jnp.int32, (side, side), 1
    )
    inside = (jnp.abs(lag) <= PSF_R + 4).astype(jnp.float32)
    copies = []
    for member in range(group):
        bases = bases_ref[member]
        row_base = jnp.broadcast_to(bases[0:1], (side, side))
        col_base = jnp.broadcast_to(bases[1:2], (side, side))
        row_kernel = (pltpu.roll(row_base, 0, 1, stride=1, stride_axis=0) * inside).astype(
            jnp.bfloat16
        )
        col_kernel_t = (pltpu.roll(col_base, 0, 1, stride=1, stride_axis=0) * inside).astype(
            jnp.bfloat16
        )
        section = jnp.dot(row_kernel, image_ref[member], preferred_element_type=jnp.float32)
        done_ref[member] = jnp.dot(
            section.astype(jnp.bfloat16), col_kernel_t, preferred_element_type=jnp.float32
        ).astype(jnp.bfloat16)
        copy = pltpu.make_async_copy(done_ref.at[member], target(slot_ref[member]), sems.at[member])
        copy.start()
        copies.append(copy)
    for copy in copies:
        copy.wait()
    weight_copy.wait()
    for slot in range(slot_total):

        @pl.when(source_ref[slot] >= group)
        def _():
            pltpu.make_async_copy(zero_ref, target(slot), fill_sems.at[slot]).wait()


def warp_slots(images, values, slot_index, slot_source, slot_weight, interpret=False):
    count, side = images.shape[0], images.shape[-1]
    owners, capacity, cell_count = slot_weight.shape
    slot_total = owners * capacity
    bases = base_rows(values, side)
    weight_rows = (
        jnp.zeros((owners, 16, side), jnp.bfloat16)
        .at[:, 0, : capacity * cell_count]
        .set(slot_weight.reshape(owners, capacity * cell_count))
    )
    return pl.pallas_call(
        warp_kernel,
        grid_spec=pltpu.PrefetchScalarGridSpec(
            num_scalar_prefetch=2,
            grid=(1,),
            in_specs=[
                pl.BlockSpec((count, 2, side), lambda b, slots, sources: (0, 0, 0)),
                pl.BlockSpec((count, side, side), lambda b, slots, sources: (0, 0, 0)),
                pl.BlockSpec((owners, 16, side), lambda b, slots, sources: (0, 0, 0)),
            ],
            out_specs=pl.BlockSpec(memory_space=pl.ANY),
            scratch_shapes=[
                pltpu.VMEM((count, side, side), jnp.bfloat16),
                pltpu.VMEM((side, side), jnp.bfloat16),
                pltpu.SemaphoreType.DMA((count,)),
                pltpu.SemaphoreType.DMA((slot_total + 1,)),
            ],
        ),
        out_shape=jax.ShapeDtypeStruct((owners, capacity * side + 16, side), jnp.bfloat16),
        cost_estimate=pl.CostEstimate(
            flops=4 * count * side**3,
            transcendentals=0,
            bytes_accessed=2 * (count + slot_total) * side * side,
        ),
        interpret=interpret,
    )(slot_index, slot_source, bases, images, weight_rows)


def gain_pieces(gain):
    high = lax.reduce_precision(gain, exponent_bits=8, mantissa_bits=7)
    rest = gain - high
    middle = lax.reduce_precision(rest, exponent_bits=8, mantissa_bits=7)
    low = lax.reduce_precision(rest - middle, exponent_bits=8, mantissa_bits=7)
    return jnp.stack([high, middle, low]).astype(jnp.bfloat16)


def filter_taps():
    values = [
        math.exp(-float(tap * tap) / (2.0 * det_sigma * det_sigma))
        for tap in range(-DET_R, DET_R + 1)
    ]
    whole = sum(values)
    return [value / whole for value in values]


def smooth_columns(padded, width):
    taps = filter_taps()
    total = jnp.zeros((padded.shape[0], width), jnp.float32)
    for index, tap in enumerate(range(-DET_R, DET_R + 1)):
        total = total + taps[index] * padded[:, DET_R + tap : DET_R + tap + width]
    return total


def smooth_rows_valid(framed, height):
    taps = filter_taps()
    total = jnp.zeros((height, framed.shape[1]), jnp.float32)
    for index, tap in enumerate(range(-DET_R, DET_R + 1)):
        total = total + taps[index] * framed[DET_R + tap : DET_R + tap + height, :]
    return total


def local(images, offsets, widths, weights, dest, cells, band_gain):
    side = images.shape[-1]
    count = images.shape[1]
    sect_count = lax.axis_size("sect")
    sub_count = lax.axis_size("sub")
    owners = sect_count * sub_count
    capacity = max(2, -(-2 * count // owners))
    slot_count = owners * capacity
    values = band_values(offsets[0], widths[0])
    target = dest[0]
    same_owner = target[:, None] == target[None, :]
    block_order = jnp.arange(count, dtype=jnp.int32)
    earlier = block_order[None, :] < block_order[:, None]
    rank_within = jnp.sum(jnp.logical_and(same_owner, earlier), axis=1)
    slot_index = target * capacity + rank_within
    matching = jnp.arange(slot_count, dtype=jnp.int32)[:, None] == slot_index[None, :]
    source = jnp.sum(jnp.where(matching, block_order[None, :], 0), axis=1)
    cell_weight = jnp.where(
        cells[0][:, None] == jnp.arange(CELL_DEV, dtype=jnp.int32)[None, :],
        weights[0][:, None],
        jnp.zeros((), jnp.bfloat16),
    )
    packed_weight = jnp.sum(
        jnp.where(matching[:, :, None], cell_weight[None].astype(jnp.float32), 0.0), axis=1
    ).astype(jnp.bfloat16)
    packed = warp_slots(
        images[0],
        values,
        jnp.minimum(slot_index, slot_count - 1).astype(jnp.int32),
        jnp.where(jnp.any(matching, axis=1), source, count).astype(jnp.int32),
        packed_weight.reshape(owners, capacity, CELL_DEV),
    )
    received = lax.all_to_all(packed, ("sect", "sub"), split_axis=0, concat_axis=0, tiled=True)
    received_weight = received[:, capacity * side, : capacity * CELL_DEV].reshape(
        slot_count, CELL_DEV
    )
    received = received[:, : capacity * side].reshape(slot_count, side, side)
    numerator = jnp.einsum(
        "sc,sij->icj", received_weight, received, preferred_element_type=jnp.float32
    )
    denominator = jnp.sum(received_weight.astype(jnp.float32), axis=0)
    cell_mean = (numerator / jnp.maximum(denominator, 1.0)[None, :, None]).astype(jnp.bfloat16)
    coadd = cell_mean.reshape(side, CELL_DEV * side)
    padded = extended(coadd, ((("sect", "sub"), 1),), DET_R)
    band_count = lax.axis_size("band")
    height = side // band_count
    framed = jnp.pad(padded, ((DET_R, DET_R), (0, 0)))
    gain_row = jnp.zeros((1, padded.shape[1]), jnp.bfloat16).at[0, :3].set(gain_pieces(band_gain[0]))
    span = height + 2 * DET_R
    me = lax.axis_index("band")
    own = lax.dynamic_slice_in_dim(framed, me * height, span, axis=0)
    combined = band_gain[0] * own.astype(jnp.float32)
    for shift in range(1, band_count):
        outgoing = jnp.concatenate(
            [lax.dynamic_slice_in_dim(framed, ((me + shift) % band_count) * height, span, axis=0), gain_row]
        )
        incoming = lax.ppermute(
            outgoing, "band", [(i, (i + shift) % band_count) for i in range(band_count)]
        )
        gain = jnp.sum(incoming[span, :3].astype(jnp.float32))
        combined = combined + gain * incoming[:span].astype(jnp.float32)
    detection = smooth_rows_valid(smooth_columns(combined, CELL_DEV * side), height)
    return (coadd[None], detection)


def solution(mesh):
    return jax.shard_map(
        local,
        mesh=mesh,
        in_specs=(
            P("band", ("groups", "sect", "sub"), None, None),
            P("band", ("groups", "sect", "sub"), None),
            P("band", ("groups", "sect", "sub"), None),
            P("band", ("groups", "sect", "sub")),
            P("band", ("groups", "sect", "sub")),
            P("band", ("groups", "sect", "sub")),
            P("band"),
        ),
        out_specs=(
            P("band", None, ("groups", "sect", "sub")),
            P("band", ("groups", "sect", "sub")),
        ),
        check_vma=False,
    )
```
